32 devices in a mesh: freq: 2 (over y), gx: 4 (over z), gy: 2 (over x), col: 2 (over core).
Axes of the slice: x: 2, y: 2, z: 4, core: 2. Of those that a mesh axis runs over, the one named last changes fastest.
Arguments:
- source: bfloat16 [12, 64, 32, 256], P('freq', 'gx', 'gy', 'col'), parts along dimension 0, may hold values from -6 to 6
- warm: bfloat16 [12, 64, 32, 256], P('freq', 'gx', 'gy', 'col'), parts along dimension 0, may hold values from -2.1 to 2.6
- forward: bfloat16 [12, 64, 32, 256], P('freq', 'gx', 'gy', 'col'), parts along dimension 0, may hold values from -6 to 6
- density: bfloat16 [64, 32, 256], P('gx', 'gy', 'col'), may hold values from 1 to 3
- material_map: int32 [8, 4, 8], P('gx', 'gy', 'col'), may hold values from 0 to 7
- material_table: float32 [8, 2], replicated, may hold values from 0.5 to 2
- iface_cells: int32 [16, 256], P(('gx', 'gy', 'col')), may hold values from 0 to 32767, as said below
- impedance: float32 [2, 3], replicated, may hold values from 2 to 8
- omega2: float32 [2], P('freq'), parts along dimension 0, may hold values from 0.5 to 1
Outputs:
- adjoint: float32 [12, 64, 32, 256], P('freq', 'gx', 'gy', 'col'), parts along dimension 0
- coarse_gradient: float32 [32, 8], P('freq'), parts along dimension 0
The draws below stay inside these ranges and needn't reach their ends.
There are 2 independent parts, one for each index of `freq`. The reference program is written for one: setup_inputs(seed, part) draws one part's arguments, and reference() takes and returns one part's arrays. A program takes and returns all parts, laid end to end along the dimension named above; an argument that names none is the same for every part. Nothing has to cross between parts.
Inputs may be any that keep to these rules, and one draw needn't show every extreme that they name: `iface_cells`: each row's entries are distinct, rising, and within the tile of 16 x 16 x 128 cells; row r belongs to the device of that index along gx, gy and col together.
All inputs are finite; a program needn't handle non-finite values.
Results may differ from the reference program's by a relative error of at most 0.0003.
Values may be sent and summed in bfloat16 or wider, within the bound.
No kernel may reach another device: no remote copies, remote signals or barrier semaphores. Data moves between devices by JAX's collectives and lax.ppermute only.
A program may use at most 64 MiB of HBM per device.

```python
import math
import jax
import jax.numpy as jnp
from jax import lax

CX = 16
CY = 16
CZ = 128
IFC = 256
NMAT = 8
GROUP = 16
NX = 64
NY = 32
NZ = 256
N_GX = 4
N_GY = 2
N_COL = 2


def draw_warm(key, part):
    noise = jnp.clip(0.4 * jax.random.normal(jax.random.fold_in(key, 11), (6, NX, NY, NZ), jnp.float32), -1.6, 1.6)
    tiles_x = NX // CX
    tiles_y = NY // CY
    tiles_z = NZ // CZ
    levels = jax.random.uniform(jax.random.fold_in(key, 12), (6, tiles_x, tiles_y, tiles_z), jnp.float32, -0.5, 1.0)
    spread = jnp.broadcast_to(levels[:, :, None, :, None, :, None], (6, tiles_x, CX, tiles_y, CY, tiles_z, CZ))
    drift = spread.reshape(6, NX, NY, NZ)
    return (noise + drift).astype(jnp.bfloat16)


def draw_iface_cells(key, part):
    stride = CX * CY * CZ // IFC
    offsets = jax.random.randint(jax.random.fold_in(key, 21), (GROUP, IFC), 0, stride)
    row_index = lax.broadcasted_iota(jnp.int32, (GROUP, IFC), 0)
    col_index = lax.broadcasted_iota(jnp.int32, (GROUP, IFC), 1)
    offsets = jnp.where((row_index == 0) & (col_index == 0), 0, offsets)
    offsets = jnp.where((row_index == GROUP - 1) & (col_index == IFC - 1), stride - 1, offsets)
    return (col_index * stride + offsets).astype(jnp.int32)


def plant(drawn, stream_key, smallest, high):
    longest = drawn.shape.index(max(drawn.shape))
    spots = []
    for shift in (0, 1):
        where = [jax.random.randint(jax.random.fold_in(stream_key, axis), (), 0, length) for axis, length in enumerate(drawn.shape)]
        where[longest] = (where[longest] + shift) % drawn.shape[longest]
        spots.append(tuple(where))
    return drawn.at[spots[0]].set(smallest).at[spots[1]].set(high)


def steps_of(stream_key, shape, shards, least, largest):
    level = 1.0
    for dim, shards_of in shards:
        draws = jax.random.uniform(jax.random.fold_in(jax.random.fold_in(stream_key, 6), dim), (shards_of,), jnp.float32, least / len(shards), largest / len(shards))
        level = level * jnp.repeat(jnp.exp(draws), shape[dim] // shards_of).reshape((-1,) + (1,) * (len(shape) - 1 - dim))
    return level


def gaussian(own_key, dims, scale, limit, shards=(), held_as=jnp.bfloat16):
    level = steps_of(own_key, dims, shards, -0.22, 0.18) if shards else 1.0
    array = jax.random.normal(own_key, dims, jnp.float32) * scale * level
    return jnp.minimum(jnp.maximum(array, -limit), limit).astype(held_as)


def setup_inputs(seed: int = 0, part: int = 0) -> dict:
    keys = jax.random.split(jax.random.key(seed), 10)
    part_keys = jax.random.split(jax.random.fold_in(keys[9], part), 10)
    return {
        "source": gaussian(part_keys[0], (6, NX, NY, NZ), 1.0, 6.0, ((1, 4), (2, 2), (3, 2))),
        "warm": draw_warm(jax.random.fold_in(jax.random.fold_in(keys[9], part), 71), part),
        "forward": gaussian(part_keys[2], (6, NX, NY, NZ), 1.0, 6.0, ((1, 4), (2, 2), (3, 2))),
        "density": jnp.clip(jnp.exp(math.log(3.0) - 1.0986123 * jax.random.uniform(keys[3], (NX, NY, NZ), jnp.float32) ** steps_of(keys[3], (NX, NY, NZ), ((0, 4), (1, 2), (2, 2)), -0.2, 0.2)), 1.0, 3.0).astype(jnp.bfloat16),
        "material_map": plant(jax.random.randint(keys[4], (NX // 8, NY // 8, NZ // 32), 0, NMAT), jax.random.fold_in(keys[4], 1), 0, NMAT - 1).astype(jnp.int32),
        "material_table": jnp.clip(jnp.exp(jax.random.uniform(keys[5], (NMAT, 2), jnp.float32, math.log(0.5), math.log(2.0))), 0.5, 2.0),
        "iface_cells": draw_iface_cells(jax.random.fold_in(keys[9], 71), part),
        "impedance": jnp.clip(jnp.exp(jax.random.uniform(keys[7], (2, 3), jnp.float32, math.log(2.0), math.log(8.0))), 2.0, 8.0),
        "omega2": jnp.clip(jax.random.uniform(part_keys[8], (1,), jnp.float32, 0.5, 1.0), 0.5, 1.0),
    }


DAMPING = 0.5
RELAXATION = 0.6


def window(padded, offset):
    size_x = padded.shape[1] - 2
    size_y = padded.shape[2] - 2
    size_z = padded.shape[3] - 2
    return padded[:, 1 + offset[0]:1 + offset[0] + size_x, 1 + offset[1]:1 + offset[1] + size_y, 1 + offset[2]:1 + offset[2] + size_z]


def navier(padded, lame_first, shear):
    units = ((1, 0, 0), (0, 1, 0), (0, 0, 1))
    centre = window(padded, (0, 0, 0))
    second = []
    for axis_d in range(3):
        ahead = units[axis_d]
        behind = tuple(-value for value in ahead)
        second.append(window(padded, ahead) + window(padded, behind) - 2.0 * centre)
    laplace = second[0] + second[1] + second[2]
    result = []
    for part_index in range(2):
        for component in range(3):
            channel = part_index * 3 + component
            divergence = second[component][channel]
            for other_axis in range(3):
                if other_axis != component:
                    source_channel = part_index * 3 + other_axis
                    single = padded[source_channel:source_channel + 1]
                    first_unit = units[component]
                    other_unit = units[other_axis]
                    plus_plus = tuple(first_unit[k] + other_unit[k] for k in range(3))
                    plus_minus = tuple(first_unit[k] - other_unit[k] for k in range(3))
                    minus_plus = tuple(-first_unit[k] + other_unit[k] for k in range(3))
                    minus_minus = tuple(-first_unit[k] - other_unit[k] for k in range(3))
                    mixed = window(single, plus_plus) - window(single, plus_minus) - window(single, minus_plus) + window(single, minus_minus)
                    divergence = divergence + 0.25 * mixed[0]
            result.append(shear * laplace[channel] + (lame_first + shear) * divergence)
    return jnp.stack(result)


def sweep(padded, lame_first, shear, density, mask, source, mean_field, omega_sq, impedance):
    field = window(padded, (0, 0, 0))
    elastic = navier(padded, lame_first, shear)
    real_part = field[:3]
    imag_part = field[3:]
    mean_real = mean_field[:3][:, None, None, None]
    mean_imag = mean_field[3:][:, None, None, None]
    imp_real = impedance[0][:, None, None, None]
    imp_imag = impedance[1][:, None, None, None]
    inertia = omega_sq * density
    diff_real = real_part - mean_real
    diff_imag = imag_part - mean_imag
    apply_real = -elastic[:3] - inertia * (real_part - DAMPING * imag_part) + mask * (imp_real * diff_real - imp_imag * diff_imag)
    apply_imag = -elastic[3:] - inertia * (imag_part + DAMPING * real_part) + mask * (imp_real * diff_imag + imp_imag * diff_real)
    resid_real = source[:3] - apply_real
    resid_imag = source[3:] - apply_imag
    diag_real = 8.0 * shear + 2.0 * lame_first - inertia + mask * imp_real
    diag_imag = -DAMPING * inertia + mask * imp_imag
    modulus = diag_real * diag_real + diag_imag * diag_imag
    new_real = real_part + RELAXATION * (resid_real * diag_real + resid_imag * diag_imag) / modulus
    new_imag = imag_part + RELAXATION * (resid_imag * diag_real - resid_real * diag_imag) / modulus
    return jnp.concatenate([new_real, new_imag], 0)


def expand(blocks):
    blocks_x, blocks_y, blocks_z = blocks.shape
    spread = jnp.broadcast_to(blocks[:, None, :, None, :, None], (blocks_x, 8, blocks_y, 8, blocks_z, 32))
    return spread.reshape(blocks_x * 8, blocks_y * 8, blocks_z * 32)


def material(block_ids, table):
    lame_first = jnp.zeros(block_ids.shape, jnp.float32)
    shear = jnp.zeros(block_ids.shape, jnp.float32)
    for entry in range(table.shape[0]):
        chosen = block_ids == entry
        lame_first = jnp.where(chosen, table[entry, 0], lame_first)
        shear = jnp.where(chosen, table[entry, 1], shear)
    return lame_first, shear


def reference(source, warm, forward, density, material_map, material_table, iface_cells, impedance, omega2):
    omega_sq = omega2[0]
    lame_first, shear = material(expand(material_map), material_table)
    density_cells = density.astype(jnp.float32)
    tile_cells = CX * CY * CZ

    def tile_mask(positions):
        return jnp.zeros((tile_cells,), jnp.float32).at[positions].set(1.0)

    local_masks = jax.vmap(tile_mask)(iface_cells)
    mask = local_masks.reshape(N_GX, N_GY, N_COL, CX, CY, CZ).transpose(0, 3, 1, 4, 2, 5).reshape(NX, NY, NZ)
    count = jnp.float32(GROUP * IFC)
    source_cells = source.astype(jnp.float32)
    field = warm.astype(jnp.float32)
    for sweep_index in range(2):
        mean_field = jnp.sum(mask * field, axis=(1, 2, 3)) / count
        padded = jnp.pad(field, ((0, 0), (1, 1), (1, 1), (1, 1)))
        field = sweep(padded, lame_first, shear, density_cells, mask, source_cells, mean_field, omega_sq, impedance)
    forward_cells = forward.astype(jnp.float32)
    correlation = (field[:3] * forward_cells[:3] - field[3:] * forward_cells[3:]) - DAMPING * (field[:3] * forward_cells[3:] + field[3:] * forward_cells[:3])
    cell_terms = -omega_sq * jnp.sum(correlation, axis=0)
    coarse = cell_terms.reshape(NX // 4, 4, NY // 4, 4, NZ).sum(axis=(1, 3, 4)) / 64.0
    return field, coarse
```

```python
import jax
import jax.numpy as jnp
from jax import lax
from jax.sharding import PartitionSpec as P

DAMPING = 0.5
RELAXATION = 0.6


def with_halo(array, sides, width):
    for axis, dim in sides:
        peers, length = (lax.axis_size(axis), array.shape[dim])
        up = [(i, (i + 1) % peers) for i in range(peers - 1)]
        down = [(j, i) for i, j in up]
        last = lax.slice_in_dim(array, length - width, length, axis=dim)
        initial = lax.slice_in_dim(array, 0, width, axis=dim)
        before = lax.ppermute(last, axis, up)
        after = lax.ppermute(initial, axis, down)
        array = jnp.concatenate([before, array, after], axis=dim)
    return array


def window(padded, offset):
    size_x = padded.shape[1] - 2
    size_y = padded.shape[2] - 2
    size_z = padded.shape[3] - 2
    return padded[
        :,
        1 + offset[0] : 1 + offset[0] + size_x,
        1 + offset[1] : 1 + offset[1] + size_y,
        1 + offset[2] : 1 + offset[2] + size_z,
    ]


def navier(padded, lame_first, shear):
    units = ((1, 0, 0), (0, 1, 0), (0, 0, 1))
    centre = window(padded, (0, 0, 0))
    second = []
    for axis_d in range(3):
        ahead = units[axis_d]
        behind = tuple((-value for value in ahead))
        second.append(window(padded, ahead) + window(padded, behind) - 2.0 * centre)
    laplace = second[0] + second[1] + second[2]
    result = []
    for part_index in range(2):
        for component in range(3):
            channel = part_index * 3 + component
            divergence = second[component][channel]
            for other_axis in range(3):
                if other_axis != component:
                    source_channel = part_index * 3 + other_axis
                    single = padded[source_channel : source_channel + 1]
                    first_unit = units[component]
                    other_unit = units[other_axis]
                    plus_plus = tuple((first_unit[k] + other_unit[k] for k in range(3)))
                    plus_minus = tuple((first_unit[k] - other_unit[k] for k in range(3)))
                    minus_plus = tuple((-first_unit[k] + other_unit[k] for k in range(3)))
                    minus_minus = tuple((-first_unit[k] - other_unit[k] for k in range(3)))
                    mixed = (
                        window(single, plus_plus)
                        - window(single, plus_minus)
                        - window(single, minus_plus)
                        + window(single, minus_minus)
                    )
                    divergence = divergence + 0.25 * mixed[0]
            result.append(shear * laplace[channel] + (lame_first + shear) * divergence)
    return jnp.stack(result)


def sweep(padded, lame_first, shear, density, mask, source, omega_sq, impedance):
    field = window(padded, (0, 0, 0))
    elastic = navier(padded, lame_first, shear)
    real_part = field[:3]
    imag_part = field[3:]
    imp_real = impedance[0][:, None, None, None]
    imp_imag = impedance[1][:, None, None, None]
    inertia = omega_sq * density
    apply_real = (
        -elastic[:3]
        - inertia * (real_part - DAMPING * imag_part)
        + mask * (imp_real * real_part - imp_imag * imag_part)
    )
    apply_imag = (
        -elastic[3:]
        - inertia * (imag_part + DAMPING * real_part)
        + mask * (imp_real * imag_part + imp_imag * real_part)
    )
    resid_real = source[:3] - apply_real
    resid_imag = source[3:] - apply_imag
    diag_real = 8.0 * shear + 2.0 * lame_first - inertia + mask * imp_real
    diag_imag = -DAMPING * inertia + mask * imp_imag
    modulus = diag_real * diag_real + diag_imag * diag_imag
    new_real = real_part + RELAXATION * (resid_real * diag_real + resid_imag * diag_imag) / modulus
    new_imag = imag_part + RELAXATION * (resid_imag * diag_real - resid_real * diag_imag) / modulus
    return jnp.concatenate([new_real, new_imag], 0)


def mean_gain(lame_first, shear, density, mask, omega_sq, impedance):
    imp_real = impedance[0][:, None, None, None]
    imp_imag = impedance[1][:, None, None, None]
    inertia = omega_sq * density
    diag_real = 8.0 * shear + 2.0 * lame_first - inertia + mask * imp_real
    diag_imag = -DAMPING * inertia + mask * imp_imag
    scale = RELAXATION * mask / (diag_real * diag_real + diag_imag * diag_imag)
    gain_real = scale * (imp_real * diag_real + imp_imag * diag_imag)
    gain_imag = scale * (imp_imag * diag_real - imp_real * diag_imag)
    return gain_real, gain_imag


def add_mean(field, gain_real, gain_imag, mean_field):
    mean_real = mean_field[:3][:, None, None, None]
    mean_imag = mean_field[3:][:, None, None, None]
    new_real = field[:3] + (gain_real * mean_real - gain_imag * mean_imag)
    new_imag = field[3:] + (gain_real * mean_imag + gain_imag * mean_real)
    return jnp.concatenate([new_real, new_imag], 0)


def group_sum(value, axes):
    size = 1
    for axis in axes:
        size *= lax.axis_size(axis)
    if size & (size - 1):
        return lax.psum(value, axes)
    stride = 1
    while stride < size:
        if stride * 4 <= size:
            got = [
                lax.ppermute(value, axes, [(i, i ^ (m * stride)) for i in range(size)])
                for m in (1, 2, 3)
            ]
            value = (value + got[0]) + (got[1] + got[2])
            stride *= 4
        else:
            value = value + lax.ppermute(value, axes, [(i, i ^ stride) for i in range(size)])
            stride *= 2
    return value


def expand(blocks):
    blocks_x, blocks_y, blocks_z = blocks.shape
    spread = jnp.broadcast_to(
        blocks[:, None, :, None, :, None], (blocks_x, 8, blocks_y, 8, blocks_z, 32)
    )
    return spread.reshape(blocks_x * 8, blocks_y * 8, blocks_z * 32)


def material(block_ids, table):
    lame_first = jnp.zeros(block_ids.shape, jnp.float32)
    shear = jnp.zeros(block_ids.shape, jnp.float32)
    for entry in range(table.shape[0]):
        chosen = block_ids == entry
        lame_first = jnp.where(chosen, table[entry, 0], lame_first)
        shear = jnp.where(chosen, table[entry, 1], shear)
    return (lame_first, shear)


def foundation(field, mask, count):
    total = group_sum(jnp.sum(mask * field, axis=(1, 2, 3)), ("gx", "gy", "col"))
    return total / count


def shards(
    source, warm, forward, density, material_map, material_table, iface_cells, impedance, omega2
):
    omega_sq = omega2[0]
    tile_shape = density.shape
    tile_cells = tile_shape[0] * tile_shape[1] * tile_shape[2]
    mask = jnp.zeros((tile_cells,), jnp.float32).at[iface_cells[0]].set(1.0).reshape(tile_shape)
    lame_tiles, shear_tiles = material(material_map, material_table)
    lame_first = expand(lame_tiles)
    shear = expand(shear_tiles)
    density_cells = density.astype(jnp.float32)
    source_cells = source.astype(jnp.float32)
    group_size = lax.axis_size("gx") * lax.axis_size("gy") * lax.axis_size("col")
    count = jnp.float32(group_size * iface_cells.shape[1])
    gain_real, gain_imag = mean_gain(lame_first, shear, density_cells, mask, omega_sq, impedance)
    field = warm.astype(jnp.float32)
    for sweep_index in range(2):
        mean_field = foundation(field, mask, count)
        padded = with_halo(field, (("gx", 1), ("gy", 2), ("col", 3)), 1)
        field = sweep(
            padded,
            lame_first,
            shear,
            density_cells,
            mask,
            source_cells,
            omega_sq,
            impedance,
        )
        field = add_mean(field, gain_real, gain_imag, mean_field)
    forward_cells = forward.astype(jnp.float32)
    correlation = (
        field[:3] * forward_cells[:3]
        - field[3:] * forward_cells[3:]
        - DAMPING * (field[:3] * forward_cells[3:] + field[3:] * forward_cells[:3])
    )
    cell_terms = -omega_sq * jnp.sum(correlation, axis=0)
    coarse_x = tile_shape[0] // 4
    coarse_y = tile_shape[1] // 4
    local_sums = cell_terms.reshape(coarse_x, 4, coarse_y, 4, tile_shape[2]).sum(axis=(1, 3, 4))
    grid = jnp.zeros(
        (lax.axis_size("gx") * coarse_x, lax.axis_size("gy") * coarse_y), jnp.float32
    )
    grid = lax.dynamic_update_slice(
        grid, local_sums, (lax.axis_index("gx") * coarse_x, lax.axis_index("gy") * coarse_y)
    )
    coarse = group_sum(grid, ("gx", "gy", "col")) / 64.0
    return (field, coarse)


def solution(mesh):
    in_specs = (
        P("freq", "gx", "gy", "col"),
        P("freq", "gx", "gy", "col"),
        P("freq", "gx", "gy", "col"),
        P("gx", "gy", "col"),
        P("gx", "gy", "col"),
        P(),
        P(("gx", "gy", "col"), None),
        P(),
        P("freq"),
    )
    out_specs = (P("freq", "gx", "gy", "col"), P("freq", None))
    return jax.shard_map(shards, mesh=mesh, in_specs=in_specs, out_specs=out_specs, check_vma=False)
```

```python
import jax
import jax.numpy as jnp
from jax import lax
from jax.sharding import PartitionSpec as P

DAMPING = 0.5
RELAXATION = 0.6


def with_halo(array, sides, width):
    for axis, dim in sides:
        peers, length = (lax.axis_size(axis), array.shape[dim])
        last = lax.slice_in_dim(array, length - width, length, axis=dim)
        initial = lax.slice_in_dim(array, 0, width, axis=dim)
        if peers == 2:
            first = lax.axis_index(axis) == 0
            got = lax.ppermute(jnp.where(first, last, initial), axis, [(0, 1), (1, 0)])
            zero = jnp.zeros_like(got)
            before = jnp.where(first, zero, got)
            after = jnp.where(first, got, zero)
        else:
            up = [(i, (i + 1) % peers) for i in range(peers - 1)]
            down = [(j, i) for i, j in up]
            before = lax.ppermute(last, axis, up)
            after = lax.ppermute(initial, axis, down)
        array = jnp.concatenate([before, array, after], axis=dim)
    return array


def window(padded, offset):
    size_x = padded.shape[1] - 2
    size_y = padded.shape[2] - 2
    size_z = padded.shape[3] - 2
    return padded[
        :,
        1 + offset[0] : 1 + offset[0] + size_x,
        1 + offset[1] : 1 + offset[1] + size_y,
        1 + offset[2] : 1 + offset[2] + size_z,
    ]


def navier(padded, lame_first, shear):
    units = ((1, 0, 0), (0, 1, 0), (0, 0, 1))
    centre = window(padded, (0, 0, 0))
    second = []
    for axis_d in range(3):
        ahead = units[axis_d]
        behind = tuple((-value for value in ahead))
        second.append(window(padded, ahead) + window(padded, behind) - 2.0 * centre)
    laplace = second[0] + second[1] + second[2]
    result = []
    for part_index in range(2):
        for component in range(3):
            channel = part_index * 3 + component
            divergence = second[component][channel]
            for other_axis in range(3):
                if other_axis != component:
                    source_channel = part_index * 3 + other_axis
                    single = padded[source_channel : source_channel + 1]
                    first_unit = units[component]
                    other_unit = units[other_axis]
                    plus_plus = tuple((first_unit[k] + other_unit[k] for k in range(3)))
                    plus_minus = tuple((first_unit[k] - other_unit[k] for k in range(3)))
                    minus_plus = tuple((-first_unit[k] + other_unit[k] for k in range(3)))
                    minus_minus = tuple((-first_unit[k] - other_unit[k] for k in range(3)))
                    mixed = (
                        window(single, plus_plus)
                        - window(single, plus_minus)
                        - window(single, minus_plus)
                        + window(single, minus_minus)
                    )
                    divergence = divergence + 0.25 * mixed[0]
            result.append(shear * laplace[channel] + (lame_first + shear) * divergence)
    return jnp.stack(result)


def sweep(padded, lame_first, shear, density, mask, source, omega_sq, impedance):
    field = window(padded, (0, 0, 0))
    elastic = navier(padded, lame_first, shear)
    real_part = field[:3]
    imag_part = field[3:]
    imp_real = impedance[0][:, None, None, None]
    imp_imag = impedance[1][:, None, None, None]
    inertia = omega_sq * density
    apply_real = (
        -elastic[:3]
        - inertia * (real_part - DAMPING * imag_part)
        + mask * (imp_real * real_part - imp_imag * imag_part)
    )
    apply_imag = (
        -elastic[3:]
        - inertia * (imag_part + DAMPING * real_part)
        + mask * (imp_real * imag_part + imp_imag * real_part)
    )
    resid_real = source[:3] - apply_real
    resid_imag = source[3:] - apply_imag
    diag_real = 8.0 * shear + 2.0 * lame_first - inertia + mask * imp_real
    diag_imag = -DAMPING * inertia + mask * imp_imag
    modulus = diag_real * diag_real + diag_imag * diag_imag
    new_real = real_part + RELAXATION * (resid_real * diag_real + resid_imag * diag_imag) / modulus
    new_imag = imag_part + RELAXATION * (resid_imag * diag_real - resid_real * diag_imag) / modulus
    return jnp.concatenate([new_real, new_imag], 0)


def mean_gain(lame_first, shear, density, mask, omega_sq, impedance):
    imp_real = impedance[0][:, None, None, None]
    imp_imag = impedance[1][:, None, None, None]
    inertia = omega_sq * density
    diag_real = 8.0 * shear + 2.0 * lame_first - inertia + mask * imp_real
    diag_imag = -DAMPING * inertia + mask * imp_imag
    scale = RELAXATION * mask / (diag_real * diag_real + diag_imag * diag_imag)
    gain_real = scale * (imp_real * diag_real + imp_imag * diag_imag)
    gain_imag = scale * (imp_imag * diag_real - imp_real * diag_imag)
    return gain_real, gain_imag


def add_mean(field, gain_real, gain_imag, mean_field):
    mean_real = mean_field[:3][:, None, None, None]
    mean_imag = mean_field[3:][:, None, None, None]
    new_real = field[:3] + (gain_real * mean_real - gain_imag * mean_imag)
    new_imag = field[3:] + (gain_real * mean_imag + gain_imag * mean_real)
    return jnp.concatenate([new_real, new_imag], 0)


def group_sum(value, axes):
    size = 1
    for axis in axes:
        size *= lax.axis_size(axis)
    if size & (size - 1):
        return lax.psum(value, axes)
    stride = 1
    while stride < size:
        if stride * 4 <= size:
            got = [
                lax.ppermute(value, axes, [(i, i ^ (m * stride)) for i in range(size)])
                for m in (1, 2, 3)
            ]
            value = (value + got[0]) + (got[1] + got[2])
            stride *= 4
        else:
            value = value + lax.ppermute(value, axes, [(i, i ^ stride) for i in range(size)])
            stride *= 2
    return value


def expand(blocks):
    blocks_x, blocks_y, blocks_z = blocks.shape
    spread = jnp.broadcast_to(
        blocks[:, None, :, None, :, None], (blocks_x, 8, blocks_y, 8, blocks_z, 32)
    )
    return spread.reshape(blocks_x * 8, blocks_y * 8, blocks_z * 32)


def material(block_ids, table):
    entries = lax.broadcasted_iota(jnp.int32, block_ids.shape + (table.shape[0],), block_ids.ndim)
    chosen = block_ids[..., None] == entries
    lame_first = jnp.sum(jnp.where(chosen, table[:, 0], 0.0), axis=-1)
    shear = jnp.sum(jnp.where(chosen, table[:, 1], 0.0), axis=-1)
    return (lame_first, shear)


def shards(
    source, warm, forward, density, material_map, material_table, iface_cells, impedance, omega2
):
    omega_sq = omega2[0]
    tile_shape = density.shape
    tile_cells = tile_shape[0] * tile_shape[1] * tile_shape[2]
    mask = jnp.zeros((tile_cells,), jnp.float32).at[iface_cells[0]].set(1.0).reshape(tile_shape)
    lame_tiles, shear_tiles = material(material_map, material_table)
    lame_first = expand(lame_tiles)
    shear = expand(shear_tiles)
    density_cells = density.astype(jnp.float32)
    source_cells = source.astype(jnp.float32)
    group_size = lax.axis_size("gx") * lax.axis_size("gy") * lax.axis_size("col")
    count = jnp.float32(group_size * iface_cells.shape[1])
    gain_real, gain_imag = mean_gain(lame_first, shear, density_cells, mask, omega_sq, impedance)
    axes = ("gx", "gy", "col")
    field = warm.astype(jnp.float32)
    first = group_sum(
        jnp.concatenate(
            [
                jnp.sum(mask * field, axis=(1, 2, 3)),
                jnp.sum(gain_real, axis=(1, 2, 3)),
                jnp.sum(gain_imag, axis=(1, 2, 3)),
            ]
        ),
        axes,
    )
    mean_field = first[:6] / count
    gain_total_real = first[6:9]
    gain_total_imag = first[9:12]
    sweep_args = (lame_first, shear, density_cells, mask, source_cells, omega_sq, impedance)
    padded = with_halo(field, (("gx", 1), ("gy", 2), ("col", 3)), 1)
    field = sweep(padded, *sweep_args)
    second = group_sum(jnp.sum(mask * field, axis=(1, 2, 3)), axes)
    field = add_mean(field, gain_real, gain_imag, mean_field)
    padded = with_halo(field, (("gx", 1), ("gy", 2), ("col", 3)), 1)
    field = sweep(padded, *sweep_args)
    mean_real = mean_field[:3]
    mean_imag = mean_field[3:]
    total_real = second[:3] + (gain_total_real * mean_real - gain_total_imag * mean_imag)
    total_imag = second[3:] + (gain_total_real * mean_imag + gain_total_imag * mean_real)
    field = add_mean(field, gain_real, gain_imag, jnp.concatenate([total_real, total_imag]) / count)
    forward_cells = forward.astype(jnp.float32)
    correlation = (
        field[:3] * forward_cells[:3]
        - field[3:] * forward_cells[3:]
        - DAMPING * (field[:3] * forward_cells[3:] + field[3:] * forward_cells[:3])
    )
    cell_terms = -omega_sq * jnp.sum(correlation, axis=0)
    coarse_x = tile_shape[0] // 4
    coarse_y = tile_shape[1] // 4
    local_sums = cell_terms.reshape(coarse_x, 4, coarse_y, 4, tile_shape[2]).sum(axis=(1, 3, 4))
    grid = jnp.zeros(
        (lax.axis_size("gx") * coarse_x, lax.axis_size("gy") * coarse_y), jnp.float32
    )
    grid = lax.dynamic_update_slice(
        grid, local_sums, (lax.axis_index("gx") * coarse_x, lax.axis_index("gy") * coarse_y)
    )
    coarse = group_sum(grid, ("gx", "gy", "col")) / 64.0
    return (field, coarse)


def solution(mesh):
    in_specs = (
        P("freq", "gx", "gy", "col"),
        P("freq", "gx", "gy", "col"),
        P("freq", "gx", "gy", "col"),
        P("gx", "gy", "col"),
        P("gx", "gy", "col"),
        P(),
        P(("gx", "gy", "col"), None),
        P(),
        P("freq"),
    )
    out_specs = (P("freq", "gx", "gy", "col"), P("freq", None))
    return jax.shard_map(shards, mesh=mesh, in_specs=in_specs, out_specs=out_specs, check_vma=False)
```

```python
import jax
import jax.numpy as jnp
from jax import lax
from jax.sharding import PartitionSpec as P

DAMPING = 0.5
RELAXATION = 0.6


def with_halo(array, sides, width, tie=None):
    for axis, dim in sides:
        peers, length = (lax.axis_size(axis), array.shape[dim])
        last = lax.slice_in_dim(array, length - width, length, axis=dim)
        initial = lax.slice_in_dim(array, 0, width, axis=dim)
        if tie is not None and axis == sides[-1][0]:
            last = last + tie
            initial = initial + tie
        if peers == 2:
            first = lax.axis_index(axis) == 0
            got = lax.ppermute(jnp.where(first, last, initial), axis, [(0, 1), (1, 0)])
            zero = jnp.zeros_like(got)
            before = jnp.where(first, zero, got)
            after = jnp.where(first, got, zero)
        else:
            up = [(i, (i + 1) % peers) for i in range(peers - 1)]
            down = [(j, i) for i, j in up]
            before = lax.ppermute(last, axis, up)
            after = lax.ppermute(initial, axis, down)
        array = jnp.concatenate([before, array, after], axis=dim)
    return array


def window(padded, offset):
    size_x = padded.shape[1] - 2
    size_y = padded.shape[2] - 2
    size_z = padded.shape[3] - 2
    return padded[
        :,
        1 + offset[0] : 1 + offset[0] + size_x,
        1 + offset[1] : 1 + offset[1] + size_y,
        1 + offset[2] : 1 + offset[2] + size_z,
    ]


def navier(padded, lame_first, shear):
    units = ((1, 0, 0), (0, 1, 0), (0, 0, 1))
    centre = window(padded, (0, 0, 0))
    second = []
    for axis_d in range(3):
        ahead = units[axis_d]
        behind = tuple((-value for value in ahead))
        second.append(window(padded, ahead) + window(padded, behind) - 2.0 * centre)
    laplace = second[0] + second[1] + second[2]
    result = []
    for part_index in range(2):
        for component in range(3):
            channel = part_index * 3 + component
            divergence = second[component][channel]
            for other_axis in range(3):
                if other_axis != component:
                    source_channel = part_index * 3 + other_axis
                    single = padded[source_channel : source_channel + 1]
                    first_unit = units[component]
                    other_unit = units[other_axis]
                    plus_plus = tuple((first_unit[k] + other_unit[k] for k in range(3)))
                    plus_minus = tuple((first_unit[k] - other_unit[k] for k in range(3)))
                    minus_plus = tuple((-first_unit[k] + other_unit[k] for k in range(3)))
                    minus_minus = tuple((-first_unit[k] - other_unit[k] for k in range(3)))
                    mixed = (
                        window(single, plus_plus)
                        - window(single, plus_minus)
                        - window(single, minus_plus)
                        + window(single, minus_minus)
                    )
                    divergence = divergence + 0.25 * mixed[0]
            result.append(shear * laplace[channel] + (lame_first + shear) * divergence)
    return jnp.stack(result)


def sweep(padded, lame_first, shear, density, mask, source, omega_sq, impedance):
    field = window(padded, (0, 0, 0))
    elastic = navier(padded, lame_first, shear)
    real_part = field[:3]
    imag_part = field[3:]
    imp_real = impedance[0][:, None, None, None]
    imp_imag = impedance[1][:, None, None, None]
    inertia = omega_sq * density
    apply_real = (
        -elastic[:3]
        - inertia * (real_part - DAMPING * imag_part)
        + mask * (imp_real * real_part - imp_imag * imag_part)
    )
    apply_imag = (
        -elastic[3:]
        - inertia * (imag_part + DAMPING * real_part)
        + mask * (imp_real * imag_part + imp_imag * real_part)
    )
    resid_real = source[:3] - apply_real
    resid_imag = source[3:] - apply_imag
    diag_real = 8.0 * shear + 2.0 * lame_first - inertia + mask * imp_real
    diag_imag = -DAMPING * inertia + mask * imp_imag
    modulus = diag_real * diag_real + diag_imag * diag_imag
    new_real = real_part + RELAXATION * (resid_real * diag_real + resid_imag * diag_imag) / modulus
    new_imag = imag_part + RELAXATION * (resid_imag * diag_real - resid_real * diag_imag) / modulus
    return jnp.concatenate([new_real, new_imag], 0)


def mean_gain(lame_first, shear, density, mask, omega_sq, impedance):
    imp_real = impedance[0][:, None, None, None]
    imp_imag = impedance[1][:, None, None, None]
    inertia = omega_sq * density
    diag_real = 8.0 * shear + 2.0 * lame_first - inertia + mask * imp_real
    diag_imag = -DAMPING * inertia + mask * imp_imag
    scale = RELAXATION * mask / (diag_real * diag_real + diag_imag * diag_imag)
    gain_real = scale * (imp_real * diag_real + imp_imag * diag_imag)
    gain_imag = scale * (imp_imag * diag_real - imp_real * diag_imag)
    return gain_real, gain_imag


def add_mean(field, gain_real, gain_imag, mean_field):
    mean_real = mean_field[:3][:, None, None, None]
    mean_imag = mean_field[3:][:, None, None, None]
    new_real = field[:3] + (gain_real * mean_real - gain_imag * mean_imag)
    new_imag = field[3:] + (gain_real * mean_imag + gain_imag * mean_real)
    return jnp.concatenate([new_real, new_imag], 0)


def group_sum(value, axes):
    size = 1
    for axis in axes:
        size *= lax.axis_size(axis)
    if size & (size - 1):
        return lax.psum(value, axes)
    stride = 1
    while stride < size:
        if stride * 4 <= size:
            got = [
                lax.ppermute(value, axes, [(i, i ^ (m * stride)) for i in range(size)])
                for m in (1, 2, 3)
            ]
            value = (value + got[0]) + (got[1] + got[2])
            stride *= 4
        else:
            value = value + lax.ppermute(value, axes, [(i, i ^ stride) for i in range(size)])
            stride *= 2
    return value


def expand(blocks):
    blocks_x, blocks_y, blocks_z = blocks.shape
    spread = jnp.broadcast_to(
        blocks[:, None, :, None, :, None], (blocks_x, 8, blocks_y, 8, blocks_z, 32)
    )
    return spread.reshape(blocks_x * 8, blocks_y * 8, blocks_z * 32)


def material(block_ids, table):
    entries = lax.broadcasted_iota(jnp.int32, block_ids.shape + (table.shape[0],), block_ids.ndim)
    chosen = block_ids[..., None] == entries
    lame_first = jnp.sum(jnp.where(chosen, table[:, 0], 0.0), axis=-1)
    shear = jnp.sum(jnp.where(chosen, table[:, 1], 0.0), axis=-1)
    return (lame_first, shear)


def shards(
    source, warm, forward, density, material_map, material_table, iface_cells, impedance, omega2
):
    omega_sq = omega2[0]
    tile_shape = density.shape
    tile_cells = tile_shape[0] * tile_shape[1] * tile_shape[2]
    mask = jnp.zeros((tile_cells,), jnp.float32).at[iface_cells[0]].set(1.0).reshape(tile_shape)
    lame_tiles, shear_tiles = material(material_map, material_table)
    lame_first = expand(lame_tiles)
    shear = expand(shear_tiles)
    density_cells = density.astype(jnp.float32)
    source_cells = source.astype(jnp.float32)
    group_size = lax.axis_size("gx") * lax.axis_size("gy") * lax.axis_size("col")
    count = jnp.float32(group_size * iface_cells.shape[1])
    gain_real, gain_imag = mean_gain(lame_first, shear, density_cells, mask, omega_sq, impedance)
    axes = ("gx", "gy", "col")
    field = warm.astype(jnp.float32)
    first = group_sum(
        jnp.concatenate(
            [
                jnp.sum(mask * field, axis=(1, 2, 3)),
                jnp.sum(gain_real, axis=(1, 2, 3)),
                jnp.sum(gain_imag, axis=(1, 2, 3)),
            ]
        ),
        axes,
    )
    mean_field = first[:6] / count
    gain_total_real = first[6:9]
    gain_total_imag = first[9:12]
    sweep_args = (lame_first, shear, density_cells, mask, source_cells, omega_sq, impedance)
    tie = 0.0 * jnp.sum(mean_field)
    padded = with_halo(field, (("gx", 1), ("gy", 2), ("col", 3)), 1, tie)
    field = sweep(padded, *sweep_args)
    second = group_sum(jnp.sum(mask * field, axis=(1, 2, 3)), axes)
    field = add_mean(field, gain_real, gain_imag, mean_field)
    padded = with_halo(field, (("gx", 1), ("gy", 2), ("col", 3)), 1)
    field = sweep(padded, *sweep_args)
    mean_real = mean_field[:3]
    mean_imag = mean_field[3:]
    total_real = second[:3] + (gain_total_real * mean_real - gain_total_imag * mean_imag)
    total_imag = second[3:] + (gain_total_real * mean_imag + gain_total_imag * mean_real)
    field = add_mean(field, gain_real, gain_imag, jnp.concatenate([total_real, total_imag]) / count)
    forward_cells = forward.astype(jnp.float32)
    correlation = (
        field[:3] * forward_cells[:3]
        - field[3:] * forward_cells[3:]
        - DAMPING * (field[:3] * forward_cells[3:] + field[3:] * forward_cells[:3])
    )
    cell_terms = -omega_sq * jnp.sum(correlation, axis=0)
    coarse_x = tile_shape[0] // 4
    coarse_y = tile_shape[1] // 4
    local_sums = cell_terms.reshape(coarse_x, 4, coarse_y, 4, tile_shape[2]).sum(axis=(1, 3, 4))
    grid = jnp.zeros(
        (lax.axis_size("gx") * coarse_x, lax.axis_size("gy") * coarse_y), jnp.float32
    )
    grid = lax.dynamic_update_slice(
        grid, local_sums, (lax.axis_index("gx") * coarse_x, lax.axis_index("gy") * coarse_y)
    )
    coarse = group_sum(grid, ("gx", "gy", "col")) / 64.0
    return (field, coarse)


def solution(mesh):
    in_specs = (
        P("freq", "gx", "gy", "col"),
        P("freq", "gx", "gy", "col"),
        P("freq", "gx", "gy", "col"),
        P("gx", "gy", "col"),
        P("gx", "gy", "col"),
        P(),
        P(("gx", "gy", "col"), None),
        P(),
        P("freq"),
    )
    out_specs = (P("freq", "gx", "gy", "col"), P("freq", None))
    return jax.shard_map(shards, mesh=mesh, in_specs=in_specs, out_specs=out_specs, check_vma=False)
```

```python
import jax
import jax.numpy as jnp
from jax import lax
from jax.sharding import PartitionSpec as P

DAMPING = 0.5
RELAXATION = 0.6


def with_halo(array, sides, width, tie=None):
    for axis, dim in sides:
        peers, length = (lax.axis_size(axis), array.shape[dim])
        last = lax.slice_in_dim(array, length - width, length, axis=dim)
        initial = lax.slice_in_dim(array, 0, width, axis=dim)
        if tie is not None and axis == sides[-1][0]:
            last = last + tie
            initial = initial + tie
        if peers == 2:
            first = lax.axis_index(axis) == 0
            got = lax.ppermute(jnp.where(first, last, initial), axis, [(0, 1), (1, 0)])
            zero = jnp.zeros_like(got)
            before = jnp.where(first, zero, got)
            after = jnp.where(first, got, zero)
        else:
            up = [(i, (i + 1) % peers) for i in range(peers - 1)]
            down = [(j, i) for i, j in up]
            before = lax.ppermute(last, axis, up)
            after = lax.ppermute(initial, axis, down)
        array = jnp.concatenate([before, array, after], axis=dim)
    return array


def window(padded, offset):
    size_x = padded.shape[1] - 2
    size_y = padded.shape[2] - 2
    size_z = padded.shape[3] - 2
    return padded[
        :,
        1 + offset[0] : 1 + offset[0] + size_x,
        1 + offset[1] : 1 + offset[1] + size_y,
        1 + offset[2] : 1 + offset[2] + size_z,
    ]


def navier(padded, lame_first, shear):
    units = ((1, 0, 0), (0, 1, 0), (0, 0, 1))
    centre = window(padded, (0, 0, 0))
    second = []
    for axis_d in range(3):
        ahead = units[axis_d]
        behind = tuple((-value for value in ahead))
        second.append(window(padded, ahead) + window(padded, behind) - 2.0 * centre)
    laplace = second[0] + second[1] + second[2]
    result = []
    for part_index in range(2):
        for component in range(3):
            channel = part_index * 3 + component
            divergence = second[component][channel]
            for other_axis in range(3):
                if other_axis != component:
                    source_channel = part_index * 3 + other_axis
                    single = padded[source_channel : source_channel + 1]
                    first_unit = units[component]
                    other_unit = units[other_axis]
                    plus_plus = tuple((first_unit[k] + other_unit[k] for k in range(3)))
                    plus_minus = tuple((first_unit[k] - other_unit[k] for k in range(3)))
                    minus_plus = tuple((-first_unit[k] + other_unit[k] for k in range(3)))
                    minus_minus = tuple((-first_unit[k] - other_unit[k] for k in range(3)))
                    mixed = (
                        window(single, plus_plus)
                        - window(single, plus_minus)
                        - window(single, minus_plus)
                        + window(single, minus_minus)
                    )
                    divergence = divergence + 0.25 * mixed[0]
            result.append(shear * laplace[channel] + (lame_first + shear) * divergence)
    return jnp.stack(result)


def sweep(padded, lame_first, shear, density, mask, source, omega_sq, impedance):
    field = window(padded, (0, 0, 0))
    elastic = navier(padded, lame_first, shear)
    real_part = field[:3]
    imag_part = field[3:]
    imp_real = impedance[0][:, None, None, None]
    imp_imag = impedance[1][:, None, None, None]
    inertia = omega_sq * density
    apply_real = (
        -elastic[:3]
        - inertia * (real_part - DAMPING * imag_part)
        + mask * (imp_real * real_part - imp_imag * imag_part)
    )
    apply_imag = (
        -elastic[3:]
        - inertia * (imag_part + DAMPING * real_part)
        + mask * (imp_real * imag_part + imp_imag * real_part)
    )
    resid_real = source[:3] - apply_real
    resid_imag = source[3:] - apply_imag
    diag_real = 8.0 * shear + 2.0 * lame_first - inertia + mask * imp_real
    diag_imag = -DAMPING * inertia + mask * imp_imag
    modulus = diag_real * diag_real + diag_imag * diag_imag
    new_real = real_part + RELAXATION * (resid_real * diag_real + resid_imag * diag_imag) / modulus
    new_imag = imag_part + RELAXATION * (resid_imag * diag_real - resid_real * diag_imag) / modulus
    return jnp.concatenate([new_real, new_imag], 0)


def mean_gain(lame_first, shear, density, mask, omega_sq, impedance):
    imp_real = impedance[0][:, None, None, None]
    imp_imag = impedance[1][:, None, None, None]
    inertia = omega_sq * density
    diag_real = 8.0 * shear + 2.0 * lame_first - inertia + mask * imp_real
    diag_imag = -DAMPING * inertia + mask * imp_imag
    scale = RELAXATION * mask / (diag_real * diag_real + diag_imag * diag_imag)
    gain_real = scale * (imp_real * diag_real + imp_imag * diag_imag)
    gain_imag = scale * (imp_imag * diag_real - imp_real * diag_imag)
    return gain_real, gain_imag


def add_mean(field, gain_real, gain_imag, mean_field):
    mean_real = mean_field[:3][:, None, None, None]
    mean_imag = mean_field[3:][:, None, None, None]
    new_real = field[:3] + (gain_real * mean_real - gain_imag * mean_imag)
    new_imag = field[3:] + (gain_real * mean_imag + gain_imag * mean_real)
    return jnp.concatenate([new_real, new_imag], 0)


def group_sum(value, axes):
    size = 1
    for axis in axes:
        size *= lax.axis_size(axis)
    if size & (size - 1):
        return lax.psum(value, axes)
    stride = 1
    while stride < size:
        value = value + lax.ppermute(value, axes, [(i, i ^ stride) for i in range(size)])
        stride *= 2
    return value


def expand(blocks):
    blocks_x, blocks_y, blocks_z = blocks.shape
    spread = jnp.broadcast_to(
        blocks[:, None, :, None, :, None], (blocks_x, 8, blocks_y, 8, blocks_z, 32)
    )
    return spread.reshape(blocks_x * 8, blocks_y * 8, blocks_z * 32)


def material(block_ids, table):
    entries = lax.broadcasted_iota(jnp.int32, block_ids.shape + (table.shape[0],), block_ids.ndim)
    chosen = block_ids[..., None] == entries
    lame_first = jnp.sum(jnp.where(chosen, table[:, 0], 0.0), axis=-1)
    shear = jnp.sum(jnp.where(chosen, table[:, 1], 0.0), axis=-1)
    return (lame_first, shear)


def shards(
    source, warm, forward, density, material_map, material_table, iface_cells, impedance, omega2
):
    omega_sq = omega2[0]
    tile_shape = density.shape
    tile_cells = tile_shape[0] * tile_shape[1] * tile_shape[2]
    mask = jnp.zeros((tile_cells,), jnp.float32).at[iface_cells[0]].set(1.0).reshape(tile_shape)
    lame_tiles, shear_tiles = material(material_map, material_table)
    lame_first = expand(lame_tiles)
    shear = expand(shear_tiles)
    density_cells = density.astype(jnp.float32)
    source_cells = source.astype(jnp.float32)
    group_size = lax.axis_size("gx") * lax.axis_size("gy") * lax.axis_size("col")
    count = jnp.float32(group_size * iface_cells.shape[1])
    gain_real, gain_imag = mean_gain(lame_first, shear, density_cells, mask, omega_sq, impedance)
    axes = ("gx", "gy", "col")
    field = warm.astype(jnp.float32)
    first = group_sum(
        jnp.concatenate(
            [
                jnp.sum(mask * field, axis=(1, 2, 3)),
                jnp.sum(gain_real, axis=(1, 2, 3)),
                jnp.sum(gain_imag, axis=(1, 2, 3)),
            ]
        ),
        axes,
    )
    mean_field = first[:6] / count
    gain_total_real = first[6:9]
    gain_total_imag = first[9:12]
    sweep_args = (lame_first, shear, density_cells, mask, source_cells, omega_sq, impedance)
    tie = 0.0 * jnp.sum(mean_field)
    padded = with_halo(field, (("gx", 1), ("gy", 2), ("col", 3)), 1, tie)
    field = sweep(padded, *sweep_args)
    second = group_sum(jnp.sum(mask * field, axis=(1, 2, 3)), axes)
    field = add_mean(field, gain_real, gain_imag, mean_field)
    padded = with_halo(field, (("gx", 1), ("gy", 2), ("col", 3)), 1)
    field = sweep(padded, *sweep_args)
    mean_real = mean_field[:3]
    mean_imag = mean_field[3:]
    total_real = second[:3] + (gain_total_real * mean_real - gain_total_imag * mean_imag)
    total_imag = second[3:] + (gain_total_real * mean_imag + gain_total_imag * mean_real)
    field = add_mean(field, gain_real, gain_imag, jnp.concatenate([total_real, total_imag]) / count)
    forward_cells = forward.astype(jnp.float32)
    correlation = (
        field[:3] * forward_cells[:3]
        - field[3:] * forward_cells[3:]
        - DAMPING * (field[:3] * forward_cells[3:] + field[3:] * forward_cells[:3])
    )
    cell_terms = -omega_sq * jnp.sum(correlation, axis=0)
    coarse_x = tile_shape[0] // 4
    coarse_y = tile_shape[1] // 4
    local_sums = cell_terms.reshape(coarse_x, 4, coarse_y, 4, tile_shape[2]).sum(axis=(1, 3, 4))
    grid = jnp.zeros(
        (lax.axis_size("gx") * coarse_x, lax.axis_size("gy") * coarse_y), jnp.float32
    )
    grid = lax.dynamic_update_slice(
        grid, local_sums, (lax.axis_index("gx") * coarse_x, lax.axis_index("gy") * coarse_y)
    )
    coarse = group_sum(grid, ("gx", "gy", "col")) / 64.0
    return (field, coarse)


def solution(mesh):
    in_specs = (
        P("freq", "gx", "gy", "col"),
        P("freq", "gx", "gy", "col"),
        P("freq", "gx", "gy", "col"),
        P("gx", "gy", "col"),
        P("gx", "gy", "col"),
        P(),
        P(("gx", "gy", "col"), None),
        P(),
        P("freq"),
    )
    out_specs = (P("freq", "gx", "gy", "col"), P("freq", None))
    return jax.shard_map(shards, mesh=mesh, in_specs=in_specs, out_specs=out_specs, check_vma=False)
```

```python
import jax
import jax.numpy as jnp
from jax import lax
from jax.sharding import PartitionSpec as P

DAMPING = 0.5
RELAXATION = 0.6


def with_halo(array, sides, width):
    for axis, dim in sides:
        peers, length = (lax.axis_size(axis), array.shape[dim])
        last = lax.slice_in_dim(array, length - width, length, axis=dim)
        initial = lax.slice_in_dim(array, 0, width, axis=dim)
        if peers == 2:
            first = lax.axis_index(axis) == 0
            got = lax.ppermute(jnp.where(first, last, initial), axis, [(0, 1), (1, 0)])
            zero = jnp.zeros_like(got)
            before = jnp.where(first, zero, got)
            after = jnp.where(first, got, zero)
        else:
            up = [(i, (i + 1) % peers) for i in range(peers - 1)]
            down = [(j, i) for i, j in up]
            before = lax.ppermute(last, axis, up)
            after = lax.ppermute(initial, axis, down)
        array = jnp.concatenate([before, array, after], axis=dim)
    return array


def window(padded, offset):
    size_x = padded.shape[1] - 2
    size_y = padded.shape[2] - 2
    size_z = padded.shape[3] - 2
    return padded[
        :,
        1 + offset[0] : 1 + offset[0] + size_x,
        1 + offset[1] : 1 + offset[1] + size_y,
        1 + offset[2] : 1 + offset[2] + size_z,
    ]


def navier(padded, lame_first, shear):
    units = ((1, 0, 0), (0, 1, 0), (0, 0, 1))
    centre = window(padded, (0, 0, 0))
    second = []
    for axis_d in range(3):
        ahead = units[axis_d]
        behind = tuple((-value for value in ahead))
        second.append(window(padded, ahead) + window(padded, behind) - 2.0 * centre)
    laplace = second[0] + second[1] + second[2]
    result = []
    for part_index in range(2):
        for component in range(3):
            channel = part_index * 3 + component
            divergence = second[component][channel]
            for other_axis in range(3):
                if other_axis != component:
                    source_channel = part_index * 3 + other_axis
                    single = padded[source_channel : source_channel + 1]
                    first_unit = units[component]
                    other_unit = units[other_axis]
                    plus_plus = tuple((first_unit[k] + other_unit[k] for k in range(3)))
                    plus_minus = tuple((first_unit[k] - other_unit[k] for k in range(3)))
                    minus_plus = tuple((-first_unit[k] + other_unit[k] for k in range(3)))
                    minus_minus = tuple((-first_unit[k] - other_unit[k] for k in range(3)))
                    mixed = (
                        window(single, plus_plus)
                        - window(single, plus_minus)
                        - window(single, minus_plus)
                        + window(single, minus_minus)
                    )
                    divergence = divergence + 0.25 * mixed[0]
            result.append(shear * laplace[channel] + (lame_first + shear) * divergence)
    return jnp.stack(result)


def sweep(padded, lame_first, shear, density, mask, source, omega_sq, impedance):
    field = window(padded, (0, 0, 0))
    elastic = navier(padded, lame_first, shear)
    real_part = field[:3]
    imag_part = field[3:]
    imp_real = impedance[0][:, None, None, None]
    imp_imag = impedance[1][:, None, None, None]
    inertia = omega_sq * density
    apply_real = (
        -elastic[:3]
        - inertia * (real_part - DAMPING * imag_part)
        + mask * (imp_real * real_part - imp_imag * imag_part)
    )
    apply_imag = (
        -elastic[3:]
        - inertia * (imag_part + DAMPING * real_part)
        + mask * (imp_real * imag_part + imp_imag * real_part)
    )
    resid_real = source[:3] - apply_real
    resid_imag = source[3:] - apply_imag
    diag_real = 8.0 * shear + 2.0 * lame_first - inertia + mask * imp_real
    diag_imag = -DAMPING * inertia + mask * imp_imag
    modulus = diag_real * diag_real + diag_imag * diag_imag
    new_real = real_part + RELAXATION * (resid_real * diag_real + resid_imag * diag_imag) / modulus
    new_imag = imag_part + RELAXATION * (resid_imag * diag_real - resid_real * diag_imag) / modulus
    return jnp.concatenate([new_real, new_imag], 0)


def mean_gain(lame_first, shear, density, mask, omega_sq, impedance):
    imp_real = impedance[0][:, None, None, None]
    imp_imag = impedance[1][:, None, None, None]
    inertia = omega_sq * density
    diag_real = 8.0 * shear + 2.0 * lame_first - inertia + mask * imp_real
    diag_imag = -DAMPING * inertia + mask * imp_imag
    scale = RELAXATION * mask / (diag_real * diag_real + diag_imag * diag_imag)
    gain_real = scale * (imp_real * diag_real + imp_imag * diag_imag)
    gain_imag = scale * (imp_imag * diag_real - imp_real * diag_imag)
    return gain_real, gain_imag


def add_mean(field, gain_real, gain_imag, mean_field):
    mean_real = mean_field[:3][:, None, None, None]
    mean_imag = mean_field[3:][:, None, None, None]
    new_real = field[:3] + (gain_real * mean_real - gain_imag * mean_imag)
    new_imag = field[3:] + (gain_real * mean_imag + gain_imag * mean_real)
    return jnp.concatenate([new_real, new_imag], 0)


def group_sum(value, axes):
    size = 1
    for axis in axes:
        size *= lax.axis_size(axis)
    if size & (size - 1):
        return lax.psum(value, axes)
    stride = 1
    while stride < size:
        if stride * 4 <= size:
            got = [
                lax.ppermute(value, axes, [(i, i ^ (m * stride)) for i in range(size)])
                for m in (1, 2, 3)
            ]
            value = (value + got[0]) + (got[1] + got[2])
            stride *= 4
        else:
            value = value + lax.ppermute(value, axes, [(i, i ^ stride) for i in range(size)])
            stride *= 2
    return value


def expand(blocks):
    blocks_x, blocks_y, blocks_z = blocks.shape
    spread = jnp.broadcast_to(
        blocks[:, None, :, None, :, None], (blocks_x, 8, blocks_y, 8, blocks_z, 32)
    )
    return spread.reshape(blocks_x * 8, blocks_y * 8, blocks_z * 32)


def material(block_ids, table):
    entries = lax.broadcasted_iota(jnp.int32, block_ids.shape + (table.shape[0],), block_ids.ndim)
    chosen = block_ids[..., None] == entries
    lame_first = jnp.sum(jnp.where(chosen, table[:, 0], 0.0), axis=-1)
    shear = jnp.sum(jnp.where(chosen, table[:, 1], 0.0), axis=-1)
    return (lame_first, shear)


def shards(
    source, warm, forward, density, material_map, material_table, iface_cells, impedance, omega2
):
    omega_sq = omega2[0]
    tile_shape = density.shape
    tile_cells = tile_shape[0] * tile_shape[1] * tile_shape[2]
    mask = jnp.zeros((tile_cells,), jnp.float32).at[iface_cells[0]].set(1.0).reshape(tile_shape)
    lame_tiles, shear_tiles = material(material_map, material_table)
    lame_first = expand(lame_tiles)
    shear = expand(shear_tiles)
    density_cells = density.astype(jnp.float32)
    source_cells = source.astype(jnp.float32)
    group_size = lax.axis_size("gx") * lax.axis_size("gy") * lax.axis_size("col")
    count = jnp.float32(group_size * iface_cells.shape[1])
    gain_real, gain_imag = mean_gain(lame_first, shear, density_cells, mask, omega_sq, impedance)
    axes = ("gx", "gy", "col")
    coarse_x = tile_shape[0] // 4
    coarse_y = tile_shape[1] // 4
    grid_shape = (lax.axis_size("gx") * coarse_x, lax.axis_size("gy") * coarse_y)
    grid_at = (lax.axis_index("gx") * coarse_x, lax.axis_index("gy") * coarse_y)

    def block_sums(cells):
        lead = cells.shape[:-3]
        local = cells.reshape(lead + (coarse_x, 4, coarse_y, 4, tile_shape[2]))
        local = local.sum(axis=(-4, -2, -1))
        grid = jnp.zeros(lead + grid_shape, jnp.float32)
        return lax.dynamic_update_slice(grid, local, (0,) * len(lead) + grid_at)

    forward_cells = forward.astype(jnp.float32)
    forward_real = forward_cells[:3]
    forward_imag = forward_cells[3:]
    plain_real = gain_real * forward_real - gain_imag * forward_imag
    plain_imag = gain_real * forward_imag + gain_imag * forward_real
    response_real = plain_real - DAMPING * plain_imag
    response_imag = plain_imag + DAMPING * plain_real
    response = block_sums(jnp.concatenate([response_real, response_imag]))
    field = warm.astype(jnp.float32)
    first = group_sum(
        jnp.concatenate(
            [
                jnp.sum(mask * field, axis=(1, 2, 3)),
                jnp.sum(gain_real, axis=(1, 2, 3)),
                jnp.sum(gain_imag, axis=(1, 2, 3)),
                response.reshape(-1),
            ]
        ),
        axes,
    )
    mean_field = first[:6] / count
    gain_total_real = first[6:9]
    gain_total_imag = first[9:12]
    response = first[12:].reshape(response.shape)
    sweep_args = (lame_first, shear, density_cells, mask, source_cells, omega_sq, impedance)
    padded = with_halo(field, (("gx", 1), ("gy", 2), ("col", 3)), 1)
    field = sweep(padded, *sweep_args)
    second_local = jnp.sum(mask * field, axis=(1, 2, 3))
    field = add_mean(field, gain_real, gain_imag, mean_field)
    padded = with_halo(field, (("gx", 1), ("gy", 2), ("col", 3)), 1)
    field = sweep(padded, *sweep_args)
    correlation = (
        field[:3] * forward_real
        - field[3:] * forward_imag
        - DAMPING * (field[:3] * forward_imag + field[3:] * forward_real)
    )
    cell_terms = -omega_sq * jnp.sum(correlation, axis=0)
    last = group_sum(jnp.concatenate([second_local, block_sums(cell_terms).reshape(-1)]), axes)
    second = last[:6]
    mean_real = mean_field[:3]
    mean_imag = mean_field[3:]
    total_real = second[:3] + (gain_total_real * mean_real - gain_total_imag * mean_imag)
    total_imag = second[3:] + (gain_total_real * mean_imag + gain_total_imag * mean_real)
    late_mean = jnp.concatenate([total_real, total_imag]) / count
    field = add_mean(field, gain_real, gain_imag, late_mean)
    late_terms = jnp.sum(
        late_mean[:3, None, None] * response[:3] - late_mean[3:, None, None] * response[3:], axis=0
    )
    coarse = (last[6:].reshape(grid_shape) - omega_sq * late_terms) / 64.0
    return (field, coarse)


def solution(mesh):
    in_specs = (
        P("freq", "gx", "gy", "col"),
        P("freq", "gx", "gy", "col"),
        P("freq", "gx", "gy", "col"),
        P("gx", "gy", "col"),
        P("gx", "gy", "col"),
        P(),
        P(("gx", "gy", "col"), None),
        P(),
        P("freq"),
    )
    out_specs = (P("freq", "gx", "gy", "col"), P("freq", None))
    return jax.shard_map(shards, mesh=mesh, in_specs=in_specs, out_specs=out_specs, check_vma=False)
```

```python
import jax
import jax.numpy as jnp
from jax import lax
from jax.sharding import PartitionSpec as P

DAMPING = 0.5
RELAXATION = 0.6


def with_halo(array, sides, width, tie=None):
    for axis, dim in sides:
        peers, length = (lax.axis_size(axis), array.shape[dim])
        last = lax.slice_in_dim(array, length - width, length, axis=dim)
        initial = lax.slice_in_dim(array, 0, width, axis=dim)
        if tie is not None:
            last = last + tie
            initial = initial + tie
        if peers == 2:
            first = lax.axis_index(axis) == 0
            got = lax.ppermute(jnp.where(first, last, initial), axis, [(0, 1), (1, 0)])
            zero = jnp.zeros_like(got)
            before = jnp.where(first, zero, got)
            after = jnp.where(first, got, zero)
        else:
            up = [(i, (i + 1) % peers) for i in range(peers - 1)]
            down = [(j, i) for i, j in up]
            before = lax.ppermute(last, axis, up)
            after = lax.ppermute(initial, axis, down)
        array = jnp.concatenate([before, array, after], axis=dim)
    return array


def window(padded, offset):
    size_x = padded.shape[1] - 2
    size_y = padded.shape[2] - 2
    size_z = padded.shape[3] - 2
    return padded[
        :,
        1 + offset[0] : 1 + offset[0] + size_x,
        1 + offset[1] : 1 + offset[1] + size_y,
        1 + offset[2] : 1 + offset[2] + size_z,
    ]


def navier(padded, lame_first, shear):
    units = ((1, 0, 0), (0, 1, 0), (0, 0, 1))
    centre = window(padded, (0, 0, 0))
    second = []
    for axis_d in range(3):
        ahead = units[axis_d]
        behind = tuple((-value for value in ahead))
        second.append(window(padded, ahead) + window(padded, behind) - 2.0 * centre)
    laplace = second[0] + second[1] + second[2]
    result = []
    for part_index in range(2):
        for component in range(3):
            channel = part_index * 3 + component
            divergence = second[component][channel]
            for other_axis in range(3):
                if other_axis != component:
                    source_channel = part_index * 3 + other_axis
                    single = padded[source_channel : source_channel + 1]
                    first_unit = units[component]
                    other_unit = units[other_axis]
                    plus_plus = tuple((first_unit[k] + other_unit[k] for k in range(3)))
                    plus_minus = tuple((first_unit[k] - other_unit[k] for k in range(3)))
                    minus_plus = tuple((-first_unit[k] + other_unit[k] for k in range(3)))
                    minus_minus = tuple((-first_unit[k] - other_unit[k] for k in range(3)))
                    mixed = (
                        window(single, plus_plus)
                        - window(single, plus_minus)
                        - window(single, minus_plus)
                        + window(single, minus_minus)
                    )
                    divergence = divergence + 0.25 * mixed[0]
            result.append(shear * laplace[channel] + (lame_first + shear) * divergence)
    return jnp.stack(result)


def sweep(padded, lame_first, shear, density, mask, source, omega_sq, impedance):
    field = window(padded, (0, 0, 0))
    elastic = navier(padded, lame_first, shear)
    real_part = field[:3]
    imag_part = field[3:]
    imp_real = impedance[0][:, None, None, None]
    imp_imag = impedance[1][:, None, None, None]
    inertia = omega_sq * density
    apply_real = (
        -elastic[:3]
        - inertia * (real_part - DAMPING * imag_part)
        + mask * (imp_real * real_part - imp_imag * imag_part)
    )
    apply_imag = (
        -elastic[3:]
        - inertia * (imag_part + DAMPING * real_part)
        + mask * (imp_real * imag_part + imp_imag * real_part)
    )
    resid_real = source[:3] - apply_real
    resid_imag = source[3:] - apply_imag
    diag_real = 8.0 * shear + 2.0 * lame_first - inertia + mask * imp_real
    diag_imag = -DAMPING * inertia + mask * imp_imag
    modulus = diag_real * diag_real + diag_imag * diag_imag
    new_real = real_part + RELAXATION * (resid_real * diag_real + resid_imag * diag_imag) / modulus
    new_imag = imag_part + RELAXATION * (resid_imag * diag_real - resid_real * diag_imag) / modulus
    return jnp.concatenate([new_real, new_imag], 0)


def mean_gain(lame_first, shear, density, mask, omega_sq, impedance):
    imp_real = impedance[0][:, None, None, None]
    imp_imag = impedance[1][:, None, None, None]
    inertia = omega_sq * density
    diag_real = 8.0 * shear + 2.0 * lame_first - inertia + mask * imp_real
    diag_imag = -DAMPING * inertia + mask * imp_imag
    scale = RELAXATION * mask / (diag_real * diag_real + diag_imag * diag_imag)
    gain_real = scale * (imp_real * diag_real + imp_imag * diag_imag)
    gain_imag = scale * (imp_imag * diag_real - imp_real * diag_imag)
    return gain_real, gain_imag


def add_mean(field, gain_real, gain_imag, mean_field):
    mean_real = mean_field[:3][:, None, None, None]
    mean_imag = mean_field[3:][:, None, None, None]
    new_real = field[:3] + (gain_real * mean_real - gain_imag * mean_imag)
    new_imag = field[3:] + (gain_real * mean_imag + gain_imag * mean_real)
    return jnp.concatenate([new_real, new_imag], 0)


def group_sum(value, axes):
    size = 1
    for axis in axes:
        size *= lax.axis_size(axis)
    if size & (size - 1):
        return lax.psum(value, axes)
    stride = 1
    while stride < size:
        if stride * 4 <= size:
            got = [
                lax.ppermute(value, axes, [(i, i ^ (m * stride)) for i in range(size)])
                for m in (1, 2, 3)
            ]
            value = (value + got[0]) + (got[1] + got[2])
            stride *= 4
        else:
            value = value + lax.ppermute(value, axes, [(i, i ^ stride) for i in range(size)])
            stride *= 2
    return value


def expand(blocks):
    blocks_x, blocks_y, blocks_z = blocks.shape
    spread = jnp.broadcast_to(
        blocks[:, None, :, None, :, None], (blocks_x, 8, blocks_y, 8, blocks_z, 32)
    )
    return spread.reshape(blocks_x * 8, blocks_y * 8, blocks_z * 32)


def material(block_ids, table):
    entries = lax.broadcasted_iota(jnp.int32, block_ids.shape + (table.shape[0],), block_ids.ndim)
    chosen = block_ids[..., None] == entries
    lame_first = jnp.sum(jnp.where(chosen, table[:, 0], 0.0), axis=-1)
    shear = jnp.sum(jnp.where(chosen, table[:, 1], 0.0), axis=-1)
    return (lame_first, shear)


def shards(
    source, warm, forward, density, material_map, material_table, iface_cells, impedance, omega2
):
    omega_sq = omega2[0]
    tile_shape = density.shape
    tile_cells = tile_shape[0] * tile_shape[1] * tile_shape[2]
    mask = jnp.zeros((tile_cells,), jnp.float32).at[iface_cells[0]].set(1.0).reshape(tile_shape)
    lame_tiles, shear_tiles = material(material_map, material_table)
    lame_first = expand(lame_tiles)
    shear = expand(shear_tiles)
    density_cells = density.astype(jnp.float32)
    source_cells = source.astype(jnp.float32)
    group_size = lax.axis_size("gx") * lax.axis_size("gy") * lax.axis_size("col")
    count = jnp.float32(group_size * iface_cells.shape[1])
    gain_real, gain_imag = mean_gain(lame_first, shear, density_cells, mask, omega_sq, impedance)
    axes = ("gx", "gy", "col")
    coarse_x = tile_shape[0] // 4
    coarse_y = tile_shape[1] // 4
    grid_shape = (lax.axis_size("gx") * coarse_x, lax.axis_size("gy") * coarse_y)
    grid_at = (lax.axis_index("gx") * coarse_x, lax.axis_index("gy") * coarse_y)

    def block_sums(cells):
        lead = cells.shape[:-3]
        local = cells.reshape(lead + (coarse_x, 4, coarse_y, 4, tile_shape[2]))
        local = local.sum(axis=(-4, -2, -1))
        grid = jnp.zeros(lead + grid_shape, jnp.float32)
        return lax.dynamic_update_slice(grid, local, (0,) * len(lead) + grid_at)

    forward_cells = forward.astype(jnp.float32)
    forward_real = forward_cells[:3]
    forward_imag = forward_cells[3:]
    plain_real = gain_real * forward_real - gain_imag * forward_imag
    plain_imag = gain_real * forward_imag + gain_imag * forward_real
    response_real = plain_real - DAMPING * plain_imag
    response_imag = plain_imag + DAMPING * plain_real
    response = block_sums(jnp.concatenate([response_real, response_imag]))
    field = warm.astype(jnp.float32)
    padded = with_halo(field, (("gx", 1),), 1)
    after_x = 0.0 * padded[0, 0, 0, 0]
    first = group_sum(
        jnp.concatenate(
            [
                jnp.sum(mask * field, axis=(1, 2, 3)),
                jnp.sum(gain_real, axis=(1, 2, 3)),
                jnp.sum(gain_imag, axis=(1, 2, 3)),
                response.reshape(-1),
            ]
        )
        + after_x,
        axes,
    )
    mean_field = first[:6] / count
    gain_total_real = first[6:9]
    gain_total_imag = first[9:12]
    response = first[12:].reshape(response.shape)
    sweep_args = (lame_first, shear, density_cells, mask, source_cells, omega_sq, impedance)
    padded = with_halo(padded, (("gy", 2),), 1)
    padded = with_halo(padded, (("col", 3),), 1, 0.0 * jnp.sum(mean_field))
    field = sweep(padded, *sweep_args)
    second_local = jnp.sum(mask * field, axis=(1, 2, 3))
    field = add_mean(field, gain_real, gain_imag, mean_field)
    padded = with_halo(field, (("gx", 1), ("gy", 2), ("col", 3)), 1)
    field = sweep(padded, *sweep_args)
    correlation = (
        field[:3] * forward_real
        - field[3:] * forward_imag
        - DAMPING * (field[:3] * forward_imag + field[3:] * forward_real)
    )
    cell_terms = -omega_sq * jnp.sum(correlation, axis=0)
    last = group_sum(jnp.concatenate([second_local, block_sums(cell_terms).reshape(-1)]), axes)
    second = last[:6]
    mean_real = mean_field[:3]
    mean_imag = mean_field[3:]
    total_real = second[:3] + (gain_total_real * mean_real - gain_total_imag * mean_imag)
    total_imag = second[3:] + (gain_total_real * mean_imag + gain_total_imag * mean_real)
    late_mean = jnp.concatenate([total_real, total_imag]) / count
    field = add_mean(field, gain_real, gain_imag, late_mean)
    late_terms = jnp.sum(
        late_mean[:3, None, None] * response[:3] - late_mean[3:, None, None] * response[3:], axis=0
    )
    coarse = (last[6:].reshape(grid_shape) - omega_sq * late_terms) / 64.0
    return (field, coarse)


def solution(mesh):
    in_specs = (
        P("freq", "gx", "gy", "col"),
        P("freq", "gx", "gy", "col"),
        P("freq", "gx", "gy", "col"),
        P("gx", "gy", "col"),
        P("gx", "gy", "col"),
        P(),
        P(("gx", "gy", "col"), None),
        P(),
        P("freq"),
    )
    out_specs = (P("freq", "gx", "gy", "col"), P("freq", None))
    return jax.shard_map(shards, mesh=mesh, in_specs=in_specs, out_specs=out_specs, check_vma=False)
```

```python
import jax
import jax.numpy as jnp
from jax import lax
from jax.sharding import PartitionSpec as P

DAMPING = 0.5
RELAXATION = 0.6


def with_halo(array, sides, width):
    for axis, dim in sides:
        peers, length = (lax.axis_size(axis), array.shape[dim])
        last = lax.slice_in_dim(array, length - width, length, axis=dim)
        initial = lax.slice_in_dim(array, 0, width, axis=dim)
        if peers == 2 and dim == array.ndim - 1:
            first = lax.axis_index(axis) == 0
            got = lax.ppermute(array, axis, [(0, 1), (1, 0)])
            got_last = lax.slice_in_dim(got, length - width, length, axis=dim)
            got_initial = lax.slice_in_dim(got, 0, width, axis=dim)
            zero = jnp.zeros_like(got_last)
            before = jnp.where(first, zero, got_last)
            after = jnp.where(first, got_initial, zero)
        elif peers == 2:
            first = lax.axis_index(axis) == 0
            got = lax.ppermute(jnp.where(first, last, initial), axis, [(0, 1), (1, 0)])
            zero = jnp.zeros_like(got)
            before = jnp.where(first, zero, got)
            after = jnp.where(first, got, zero)
        else:
            up = [(i, (i + 1) % peers) for i in range(peers - 1)]
            down = [(j, i) for i, j in up]
            before = lax.ppermute(last, axis, up)
            after = lax.ppermute(initial, axis, down)
        array = jnp.concatenate([before, array, after], axis=dim)
    return array


def window(padded, offset):
    size_x = padded.shape[1] - 2
    size_y = padded.shape[2] - 2
    size_z = padded.shape[3] - 2
    return padded[
        :,
        1 + offset[0] : 1 + offset[0] + size_x,
        1 + offset[1] : 1 + offset[1] + size_y,
        1 + offset[2] : 1 + offset[2] + size_z,
    ]


def navier(padded, lame_first, shear):
    units = ((1, 0, 0), (0, 1, 0), (0, 0, 1))
    centre = window(padded, (0, 0, 0))
    second = []
    for axis_d in range(3):
        ahead = units[axis_d]
        behind = tuple((-value for value in ahead))
        second.append(window(padded, ahead) + window(padded, behind) - 2.0 * centre)
    laplace = second[0] + second[1] + second[2]
    result = []
    for part_index in range(2):
        for component in range(3):
            channel = part_index * 3 + component
            divergence = second[component][channel]
            for other_axis in range(3):
                if other_axis != component:
                    source_channel = part_index * 3 + other_axis
                    single = padded[source_channel : source_channel + 1]
                    first_unit = units[component]
                    other_unit = units[other_axis]
                    plus_plus = tuple((first_unit[k] + other_unit[k] for k in range(3)))
                    plus_minus = tuple((first_unit[k] - other_unit[k] for k in range(3)))
                    minus_plus = tuple((-first_unit[k] + other_unit[k] for k in range(3)))
                    minus_minus = tuple((-first_unit[k] - other_unit[k] for k in range(3)))
                    mixed = (
                        window(single, plus_plus)
                        - window(single, plus_minus)
                        - window(single, minus_plus)
                        + window(single, minus_minus)
                    )
                    divergence = divergence + 0.25 * mixed[0]
            result.append(shear * laplace[channel] + (lame_first + shear) * divergence)
    return jnp.stack(result)


def sweep(padded, lame_first, shear, density, mask, source, omega_sq, impedance):
    field = window(padded, (0, 0, 0))
    elastic = navier(padded, lame_first, shear)
    real_part = field[:3]
    imag_part = field[3:]
    imp_real = impedance[0][:, None, None, None]
    imp_imag = impedance[1][:, None, None, None]
    inertia = omega_sq * density
    apply_real = (
        -elastic[:3]
        - inertia * (real_part - DAMPING * imag_part)
        + mask * (imp_real * real_part - imp_imag * imag_part)
    )
    apply_imag = (
        -elastic[3:]
        - inertia * (imag_part + DAMPING * real_part)
        + mask * (imp_real * imag_part + imp_imag * real_part)
    )
    resid_real = source[:3] - apply_real
    resid_imag = source[3:] - apply_imag
    diag_real = 8.0 * shear + 2.0 * lame_first - inertia + mask * imp_real
    diag_imag = -DAMPING * inertia + mask * imp_imag
    modulus = diag_real * diag_real + diag_imag * diag_imag
    new_real = real_part + RELAXATION * (resid_real * diag_real + resid_imag * diag_imag) / modulus
    new_imag = imag_part + RELAXATION * (resid_imag * diag_real - resid_real * diag_imag) / modulus
    return jnp.concatenate([new_real, new_imag], 0)


def mean_gain(lame_first, shear, density, mask, omega_sq, impedance):
    imp_real = impedance[0][:, None, None, None]
    imp_imag = impedance[1][:, None, None, None]
    inertia = omega_sq * density
    diag_real = 8.0 * shear + 2.0 * lame_first - inertia + mask * imp_real
    diag_imag = -DAMPING * inertia + mask * imp_imag
    scale = RELAXATION * mask / (diag_real * diag_real + diag_imag * diag_imag)
    gain_real = scale * (imp_real * diag_real + imp_imag * diag_imag)
    gain_imag = scale * (imp_imag * diag_real - imp_real * diag_imag)
    return gain_real, gain_imag


def add_mean(field, gain_real, gain_imag, mean_field):
    mean_real = mean_field[:3][:, None, None, None]
    mean_imag = mean_field[3:][:, None, None, None]
    new_real = field[:3] + (gain_real * mean_real - gain_imag * mean_imag)
    new_imag = field[3:] + (gain_real * mean_imag + gain_imag * mean_real)
    return jnp.concatenate([new_real, new_imag], 0)


def group_sum(value, axes):
    size = 1
    for axis in axes:
        size *= lax.axis_size(axis)
    if size & (size - 1):
        return lax.psum(value, axes)
    stride = 1
    while stride < size:
        if stride * 4 <= size:
            got = [
                lax.ppermute(value, axes, [(i, i ^ (m * stride)) for i in range(size)])
                for m in (1, 2, 3)
            ]
            value = (value + got[0]) + (got[1] + got[2])
            stride *= 4
        else:
            value = value + lax.ppermute(value, axes, [(i, i ^ stride) for i in range(size)])
            stride *= 2
    return value


def expand(blocks):
    blocks_x, blocks_y, blocks_z = blocks.shape
    spread = jnp.broadcast_to(
        blocks[:, None, :, None, :, None], (blocks_x, 8, blocks_y, 8, blocks_z, 32)
    )
    return spread.reshape(blocks_x * 8, blocks_y * 8, blocks_z * 32)


def material(block_ids, table):
    entries = lax.broadcasted_iota(jnp.int32, block_ids.shape + (table.shape[0],), block_ids.ndim)
    chosen = block_ids[..., None] == entries
    lame_first = jnp.sum(jnp.where(chosen, table[:, 0], 0.0), axis=-1)
    shear = jnp.sum(jnp.where(chosen, table[:, 1], 0.0), axis=-1)
    return (lame_first, shear)


def shards(
    source, warm, forward, density, material_map, material_table, iface_cells, impedance, omega2
):
    omega_sq = omega2[0]
    tile_shape = density.shape
    tile_cells = tile_shape[0] * tile_shape[1] * tile_shape[2]
    mask = jnp.zeros((tile_cells,), jnp.float32).at[iface_cells[0]].set(1.0).reshape(tile_shape)
    lame_tiles, shear_tiles = material(material_map, material_table)
    lame_first = expand(lame_tiles)
    shear = expand(shear_tiles)
    density_cells = density.astype(jnp.float32)
    source_cells = source.astype(jnp.float32)
    group_size = lax.axis_size("gx") * lax.axis_size("gy") * lax.axis_size("col")
    count = jnp.float32(group_size * iface_cells.shape[1])
    gain_real, gain_imag = mean_gain(lame_first, shear, density_cells, mask, omega_sq, impedance)
    axes = ("gx", "gy", "col")
    coarse_x = tile_shape[0] // 4
    coarse_y = tile_shape[1] // 4
    grid_shape = (lax.axis_size("gx") * coarse_x, lax.axis_size("gy") * coarse_y)
    grid_at = (lax.axis_index("gx") * coarse_x, lax.axis_index("gy") * coarse_y)

    def block_sums(cells):
        lead = cells.shape[:-3]
        local = cells.reshape(lead + (coarse_x, 4, coarse_y, 4, tile_shape[2]))
        local = local.sum(axis=(-4, -2, -1))
        grid = jnp.zeros(lead + grid_shape, jnp.float32)
        return lax.dynamic_update_slice(grid, local, (0,) * len(lead) + grid_at)

    forward_cells = forward.astype(jnp.float32)
    forward_real = forward_cells[:3]
    forward_imag = forward_cells[3:]
    plain_real = gain_real * forward_real - gain_imag * forward_imag
    plain_imag = gain_real * forward_imag + gain_imag * forward_real
    response_real = plain_real - DAMPING * plain_imag
    response_imag = plain_imag + DAMPING * plain_real
    response = block_sums(jnp.concatenate([response_real, response_imag]))
    field = warm.astype(jnp.float32)
    first = group_sum(
        jnp.concatenate(
            [
                jnp.sum(mask * field, axis=(1, 2, 3)),
                jnp.sum(gain_real, axis=(1, 2, 3)),
                jnp.sum(gain_imag, axis=(1, 2, 3)),
                response.reshape(-1),
            ]
        ),
        axes,
    )
    mean_field = first[:6] / count
    gain_total_real = first[6:9]
    gain_total_imag = first[9:12]
    response = first[12:].reshape(response.shape)
    sweep_args = (lame_first, shear, density_cells, mask, source_cells, omega_sq, impedance)
    padded = with_halo(field, (("gx", 1), ("gy", 2), ("col", 3)), 1)
    field = sweep(padded, *sweep_args)
    second_local = jnp.sum(mask * field, axis=(1, 2, 3))
    field = add_mean(field, gain_real, gain_imag, mean_field)
    padded = with_halo(field, (("gx", 1), ("gy", 2), ("col", 3)), 1)
    field = sweep(padded, *sweep_args)
    correlation = (
        field[:3] * forward_real
        - field[3:] * forward_imag
        - DAMPING * (field[:3] * forward_imag + field[3:] * forward_real)
    )
    cell_terms = -omega_sq * jnp.sum(correlation, axis=0)
    last = group_sum(jnp.concatenate([second_local, block_sums(cell_terms).reshape(-1)]), axes)
    second = last[:6]
    mean_real = mean_field[:3]
    mean_imag = mean_field[3:]
    total_real = second[:3] + (gain_total_real * mean_real - gain_total_imag * mean_imag)
    total_imag = second[3:] + (gain_total_real * mean_imag + gain_total_imag * mean_real)
    late_mean = jnp.concatenate([total_real, total_imag]) / count
    field = add_mean(field, gain_real, gain_imag, late_mean)
    late_terms = jnp.sum(
        late_mean[:3, None, None] * response[:3] - late_mean[3:, None, None] * response[3:], axis=0
    )
    coarse = (last[6:].reshape(grid_shape) - omega_sq * late_terms) / 64.0
    return (field, coarse)


def solution(mesh):
    in_specs = (
        P("freq", "gx", "gy", "col"),
        P("freq", "gx", "gy", "col"),
        P("freq", "gx", "gy", "col"),
        P("gx", "gy", "col"),
        P("gx", "gy", "col"),
        P(),
        P(("gx", "gy", "col"), None),
        P(),
        P("freq"),
    )
    out_specs = (P("freq", "gx", "gy", "col"), P("freq", None))
    return jax.shard_map(shards, mesh=mesh, in_specs=in_specs, out_specs=out_specs, check_vma=False)
```

```python
import jax
import jax.numpy as jnp
from jax import lax
from jax.sharding import PartitionSpec as P

DAMPING = 0.5
RELAXATION = 0.6


def with_halo(array, sides, width):
    for axis, dim in sides:
        peers, length = (lax.axis_size(axis), array.shape[dim])
        last = lax.slice_in_dim(array, length - width, length, axis=dim)
        initial = lax.slice_in_dim(array, 0, width, axis=dim)
        if peers == 2 and dim == array.ndim - 1:
            first = lax.axis_index(axis) == 0
            got = lax.ppermute(array, axis, [(0, 1), (1, 0)])
            got_last = lax.slice_in_dim(got, length - width, length, axis=dim)
            got_initial = lax.slice_in_dim(got, 0, width, axis=dim)
            zero = jnp.zeros_like(got_last)
            before = jnp.where(first, zero, got_last)
            after = jnp.where(first, got_initial, zero)
        elif peers == 2:
            first = lax.axis_index(axis) == 0
            got = lax.ppermute(jnp.where(first, last, initial), axis, [(0, 1), (1, 0)])
            zero = jnp.zeros_like(got)
            before = jnp.where(first, zero, got)
            after = jnp.where(first, got, zero)
        else:
            up = [(i, (i + 1) % peers) for i in range(peers - 1)]
            down = [(j, i) for i, j in up]
            before = lax.ppermute(last, axis, up)
            after = lax.ppermute(initial, axis, down)
        array = jnp.concatenate([before, array, after], axis=dim)
    return array


def window(padded, offset):
    size_x = padded.shape[1] - 2
    size_y = padded.shape[2] - 2
    size_z = padded.shape[3] - 2
    return padded[
        :,
        1 + offset[0] : 1 + offset[0] + size_x,
        1 + offset[1] : 1 + offset[1] + size_y,
        1 + offset[2] : 1 + offset[2] + size_z,
    ]


def navier(padded, lame_first, shear):
    units = ((1, 0, 0), (0, 1, 0), (0, 0, 1))
    centre = window(padded, (0, 0, 0))
    second = []
    for axis_d in range(3):
        ahead = units[axis_d]
        behind = tuple((-value for value in ahead))
        second.append(window(padded, ahead) + window(padded, behind) - 2.0 * centre)
    laplace = second[0] + second[1] + second[2]
    result = []
    for part_index in range(2):
        for component in range(3):
            channel = part_index * 3 + component
            divergence = second[component][channel]
            for other_axis in range(3):
                if other_axis != component:
                    source_channel = part_index * 3 + other_axis
                    single = padded[source_channel : source_channel + 1]
                    first_unit = units[component]
                    other_unit = units[other_axis]
                    plus_plus = tuple((first_unit[k] + other_unit[k] for k in range(3)))
                    plus_minus = tuple((first_unit[k] - other_unit[k] for k in range(3)))
                    minus_plus = tuple((-first_unit[k] + other_unit[k] for k in range(3)))
                    minus_minus = tuple((-first_unit[k] - other_unit[k] for k in range(3)))
                    mixed = (
                        window(single, plus_plus)
                        - window(single, plus_minus)
                        - window(single, minus_plus)
                        + window(single, minus_minus)
                    )
                    divergence = divergence + 0.25 * mixed[0]
            result.append(shear * laplace[channel] + (lame_first + shear) * divergence)
    return jnp.stack(result)


def sweep(padded, lame_first, shear, density, mask, source, omega_sq, impedance):
    field = window(padded, (0, 0, 0))
    elastic = navier(padded, lame_first, shear)
    real_part = field[:3]
    imag_part = field[3:]
    imp_real = impedance[0][:, None, None, None]
    imp_imag = impedance[1][:, None, None, None]
    inertia = omega_sq * density
    apply_real = (
        -elastic[:3]
        - inertia * (real_part - DAMPING * imag_part)
        + mask * (imp_real * real_part - imp_imag * imag_part)
    )
    apply_imag = (
        -elastic[3:]
        - inertia * (imag_part + DAMPING * real_part)
        + mask * (imp_real * imag_part + imp_imag * real_part)
    )
    resid_real = source[:3] - apply_real
    resid_imag = source[3:] - apply_imag
    diag_real = 8.0 * shear + 2.0 * lame_first - inertia + mask * imp_real
    diag_imag = -DAMPING * inertia + mask * imp_imag
    modulus = diag_real * diag_real + diag_imag * diag_imag
    new_real = real_part + RELAXATION * (resid_real * diag_real + resid_imag * diag_imag) / modulus
    new_imag = imag_part + RELAXATION * (resid_imag * diag_real - resid_real * diag_imag) / modulus
    return jnp.concatenate([new_real, new_imag], 0)


def mean_gain(lame_first, shear, density, mask, omega_sq, impedance):
    imp_real = impedance[0][:, None, None, None]
    imp_imag = impedance[1][:, None, None, None]
    inertia = omega_sq * density
    diag_real = 8.0 * shear + 2.0 * lame_first - inertia + mask * imp_real
    diag_imag = -DAMPING * inertia + mask * imp_imag
    scale = RELAXATION * mask / (diag_real * diag_real + diag_imag * diag_imag)
    gain_real = scale * (imp_real * diag_real + imp_imag * diag_imag)
    gain_imag = scale * (imp_imag * diag_real - imp_real * diag_imag)
    return gain_real, gain_imag


def add_mean(field, gain_real, gain_imag, mean_field):
    mean_real = mean_field[:3][:, None, None, None]
    mean_imag = mean_field[3:][:, None, None, None]
    new_real = field[:3] + (gain_real * mean_real - gain_imag * mean_imag)
    new_imag = field[3:] + (gain_real * mean_imag + gain_imag * mean_real)
    return jnp.concatenate([new_real, new_imag], 0)


def group_sum(value, axes):
    size = 1
    for axis in axes:
        size *= lax.axis_size(axis)
    if size & (size - 1):
        return lax.psum(value, axes)
    stride = 1
    while stride < size:
        if stride * 4 <= size:
            got = [
                lax.ppermute(value, axes, [(i, i ^ (m * stride)) for i in range(size)])
                for m in (1, 2, 3)
            ]
            value = (value + got[0]) + (got[1] + got[2])
            stride *= 4
        else:
            value = value + lax.ppermute(value, axes, [(i, i ^ stride) for i in range(size)])
            stride *= 2
    return value


def expand(blocks):
    blocks_x, blocks_y, blocks_z = blocks.shape
    spread = jnp.broadcast_to(
        blocks[:, None, :, None, :, None], (blocks_x, 8, blocks_y, 8, blocks_z, 32)
    )
    return spread.reshape(blocks_x * 8, blocks_y * 8, blocks_z * 32)


def material(block_ids, table):
    entries = lax.broadcasted_iota(jnp.int32, block_ids.shape + (table.shape[0],), block_ids.ndim)
    chosen = block_ids[..., None] == entries
    lame_first = jnp.sum(jnp.where(chosen, table[:, 0], 0.0), axis=-1)
    shear = jnp.sum(jnp.where(chosen, table[:, 1], 0.0), axis=-1)
    return (lame_first, shear)


def shards(
    source, warm, forward, density, material_map, material_table, iface_cells, impedance, omega2
):
    omega_sq = omega2[0]
    tile_shape = density.shape
    tile_cells = tile_shape[0] * tile_shape[1] * tile_shape[2]
    mask = jnp.zeros((tile_cells,), jnp.float32).at[iface_cells[0]].set(1.0).reshape(tile_shape)
    lame_tiles, shear_tiles = material(material_map, material_table)
    lame_first = expand(lame_tiles)
    shear = expand(shear_tiles)
    density_cells = density.astype(jnp.float32)
    source_cells = source.astype(jnp.float32)
    group_size = lax.axis_size("gx") * lax.axis_size("gy") * lax.axis_size("col")
    count = jnp.float32(group_size * iface_cells.shape[1])
    gain_real, gain_imag = mean_gain(lame_first, shear, density_cells, mask, omega_sq, impedance)
    axes = ("gx", "gy", "col")
    coarse_x = tile_shape[0] // 4
    coarse_y = tile_shape[1] // 4
    grid_shape = (lax.axis_size("gx") * coarse_x, lax.axis_size("gy") * coarse_y)
    grid_at = (lax.axis_index("gx") * coarse_x, lax.axis_index("gy") * coarse_y)

    def block_sums(cells):
        lead = cells.shape[:-3]
        local = cells.reshape(lead + (coarse_x, 4, coarse_y, 4, tile_shape[2]))
        local = local.sum(axis=(-4, -2, -1))
        grid = jnp.zeros(lead + grid_shape, jnp.float32)
        return lax.dynamic_update_slice(grid, local, (0,) * len(lead) + grid_at)

    forward_cells = forward.astype(jnp.float32)
    forward_real = forward_cells[:3]
    forward_imag = forward_cells[3:]
    plain_real = gain_real * forward_real - gain_imag * forward_imag
    plain_imag = gain_real * forward_imag + gain_imag * forward_real
    response_real = plain_real - DAMPING * plain_imag
    response_imag = plain_imag + DAMPING * plain_real
    response = block_sums(jnp.concatenate([response_real, response_imag]))
    field = warm.astype(jnp.float32)
    first = group_sum(
        jnp.concatenate(
            [
                jnp.sum(mask * field, axis=(1, 2, 3)),
                jnp.sum(gain_real, axis=(1, 2, 3)),
                jnp.sum(gain_imag, axis=(1, 2, 3)),
            ]
        ),
        axes,
    )
    mean_field = first[:6] / count
    gain_total_real = first[6:9]
    gain_total_imag = first[9:12]
    sweep_args = (lame_first, shear, density_cells, mask, source_cells, omega_sq, impedance)
    padded = with_halo(field, (("gx", 1), ("gy", 2), ("col", 3)), 1)
    field = sweep(padded, *sweep_args)
    second_local = jnp.sum(mask * field, axis=(1, 2, 3))
    field = add_mean(field, gain_real, gain_imag, mean_field)
    padded = with_halo(field, (("gx", 1), ("gy", 2), ("col", 3)), 1)
    field = sweep(padded, *sweep_args)
    correlation = (
        field[:3] * forward_real
        - field[3:] * forward_imag
        - DAMPING * (field[:3] * forward_imag + field[3:] * forward_real)
    )
    cell_terms = -omega_sq * jnp.sum(correlation, axis=0)
    last = group_sum(
        jnp.concatenate([second_local, block_sums(cell_terms).reshape(-1), response.reshape(-1)]),
        axes,
    )
    second = last[:6]
    grid_size = grid_shape[0] * grid_shape[1]
    response = last[6 + grid_size :].reshape(response.shape)
    mean_real = mean_field[:3]
    mean_imag = mean_field[3:]
    total_real = second[:3] + (gain_total_real * mean_real - gain_total_imag * mean_imag)
    total_imag = second[3:] + (gain_total_real * mean_imag + gain_total_imag * mean_real)
    late_mean = jnp.concatenate([total_real, total_imag]) / count
    field = add_mean(field, gain_real, gain_imag, late_mean)
    late_terms = jnp.sum(
        late_mean[:3, None, None] * response[:3] - late_mean[3:, None, None] * response[3:], axis=0
    )
    coarse = (last[6 : 6 + grid_size].reshape(grid_shape) - omega_sq * late_terms) / 64.0
    return (field, coarse)


def solution(mesh):
    in_specs = (
        P("freq", "gx", "gy", "col"),
        P("freq", "gx", "gy", "col"),
        P("freq", "gx", "gy", "col"),
        P("gx", "gy", "col"),
        P("gx", "gy", "col"),
        P(),
        P(("gx", "gy", "col"), None),
        P(),
        P("freq"),
    )
    out_specs = (P("freq", "gx", "gy", "col"), P("freq", None))
    return jax.shard_map(shards, mesh=mesh, in_specs=in_specs, out_specs=out_specs, check_vma=False)
```

```python
import jax
import jax.numpy as jnp
from jax import lax
from jax.sharding import PartitionSpec as P

DAMPING = 0.5
RELAXATION = 0.6


def with_halo(array, sides, width, tie=None):
    for axis, dim in sides:
        peers, length = (lax.axis_size(axis), array.shape[dim])
        last = lax.slice_in_dim(array, length - width, length, axis=dim)
        initial = lax.slice_in_dim(array, 0, width, axis=dim)
        if peers == 2 and dim == array.ndim - 1:
            first = lax.axis_index(axis) == 0
            sent = array if tie is None else array + tie
            got = lax.ppermute(sent, axis, [(0, 1), (1, 0)])
            got_last = lax.slice_in_dim(got, length - width, length, axis=dim)
            got_initial = lax.slice_in_dim(got, 0, width, axis=dim)
            zero = jnp.zeros_like(got_last)
            before = jnp.where(first, zero, got_last)
            after = jnp.where(first, got_initial, zero)
        elif peers == 2:
            first = lax.axis_index(axis) == 0
            got = lax.ppermute(jnp.where(first, last, initial), axis, [(0, 1), (1, 0)])
            zero = jnp.zeros_like(got)
            before = jnp.where(first, zero, got)
            after = jnp.where(first, got, zero)
        else:
            up = [(i, (i + 1) % peers) for i in range(peers - 1)]
            down = [(j, i) for i, j in up]
            before = lax.ppermute(last, axis, up)
            after = lax.ppermute(initial, axis, down)
        array = jnp.concatenate([before, array, after], axis=dim)
    return array


def window(padded, offset):
    size_x = padded.shape[1] - 2
    size_y = padded.shape[2] - 2
    size_z = padded.shape[3] - 2
    return padded[
        :,
        1 + offset[0] : 1 + offset[0] + size_x,
        1 + offset[1] : 1 + offset[1] + size_y,
        1 + offset[2] : 1 + offset[2] + size_z,
    ]


def navier(padded, lame_first, shear):
    units = ((1, 0, 0), (0, 1, 0), (0, 0, 1))
    centre = window(padded, (0, 0, 0))
    second = []
    for axis_d in range(3):
        ahead = units[axis_d]
        behind = tuple((-value for value in ahead))
        second.append(window(padded, ahead) + window(padded, behind) - 2.0 * centre)
    laplace = second[0] + second[1] + second[2]
    result = []
    for part_index in range(2):
        for component in range(3):
            channel = part_index * 3 + component
            divergence = second[component][channel]
            for other_axis in range(3):
                if other_axis != component:
                    source_channel = part_index * 3 + other_axis
                    single = padded[source_channel : source_channel + 1]
                    first_unit = units[component]
                    other_unit = units[other_axis]
                    plus_plus = tuple((first_unit[k] + other_unit[k] for k in range(3)))
                    plus_minus = tuple((first_unit[k] - other_unit[k] for k in range(3)))
                    minus_plus = tuple((-first_unit[k] + other_unit[k] for k in range(3)))
                    minus_minus = tuple((-first_unit[k] - other_unit[k] for k in range(3)))
                    mixed = (
                        window(single, plus_plus)
                        - window(single, plus_minus)
                        - window(single, minus_plus)
                        + window(single, minus_minus)
                    )
                    divergence = divergence + 0.25 * mixed[0]
            result.append(shear * laplace[channel] + (lame_first + shear) * divergence)
    return jnp.stack(result)


def sweep(padded, lame_first, shear, density, mask, source, omega_sq, impedance):
    field = window(padded, (0, 0, 0))
    elastic = navier(padded, lame_first, shear)
    real_part = field[:3]
    imag_part = field[3:]
    imp_real = impedance[0][:, None, None, None]
    imp_imag = impedance[1][:, None, None, None]
    inertia = omega_sq * density
    apply_real = (
        -elastic[:3]
        - inertia * (real_part - DAMPING * imag_part)
        + mask * (imp_real * real_part - imp_imag * imag_part)
    )
    apply_imag = (
        -elastic[3:]
        - inertia * (imag_part + DAMPING * real_part)
        + mask * (imp_real * imag_part + imp_imag * real_part)
    )
    resid_real = source[:3] - apply_real
    resid_imag = source[3:] - apply_imag
    diag_real = 8.0 * shear + 2.0 * lame_first - inertia + mask * imp_real
    diag_imag = -DAMPING * inertia + mask * imp_imag
    modulus = diag_real * diag_real + diag_imag * diag_imag
    new_real = real_part + RELAXATION * (resid_real * diag_real + resid_imag * diag_imag) / modulus
    new_imag = imag_part + RELAXATION * (resid_imag * diag_real - resid_real * diag_imag) / modulus
    return jnp.concatenate([new_real, new_imag], 0)


def mean_gain(lame_first, shear, density, mask, omega_sq, impedance):
    imp_real = impedance[0][:, None, None, None]
    imp_imag = impedance[1][:, None, None, None]
    inertia = omega_sq * density
    diag_real = 8.0 * shear + 2.0 * lame_first - inertia + mask * imp_real
    diag_imag = -DAMPING * inertia + mask * imp_imag
    scale = RELAXATION * mask / (diag_real * diag_real + diag_imag * diag_imag)
    gain_real = scale * (imp_real * diag_real + imp_imag * diag_imag)
    gain_imag = scale * (imp_imag * diag_real - imp_real * diag_imag)
    return gain_real, gain_imag


def add_mean(field, gain_real, gain_imag, mean_field):
    mean_real = mean_field[:3][:, None, None, None]
    mean_imag = mean_field[3:][:, None, None, None]
    new_real = field[:3] + (gain_real * mean_real - gain_imag * mean_imag)
    new_imag = field[3:] + (gain_real * mean_imag + gain_imag * mean_real)
    return jnp.concatenate([new_real, new_imag], 0)


def group_rounds(value, axes):
    size = 1
    for axis in axes:
        size *= lax.axis_size(axis)
    if size & (size - 1):
        return [lax.psum(value, axes)]
    rounds = []
    stride = 1
    while stride < size:
        if stride * 4 <= size:
            got = [
                lax.ppermute(value, axes, [(i, i ^ (m * stride)) for i in range(size)])
                for m in (1, 2, 3)
            ]
            value = (value + got[0]) + (got[1] + got[2])
            stride *= 4
        else:
            value = value + lax.ppermute(value, axes, [(i, i ^ stride) for i in range(size)])
            stride *= 2
        rounds.append(value)
    return rounds


def group_sum(value, axes):
    return group_rounds(value, axes)[-1]


def expand(blocks):
    blocks_x, blocks_y, blocks_z = blocks.shape
    spread = jnp.broadcast_to(
        blocks[:, None, :, None, :, None], (blocks_x, 8, blocks_y, 8, blocks_z, 32)
    )
    return spread.reshape(blocks_x * 8, blocks_y * 8, blocks_z * 32)


def material(block_ids, table):
    entries = lax.broadcasted_iota(jnp.int32, block_ids.shape + (table.shape[0],), block_ids.ndim)
    chosen = block_ids[..., None] == entries
    lame_first = jnp.sum(jnp.where(chosen, table[:, 0], 0.0), axis=-1)
    shear = jnp.sum(jnp.where(chosen, table[:, 1], 0.0), axis=-1)
    return (lame_first, shear)


def shards(
    source, warm, forward, density, material_map, material_table, iface_cells, impedance, omega2
):
    omega_sq = omega2[0]
    tile_shape = density.shape
    tile_cells = tile_shape[0] * tile_shape[1] * tile_shape[2]
    mask = jnp.zeros((tile_cells,), jnp.float32).at[iface_cells[0]].set(1.0).reshape(tile_shape)
    lame_tiles, shear_tiles = material(material_map, material_table)
    lame_first = expand(lame_tiles)
    shear = expand(shear_tiles)
    density_cells = density.astype(jnp.float32)
    source_cells = source.astype(jnp.float32)
    group_size = lax.axis_size("gx") * lax.axis_size("gy") * lax.axis_size("col")
    count = jnp.float32(group_size * iface_cells.shape[1])
    gain_real, gain_imag = mean_gain(lame_first, shear, density_cells, mask, omega_sq, impedance)
    axes = ("gx", "gy", "col")
    coarse_x = tile_shape[0] // 4
    coarse_y = tile_shape[1] // 4
    grid_shape = (lax.axis_size("gx") * coarse_x, lax.axis_size("gy") * coarse_y)
    grid_at = (lax.axis_index("gx") * coarse_x, lax.axis_index("gy") * coarse_y)

    def block_sums(cells):
        lead = cells.shape[:-3]
        local = cells.reshape(lead + (coarse_x, 4, coarse_y, 4, tile_shape[2]))
        local = local.sum(axis=(-4, -2, -1))
        grid = jnp.zeros(lead + grid_shape, jnp.float32)
        return lax.dynamic_update_slice(grid, local, (0,) * len(lead) + grid_at)

    forward_cells = forward.astype(jnp.float32)
    forward_real = forward_cells[:3]
    forward_imag = forward_cells[3:]
    plain_real = gain_real * forward_real - gain_imag * forward_imag
    plain_imag = gain_real * forward_imag + gain_imag * forward_real
    response_real = plain_real - DAMPING * plain_imag
    response_imag = plain_imag + DAMPING * plain_real
    response = block_sums(jnp.concatenate([response_real, response_imag]))
    field = warm.astype(jnp.float32)
    rounds = group_rounds(
        jnp.concatenate(
            [
                jnp.sum(mask * field, axis=(1, 2, 3)),
                jnp.sum(gain_real, axis=(1, 2, 3)),
                jnp.sum(gain_imag, axis=(1, 2, 3)),
            ]
        ),
        axes,
    )
    first = rounds[-1]
    mean_field = first[:6] / count
    gain_total_real = first[6:9]
    gain_total_imag = first[9:12]
    sweep_args = (lame_first, shear, density_cells, mask, source_cells, omega_sq, impedance)
    padded = with_halo(field, (("gx", 1), ("gy", 2)), 1)
    padded = with_halo(padded, (("col", 3),), 1, 0.0 * rounds[0][0])
    tied_source = source_cells + 0.0 * first[0]
    field = sweep(padded, lame_first, shear, density_cells, mask, tied_source, omega_sq, impedance)
    second_local = jnp.sum(mask * field, axis=(1, 2, 3))
    field = add_mean(field, gain_real, gain_imag, mean_field)
    padded = with_halo(field, (("gx", 1), ("gy", 2), ("col", 3)), 1)
    field = sweep(padded, *sweep_args)
    correlation = (
        field[:3] * forward_real
        - field[3:] * forward_imag
        - DAMPING * (field[:3] * forward_imag + field[3:] * forward_real)
    )
    cell_terms = -omega_sq * jnp.sum(correlation, axis=0)
    last = group_sum(
        jnp.concatenate([second_local, block_sums(cell_terms).reshape(-1), response.reshape(-1)]),
        axes,
    )
    second = last[:6]
    grid_size = grid_shape[0] * grid_shape[1]
    response = last[6 + grid_size :].reshape(response.shape)
    mean_real = mean_field[:3]
    mean_imag = mean_field[3:]
    total_real = second[:3] + (gain_total_real * mean_real - gain_total_imag * mean_imag)
    total_imag = second[3:] + (gain_total_real * mean_imag + gain_total_imag * mean_real)
    late_mean = jnp.concatenate([total_real, total_imag]) / count
    field = add_mean(field, gain_real, gain_imag, late_mean)
    late_terms = jnp.sum(
        late_mean[:3, None, None] * response[:3] - late_mean[3:, None, None] * response[3:], axis=0
    )
    coarse = (last[6 : 6 + grid_size].reshape(grid_shape) - omega_sq * late_terms) / 64.0
    return (field, coarse)


def solution(mesh):
    in_specs = (
        P("freq", "gx", "gy", "col"),
        P("freq", "gx", "gy", "col"),
        P("freq", "gx", "gy", "col"),
        P("gx", "gy", "col"),
        P("gx", "gy", "col"),
        P(),
        P(("gx", "gy", "col"), None),
        P(),
        P("freq"),
    )
    out_specs = (P("freq", "gx", "gy", "col"), P("freq", None))
    return jax.shard_map(shards, mesh=mesh, in_specs=in_specs, out_specs=out_specs, check_vma=False)
```

```python
import jax
import jax.numpy as jnp
from jax import lax
from jax.sharding import PartitionSpec as P

DAMPING = 0.5
RELAXATION = 0.6


def with_halo(array, sides, width, tie=None):
    for axis, dim in sides:
        peers, length = (lax.axis_size(axis), array.shape[dim])
        last = lax.slice_in_dim(array, length - width, length, axis=dim)
        initial = lax.slice_in_dim(array, 0, width, axis=dim)
        if peers == 2 and dim == array.ndim - 1:
            first = lax.axis_index(axis) == 0
            sent = array if tie is None else array + tie
            got = lax.ppermute(sent, axis, [(0, 1), (1, 0)])
            got_last = lax.slice_in_dim(got, length - width, length, axis=dim)
            got_initial = lax.slice_in_dim(got, 0, width, axis=dim)
            zero = jnp.zeros_like(got_last)
            before = jnp.where(first, zero, got_last)
            after = jnp.where(first, got_initial, zero)
        elif peers == 2:
            first = lax.axis_index(axis) == 0
            got = lax.ppermute(jnp.where(first, last, initial), axis, [(0, 1), (1, 0)])
            zero = jnp.zeros_like(got)
            before = jnp.where(first, zero, got)
            after = jnp.where(first, got, zero)
        else:
            up = [(i, (i + 1) % peers) for i in range(peers - 1)]
            down = [(j, i) for i, j in up]
            before = lax.ppermute(last, axis, up)
            after = lax.ppermute(initial, axis, down)
        array = jnp.concatenate([before, array, after], axis=dim)
    return array


def window(padded, offset):
    size_x = padded.shape[1] - 2
    size_y = padded.shape[2] - 2
    size_z = padded.shape[3] - 2
    return padded[
        :,
        1 + offset[0] : 1 + offset[0] + size_x,
        1 + offset[1] : 1 + offset[1] + size_y,
        1 + offset[2] : 1 + offset[2] + size_z,
    ]


def navier(padded, lame_first, shear):
    units = ((1, 0, 0), (0, 1, 0), (0, 0, 1))
    centre = window(padded, (0, 0, 0))
    second = []
    for axis_d in range(3):
        ahead = units[axis_d]
        behind = tuple((-value for value in ahead))
        second.append(window(padded, ahead) + window(padded, behind) - 2.0 * centre)
    laplace = second[0] + second[1] + second[2]
    result = []
    for part_index in range(2):
        for component in range(3):
            channel = part_index * 3 + component
            divergence = second[component][channel]
            for other_axis in range(3):
                if other_axis != component:
                    source_channel = part_index * 3 + other_axis
                    single = padded[source_channel : source_channel + 1]
                    first_unit = units[component]
                    other_unit = units[other_axis]
                    plus_plus = tuple((first_unit[k] + other_unit[k] for k in range(3)))
                    plus_minus = tuple((first_unit[k] - other_unit[k] for k in range(3)))
                    minus_plus = tuple((-first_unit[k] + other_unit[k] for k in range(3)))
                    minus_minus = tuple((-first_unit[k] - other_unit[k] for k in range(3)))
                    mixed = (
                        window(single, plus_plus)
                        - window(single, plus_minus)
                        - window(single, minus_plus)
                        + window(single, minus_minus)
                    )
                    divergence = divergence + 0.25 * mixed[0]
            result.append(shear * laplace[channel] + (lame_first + shear) * divergence)
    return jnp.stack(result)


def sweep(padded, lame_first, shear, density, mask, source, omega_sq, impedance):
    field = window(padded, (0, 0, 0))
    elastic = navier(padded, lame_first, shear)
    real_part = field[:3]
    imag_part = field[3:]
    imp_real = impedance[0][:, None, None, None]
    imp_imag = impedance[1][:, None, None, None]
    inertia = omega_sq * density
    apply_real = (
        -elastic[:3]
        - inertia * (real_part - DAMPING * imag_part)
        + mask * (imp_real * real_part - imp_imag * imag_part)
    )
    apply_imag = (
        -elastic[3:]
        - inertia * (imag_part + DAMPING * real_part)
        + mask * (imp_real * imag_part + imp_imag * real_part)
    )
    resid_real = source[:3] - apply_real
    resid_imag = source[3:] - apply_imag
    diag_real = 8.0 * shear + 2.0 * lame_first - inertia + mask * imp_real
    diag_imag = -DAMPING * inertia + mask * imp_imag
    modulus = diag_real * diag_real + diag_imag * diag_imag
    new_real = real_part + RELAXATION * (resid_real * diag_real + resid_imag * diag_imag) / modulus
    new_imag = imag_part + RELAXATION * (resid_imag * diag_real - resid_real * diag_imag) / modulus
    return jnp.concatenate([new_real, new_imag], 0)


def mean_gain(lame_first, shear, density, mask, omega_sq, impedance):
    imp_real = impedance[0][:, None, None, None]
    imp_imag = impedance[1][:, None, None, None]
    inertia = omega_sq * density
    diag_real = 8.0 * shear + 2.0 * lame_first - inertia + mask * imp_real
    diag_imag = -DAMPING * inertia + mask * imp_imag
    scale = RELAXATION * mask / (diag_real * diag_real + diag_imag * diag_imag)
    gain_real = scale * (imp_real * diag_real + imp_imag * diag_imag)
    gain_imag = scale * (imp_imag * diag_real - imp_real * diag_imag)
    return gain_real, gain_imag


def add_mean(field, gain_real, gain_imag, mean_field):
    mean_real = mean_field[:3][:, None, None, None]
    mean_imag = mean_field[3:][:, None, None, None]
    new_real = field[:3] + (gain_real * mean_real - gain_imag * mean_imag)
    new_imag = field[3:] + (gain_real * mean_imag + gain_imag * mean_real)
    return jnp.concatenate([new_real, new_imag], 0)


def group_rounds(value, axes, radix=4):
    size = 1
    for axis in axes:
        size *= lax.axis_size(axis)
    if size & (size - 1):
        return [lax.psum(value, axes)]
    rounds = []
    stride = 1
    while stride < size:
        if radix == 4 and stride * 4 <= size:
            got = [
                lax.ppermute(value, axes, [(i, i ^ (m * stride)) for i in range(size)])
                for m in (1, 2, 3)
            ]
            value = (value + got[0]) + (got[1] + got[2])
            stride *= 4
        else:
            value = value + lax.ppermute(value, axes, [(i, i ^ stride) for i in range(size)])
            stride *= 2
        rounds.append(value)
    return rounds


def group_sum(value, axes):
    return group_rounds(value, axes)[-1]


def expand(blocks):
    blocks_x, blocks_y, blocks_z = blocks.shape
    spread = jnp.broadcast_to(
        blocks[:, None, :, None, :, None], (blocks_x, 8, blocks_y, 8, blocks_z, 32)
    )
    return spread.reshape(blocks_x * 8, blocks_y * 8, blocks_z * 32)


def material(block_ids, table):
    entries = lax.broadcasted_iota(jnp.int32, block_ids.shape + (table.shape[0],), block_ids.ndim)
    chosen = block_ids[..., None] == entries
    lame_first = jnp.sum(jnp.where(chosen, table[:, 0], 0.0), axis=-1)
    shear = jnp.sum(jnp.where(chosen, table[:, 1], 0.0), axis=-1)
    return (lame_first, shear)


def shards(
    source, warm, forward, density, material_map, material_table, iface_cells, impedance, omega2
):
    omega_sq = omega2[0]
    tile_shape = density.shape
    tile_cells = tile_shape[0] * tile_shape[1] * tile_shape[2]
    mask = jnp.zeros((tile_cells,), jnp.float32).at[iface_cells[0]].set(1.0).reshape(tile_shape)
    lame_tiles, shear_tiles = material(material_map, material_table)
    lame_first = expand(lame_tiles)
    shear = expand(shear_tiles)
    density_cells = density.astype(jnp.float32)
    source_cells = source.astype(jnp.float32)
    group_size = lax.axis_size("gx") * lax.axis_size("gy") * lax.axis_size("col")
    count = jnp.float32(group_size * iface_cells.shape[1])
    gain_real, gain_imag = mean_gain(lame_first, shear, density_cells, mask, omega_sq, impedance)
    axes = ("gx", "gy", "col")
    coarse_x = tile_shape[0] // 4
    coarse_y = tile_shape[1] // 4
    grid_shape = (lax.axis_size("gx") * coarse_x, lax.axis_size("gy") * coarse_y)
    grid_at = (lax.axis_index("gx") * coarse_x, lax.axis_index("gy") * coarse_y)

    def block_sums(cells):
        lead = cells.shape[:-3]
        local = cells.reshape(lead + (coarse_x, 4, coarse_y, 4, tile_shape[2]))
        local = local.sum(axis=(-4, -2, -1))
        grid = jnp.zeros(lead + grid_shape, jnp.float32)
        return lax.dynamic_update_slice(grid, local, (0,) * len(lead) + grid_at)

    forward_cells = forward.astype(jnp.float32)
    forward_real = forward_cells[:3]
    forward_imag = forward_cells[3:]
    plain_real = gain_real * forward_real - gain_imag * forward_imag
    plain_imag = gain_real * forward_imag + gain_imag * forward_real
    response_real = plain_real - DAMPING * plain_imag
    response_imag = plain_imag + DAMPING * plain_real
    response = block_sums(jnp.concatenate([response_real, response_imag]))
    field = warm.astype(jnp.float32)
    rounds = group_rounds(
        jnp.concatenate(
            [
                jnp.sum(mask * field, axis=(1, 2, 3)),
                jnp.sum(gain_real, axis=(1, 2, 3)),
                jnp.sum(gain_imag, axis=(1, 2, 3)),
            ]
        ),
        axes,
        radix=2,
    )
    first = rounds[-1]
    mean_field = first[:6] / count
    gain_total_real = first[6:9]
    gain_total_imag = first[9:12]
    sweep_args = (lame_first, shear, density_cells, mask, source_cells, omega_sq, impedance)
    padded = with_halo(field, (("gx", 1), ("gy", 2)), 1)
    padded = with_halo(padded, (("col", 3),), 1, 0.0 * rounds[(len(rounds) - 1) // 2][0])
    tied_source = source_cells + 0.0 * first[0]
    field = sweep(padded, lame_first, shear, density_cells, mask, tied_source, omega_sq, impedance)
    second_local = jnp.sum(mask * field, axis=(1, 2, 3))
    field = add_mean(field, gain_real, gain_imag, mean_field)
    padded = with_halo(field, (("gx", 1), ("gy", 2), ("col", 3)), 1)
    field = sweep(padded, *sweep_args)
    correlation = (
        field[:3] * forward_real
        - field[3:] * forward_imag
        - DAMPING * (field[:3] * forward_imag + field[3:] * forward_real)
    )
    cell_terms = -omega_sq * jnp.sum(correlation, axis=0)
    last = group_sum(
        jnp.concatenate([second_local, block_sums(cell_terms).reshape(-1), response.reshape(-1)]),
        axes,
    )
    second = last[:6]
    grid_size = grid_shape[0] * grid_shape[1]
    response = last[6 + grid_size :].reshape(response.shape)
    mean_real = mean_field[:3]
    mean_imag = mean_field[3:]
    total_real = second[:3] + (gain_total_real * mean_real - gain_total_imag * mean_imag)
    total_imag = second[3:] + (gain_total_real * mean_imag + gain_total_imag * mean_real)
    late_mean = jnp.concatenate([total_real, total_imag]) / count
    field = add_mean(field, gain_real, gain_imag, late_mean)
    late_terms = jnp.sum(
        late_mean[:3, None, None] * response[:3] - late_mean[3:, None, None] * response[3:], axis=0
    )
    coarse = (last[6 : 6 + grid_size].reshape(grid_shape) - omega_sq * late_terms) / 64.0
    return (field, coarse)


def solution(mesh):
    in_specs = (
        P("freq", "gx", "gy", "col"),
        P("freq", "gx", "gy", "col"),
        P("freq", "gx", "gy", "col"),
        P("gx", "gy", "col"),
        P("gx", "gy", "col"),
        P(),
        P(("gx", "gy", "col"), None),
        P(),
        P("freq"),
    )
    out_specs = (P("freq", "gx", "gy", "col"), P("freq", None))
    return jax.shard_map(shards, mesh=mesh, in_specs=in_specs, out_specs=out_specs, check_vma=False)
```

```python
import jax
import jax.numpy as jnp
from jax import lax
from jax.sharding import PartitionSpec as P

DAMPING = 0.5
RELAXATION = 0.6


def with_halo(array, sides, width, tie=None):
    for axis, dim in sides:
        peers, length = (lax.axis_size(axis), array.shape[dim])
        last = lax.slice_in_dim(array, length - width, length, axis=dim)
        initial = lax.slice_in_dim(array, 0, width, axis=dim)
        if peers == 2 and dim == array.ndim - 1:
            first = lax.axis_index(axis) == 0
            sent = array if tie is None else array + tie
            got = lax.ppermute(sent, axis, [(0, 1), (1, 0)])
            got_last = lax.slice_in_dim(got, length - width, length, axis=dim)
            got_initial = lax.slice_in_dim(got, 0, width, axis=dim)
            zero = jnp.zeros_like(got_last)
            before = jnp.where(first, zero, got_last)
            after = jnp.where(first, got_initial, zero)
        elif peers == 2:
            first = lax.axis_index(axis) == 0
            got = lax.ppermute(jnp.where(first, last, initial), axis, [(0, 1), (1, 0)])
            zero = jnp.zeros_like(got)
            before = jnp.where(first, zero, got)
            after = jnp.where(first, got, zero)
        else:
            up = [(i, (i + 1) % peers) for i in range(peers - 1)]
            down = [(j, i) for i, j in up]
            before = lax.ppermute(last, axis, up)
            after = lax.ppermute(initial, axis, down)
        array = jnp.concatenate([before, array, after], axis=dim)
    return array


def window(padded, offset):
    size_x = padded.shape[1] - 2
    size_y = padded.shape[2] - 2
    size_z = padded.shape[3] - 2
    return padded[
        :,
        1 + offset[0] : 1 + offset[0] + size_x,
        1 + offset[1] : 1 + offset[1] + size_y,
        1 + offset[2] : 1 + offset[2] + size_z,
    ]


def navier(padded, lame_first, shear):
    units = ((1, 0, 0), (0, 1, 0), (0, 0, 1))
    centre = window(padded, (0, 0, 0))
    second = []
    for axis_d in range(3):
        ahead = units[axis_d]
        behind = tuple((-value for value in ahead))
        second.append(window(padded, ahead) + window(padded, behind) - 2.0 * centre)
    laplace = second[0] + second[1] + second[2]
    result = []
    for part_index in range(2):
        for component in range(3):
            channel = part_index * 3 + component
            divergence = second[component][channel]
            for other_axis in range(3):
                if other_axis != component:
                    source_channel = part_index * 3 + other_axis
                    single = padded[source_channel : source_channel + 1]
                    first_unit = units[component]
                    other_unit = units[other_axis]
                    plus_plus = tuple((first_unit[k] + other_unit[k] for k in range(3)))
                    plus_minus = tuple((first_unit[k] - other_unit[k] for k in range(3)))
                    minus_plus = tuple((-first_unit[k] + other_unit[k] for k in range(3)))
                    minus_minus = tuple((-first_unit[k] - other_unit[k] for k in range(3)))
                    mixed = (
                        window(single, plus_plus)
                        - window(single, plus_minus)
                        - window(single, minus_plus)
                        + window(single, minus_minus)
                    )
                    divergence = divergence + 0.25 * mixed[0]
            result.append(shear * laplace[channel] + (lame_first + shear) * divergence)
    return jnp.stack(result)


def sweep(padded, lame_first, shear, density, mask, source, omega_sq, impedance):
    field = window(padded, (0, 0, 0))
    elastic = navier(padded, lame_first, shear)
    real_part = field[:3]
    imag_part = field[3:]
    imp_real = impedance[0][:, None, None, None]
    imp_imag = impedance[1][:, None, None, None]
    inertia = omega_sq * density
    apply_real = (
        -elastic[:3]
        - inertia * (real_part - DAMPING * imag_part)
        + mask * (imp_real * real_part - imp_imag * imag_part)
    )
    apply_imag = (
        -elastic[3:]
        - inertia * (imag_part + DAMPING * real_part)
        + mask * (imp_real * imag_part + imp_imag * real_part)
    )
    resid_real = source[:3] - apply_real
    resid_imag = source[3:] - apply_imag
    diag_real = 8.0 * shear + 2.0 * lame_first - inertia + mask * imp_real
    diag_imag = -DAMPING * inertia + mask * imp_imag
    modulus = diag_real * diag_real + diag_imag * diag_imag
    new_real = real_part + RELAXATION * (resid_real * diag_real + resid_imag * diag_imag) / modulus
    new_imag = imag_part + RELAXATION * (resid_imag * diag_real - resid_real * diag_imag) / modulus
    return jnp.concatenate([new_real, new_imag], 0)


def mean_gain(lame_first, shear, density, mask, omega_sq, impedance):
    imp_real = impedance[0][:, None, None, None]
    imp_imag = impedance[1][:, None, None, None]
    inertia = omega_sq * density
    diag_real = 8.0 * shear + 2.0 * lame_first - inertia + mask * imp_real
    diag_imag = -DAMPING * inertia + mask * imp_imag
    scale = RELAXATION * mask / (diag_real * diag_real + diag_imag * diag_imag)
    gain_real = scale * (imp_real * diag_real + imp_imag * diag_imag)
    gain_imag = scale * (imp_imag * diag_real - imp_real * diag_imag)
    return gain_real, gain_imag


def add_mean(field, gain_real, gain_imag, mean_field):
    mean_real = mean_field[:3][:, None, None, None]
    mean_imag = mean_field[3:][:, None, None, None]
    new_real = field[:3] + (gain_real * mean_real - gain_imag * mean_imag)
    new_imag = field[3:] + (gain_real * mean_imag + gain_imag * mean_real)
    return jnp.concatenate([new_real, new_imag], 0)


def group_rounds(value, axes):
    size = 1
    for axis in axes:
        size *= lax.axis_size(axis)
    if size & (size - 1):
        return [lax.psum(value, axes)]
    rounds = []
    stride = 1
    while stride < size:
        if stride * 4 <= size:
            got = [
                lax.ppermute(value, axes, [(i, i ^ (m * stride)) for i in range(size)])
                for m in (1, 2, 3)
            ]
            value = (value + got[0]) + (got[1] + got[2])
            stride *= 4
        else:
            value = value + lax.ppermute(value, axes, [(i, i ^ stride) for i in range(size)])
            stride *= 2
        rounds.append(value)
    return rounds


def group_sum(value, axes):
    return group_rounds(value, axes)[-1]


def expand(blocks):
    blocks_x, blocks_y, blocks_z = blocks.shape
    depth_tile = lax.broadcasted_iota(jnp.int32, (1, 1, blocks_z * 32), 2) // 32
    rows = jnp.zeros((blocks_x, blocks_y, blocks_z * 32), blocks.dtype)
    for tile in range(blocks_z):
        rows = jnp.where(depth_tile == tile, blocks[:, :, tile : tile + 1], rows)
    spread = jnp.broadcast_to(
        rows[:, None, :, None, :], (blocks_x, 8, blocks_y, 8, blocks_z * 32)
    )
    return spread.reshape(blocks_x * 8, blocks_y * 8, blocks_z * 32)


def material(block_ids, table):
    entries = lax.broadcasted_iota(jnp.int32, block_ids.shape + (table.shape[0],), block_ids.ndim)
    chosen = block_ids[..., None] == entries
    lame_first = jnp.sum(jnp.where(chosen, table[:, 0], 0.0), axis=-1)
    shear = jnp.sum(jnp.where(chosen, table[:, 1], 0.0), axis=-1)
    return (lame_first, shear)


def shards(
    source, warm, forward, density, material_map, material_table, iface_cells, impedance, omega2
):
    omega_sq = omega2[0]
    tile_shape = density.shape
    tile_cells = tile_shape[0] * tile_shape[1] * tile_shape[2]
    mask = jnp.zeros((tile_cells,), jnp.float32).at[iface_cells[0]].set(1.0).reshape(tile_shape)
    lame_tiles, shear_tiles = material(material_map, material_table)
    lame_first = expand(lame_tiles)
    shear = expand(shear_tiles)
    density_cells = density.astype(jnp.float32)
    source_cells = source.astype(jnp.float32)
    group_size = lax.axis_size("gx") * lax.axis_size("gy") * lax.axis_size("col")
    count = jnp.float32(group_size * iface_cells.shape[1])
    gain_real, gain_imag = mean_gain(lame_first, shear, density_cells, mask, omega_sq, impedance)
    axes = ("gx", "gy", "col")
    coarse_x = tile_shape[0] // 4
    coarse_y = tile_shape[1] // 4
    grid_shape = (lax.axis_size("gx") * coarse_x, lax.axis_size("gy") * coarse_y)
    grid_at = (lax.axis_index("gx") * coarse_x, lax.axis_index("gy") * coarse_y)

    def block_sums(cells):
        lead = cells.shape[:-3]
        local = cells.reshape(lead + (coarse_x, 4, coarse_y, 4, tile_shape[2]))
        local = local.sum(axis=(-4, -2, -1))
        grid = jnp.zeros(lead + grid_shape, jnp.float32)
        return lax.dynamic_update_slice(grid, local, (0,) * len(lead) + grid_at)

    forward_cells = forward.astype(jnp.float32)
    forward_real = forward_cells[:3]
    forward_imag = forward_cells[3:]
    plain_real = gain_real * forward_real - gain_imag * forward_imag
    plain_imag = gain_real * forward_imag + gain_imag * forward_real
    response_real = plain_real - DAMPING * plain_imag
    response_imag = plain_imag + DAMPING * plain_real
    response = block_sums(jnp.concatenate([response_real, response_imag]))
    field = warm.astype(jnp.float32)
    rounds = group_rounds(
        jnp.concatenate(
            [
                jnp.sum(mask * field, axis=(1, 2, 3)),
                jnp.sum(gain_real, axis=(1, 2, 3)),
                jnp.sum(gain_imag, axis=(1, 2, 3)),
            ]
        ),
        axes,
    )
    first = rounds[-1]
    mean_field = first[:6] / count
    gain_total_real = first[6:9]
    gain_total_imag = first[9:12]
    sweep_args = (lame_first, shear, density_cells, mask, source_cells, omega_sq, impedance)
    padded = with_halo(field, (("gx", 1), ("gy", 2)), 1)
    padded = with_halo(padded, (("col", 3),), 1, 0.0 * rounds[0][0])
    tied_source = source_cells + 0.0 * first[0]
    field = sweep(padded, lame_first, shear, density_cells, mask, tied_source, omega_sq, impedance)
    second_local = jnp.sum(mask * field, axis=(1, 2, 3))
    field = add_mean(field, gain_real, gain_imag, mean_field)
    padded = with_halo(field, (("gx", 1), ("gy", 2), ("col", 3)), 1)
    field = sweep(padded, *sweep_args)
    correlation = (
        field[:3] * forward_real
        - field[3:] * forward_imag
        - DAMPING * (field[:3] * forward_imag + field[3:] * forward_real)
    )
    cell_terms = -omega_sq * jnp.sum(correlation, axis=0)
    last = group_sum(
        jnp.concatenate([second_local, block_sums(cell_terms).reshape(-1), response.reshape(-1)]),
        axes,
    )
    second = last[:6]
    grid_size = grid_shape[0] * grid_shape[1]
    response = last[6 + grid_size :].reshape(response.shape)
    mean_real = mean_field[:3]
    mean_imag = mean_field[3:]
    total_real = second[:3] + (gain_total_real * mean_real - gain_total_imag * mean_imag)
    total_imag = second[3:] + (gain_total_real * mean_imag + gain_total_imag * mean_real)
    late_mean = jnp.concatenate([total_real, total_imag]) / count
    field = add_mean(field, gain_real, gain_imag, late_mean)
    late_terms = jnp.sum(
        late_mean[:3, None, None] * response[:3] - late_mean[3:, None, None] * response[3:], axis=0
    )
    coarse = (last[6 : 6 + grid_size].reshape(grid_shape) - omega_sq * late_terms) / 64.0
    return (field, coarse)


def solution(mesh):
    in_specs = (
        P("freq", "gx", "gy", "col"),
        P("freq", "gx", "gy", "col"),
        P("freq", "gx", "gy", "col"),
        P("gx", "gy", "col"),
        P("gx", "gy", "col"),
        P(),
        P(("gx", "gy", "col"), None),
        P(),
        P("freq"),
    )
    out_specs = (P("freq", "gx", "gy", "col"), P("freq", None))
    return jax.shard_map(shards, mesh=mesh, in_specs=in_specs, out_specs=out_specs, check_vma=False)
```

```python
import jax
import jax.numpy as jnp
from jax import lax
from jax.sharding import PartitionSpec as P

DAMPING = 0.5
RELAXATION = 0.6


def with_halo(array, sides, width, tie=None):
    for axis, dim in sides:
        peers, length = (lax.axis_size(axis), array.shape[dim])
        last = lax.slice_in_dim(array, length - width, length, axis=dim)
        initial = lax.slice_in_dim(array, 0, width, axis=dim)
        if peers == 2 and dim == array.ndim - 1:
            first = lax.axis_index(axis) == 0
            sent = array if tie is None else array + tie
            got = lax.ppermute(sent, axis, [(0, 1), (1, 0)])
            got_last = lax.slice_in_dim(got, length - width, length, axis=dim)
            got_initial = lax.slice_in_dim(got, 0, width, axis=dim)
            zero = jnp.zeros_like(got_last)
            before = jnp.where(first, zero, got_last)
            after = jnp.where(first, got_initial, zero)
        elif peers == 2:
            first = lax.axis_index(axis) == 0
            got = lax.ppermute(jnp.where(first, last, initial), axis, [(0, 1), (1, 0)])
            zero = jnp.zeros_like(got)
            before = jnp.where(first, zero, got)
            after = jnp.where(first, got, zero)
        else:
            up = [(i, (i + 1) % peers) for i in range(peers - 1)]
            down = [(j, i) for i, j in up]
            before = lax.ppermute(last, axis, up)
            after = lax.ppermute(initial, axis, down)
        array = jnp.concatenate([before, array, after], axis=dim)
    return array


def window(padded, offset):
    size_x = padded.shape[1] - 2
    size_y = padded.shape[2] - 2
    size_z = padded.shape[3] - 2
    return padded[
        :,
        1 + offset[0] : 1 + offset[0] + size_x,
        1 + offset[1] : 1 + offset[1] + size_y,
        1 + offset[2] : 1 + offset[2] + size_z,
    ]


def navier(padded, lame_first, shear):
    units = ((1, 0, 0), (0, 1, 0), (0, 0, 1))
    centre = window(padded, (0, 0, 0))
    second = []
    for axis_d in range(3):
        ahead = units[axis_d]
        behind = tuple((-value for value in ahead))
        second.append(window(padded, ahead) + window(padded, behind) - 2.0 * centre)
    laplace = second[0] + second[1] + second[2]
    result = []
    for part_index in range(2):
        for component in range(3):
            channel = part_index * 3 + component
            divergence = second[component][channel]
            for other_axis in range(3):
                if other_axis != component:
                    source_channel = part_index * 3 + other_axis
                    single = padded[source_channel : source_channel + 1]
                    first_unit = units[component]
                    other_unit = units[other_axis]
                    plus_plus = tuple((first_unit[k] + other_unit[k] for k in range(3)))
                    plus_minus = tuple((first_unit[k] - other_unit[k] for k in range(3)))
                    minus_plus = tuple((-first_unit[k] + other_unit[k] for k in range(3)))
                    minus_minus = tuple((-first_unit[k] - other_unit[k] for k in range(3)))
                    mixed = (
                        window(single, plus_plus)
                        - window(single, plus_minus)
                        - window(single, minus_plus)
                        + window(single, minus_minus)
                    )
                    divergence = divergence + 0.25 * mixed[0]
            result.append(shear * laplace[channel] + (lame_first + shear) * divergence)
    return jnp.stack(result)


def sweep(padded, lame_first, shear, density, mask, source, omega_sq, impedance):
    field = window(padded, (0, 0, 0))
    elastic = navier(padded, lame_first, shear)
    real_part = field[:3]
    imag_part = field[3:]
    imp_real = impedance[0][:, None, None, None]
    imp_imag = impedance[1][:, None, None, None]
    inertia = omega_sq * density
    apply_real = (
        -elastic[:3]
        - inertia * (real_part - DAMPING * imag_part)
        + mask * (imp_real * real_part - imp_imag * imag_part)
    )
    apply_imag = (
        -elastic[3:]
        - inertia * (imag_part + DAMPING * real_part)
        + mask * (imp_real * imag_part + imp_imag * real_part)
    )
    resid_real = source[:3] - apply_real
    resid_imag = source[3:] - apply_imag
    diag_real = 8.0 * shear + 2.0 * lame_first - inertia + mask * imp_real
    diag_imag = -DAMPING * inertia + mask * imp_imag
    modulus = diag_real * diag_real + diag_imag * diag_imag
    new_real = real_part + RELAXATION * (resid_real * diag_real + resid_imag * diag_imag) / modulus
    new_imag = imag_part + RELAXATION * (resid_imag * diag_real - resid_real * diag_imag) / modulus
    return jnp.concatenate([new_real, new_imag], 0)


def mean_gain(lame_first, shear, density, mask, omega_sq, impedance):
    imp_real = impedance[0][:, None, None, None]
    imp_imag = impedance[1][:, None, None, None]
    inertia = omega_sq * density
    diag_real = 8.0 * shear + 2.0 * lame_first - inertia + mask * imp_real
    diag_imag = -DAMPING * inertia + mask * imp_imag
    scale = RELAXATION * mask / (diag_real * diag_real + diag_imag * diag_imag)
    gain_real = scale * (imp_real * diag_real + imp_imag * diag_imag)
    gain_imag = scale * (imp_imag * diag_real - imp_real * diag_imag)
    return gain_real, gain_imag


def add_mean(field, gain_real, gain_imag, mean_field):
    mean_real = mean_field[:3]
    mean_imag = mean_field[3:]
    straight = jnp.concatenate([mean_real, mean_imag])[:, None, None, None]
    crossed = jnp.concatenate([-mean_imag, mean_real])[:, None, None, None]
    return field + (gain_real * straight + gain_imag * crossed)


def group_rounds(value, axes):
    size = 1
    for axis in axes:
        size *= lax.axis_size(axis)
    if size & (size - 1):
        return [lax.psum(value, axes)]
    rounds = []
    stride = 1
    while stride < size:
        if stride * 4 <= size:
            got = [
                lax.ppermute(value, axes, [(i, i ^ (m * stride)) for i in range(size)])
                for m in (1, 2, 3)
            ]
            value = (value + got[0]) + (got[1] + got[2])
            stride *= 4
        else:
            value = value + lax.ppermute(value, axes, [(i, i ^ stride) for i in range(size)])
            stride *= 2
        rounds.append(value)
    return rounds


def group_sum(value, axes):
    return group_rounds(value, axes)[-1]


def expand(blocks):
    blocks_x, blocks_y, blocks_z = blocks.shape
    depth_tile = lax.broadcasted_iota(jnp.int32, (1, 1, blocks_z * 32), 2) // 32
    rows = jnp.zeros((blocks_x, blocks_y, blocks_z * 32), blocks.dtype)
    for tile in range(blocks_z):
        rows = jnp.where(depth_tile == tile, blocks[:, :, tile : tile + 1], rows)
    spread = jnp.broadcast_to(
        rows[:, None, :, None, :], (blocks_x, 8, blocks_y, 8, blocks_z * 32)
    )
    return spread.reshape(blocks_x * 8, blocks_y * 8, blocks_z * 32)


def material(block_ids, table):
    entries = lax.broadcasted_iota(jnp.int32, block_ids.shape + (table.shape[0],), block_ids.ndim)
    chosen = block_ids[..., None] == entries
    lame_first = jnp.sum(jnp.where(chosen, table[:, 0], 0.0), axis=-1)
    shear = jnp.sum(jnp.where(chosen, table[:, 1], 0.0), axis=-1)
    return (lame_first, shear)


def shards(
    source, warm, forward, density, material_map, material_table, iface_cells, impedance, omega2
):
    omega_sq = omega2[0]
    tile_shape = density.shape
    tile_cells = tile_shape[0] * tile_shape[1] * tile_shape[2]
    mask = jnp.zeros((tile_cells,), jnp.float32).at[iface_cells[0]].set(1.0).reshape(tile_shape)
    lame_tiles, shear_tiles = material(material_map, material_table)
    lame_first = expand(lame_tiles)
    shear = expand(shear_tiles)
    density_cells = density.astype(jnp.float32)
    source_cells = source.astype(jnp.float32)
    group_size = lax.axis_size("gx") * lax.axis_size("gy") * lax.axis_size("col")
    count = jnp.float32(group_size * iface_cells.shape[1])
    gain_real, gain_imag = mean_gain(lame_first, shear, density_cells, mask, omega_sq, impedance)
    gain_both_real = jnp.concatenate([gain_real, gain_real])
    gain_both_imag = jnp.concatenate([gain_imag, gain_imag])
    axes = ("gx", "gy", "col")
    coarse_x = tile_shape[0] // 4
    coarse_y = tile_shape[1] // 4
    grid_shape = (lax.axis_size("gx") * coarse_x, lax.axis_size("gy") * coarse_y)
    grid_at = (lax.axis_index("gx") * coarse_x, lax.axis_index("gy") * coarse_y)

    def block_sums(cells):
        lead = cells.shape[:-3]
        local = cells.reshape(lead + (coarse_x, 4, coarse_y, 4, tile_shape[2]))
        local = local.sum(axis=(-4, -2, -1))
        grid = jnp.zeros(lead + grid_shape, jnp.float32)
        return lax.dynamic_update_slice(grid, local, (0,) * len(lead) + grid_at)

    forward_cells = forward.astype(jnp.float32)
    forward_real = forward_cells[:3]
    forward_imag = forward_cells[3:]
    plain_real = gain_real * forward_real - gain_imag * forward_imag
    plain_imag = gain_real * forward_imag + gain_imag * forward_real
    response_real = plain_real - DAMPING * plain_imag
    response_imag = plain_imag + DAMPING * plain_real
    response = block_sums(jnp.concatenate([response_real, response_imag]))
    field = warm.astype(jnp.float32)
    rounds = group_rounds(
        jnp.concatenate(
            [
                jnp.sum(mask * field, axis=(1, 2, 3)),
                jnp.sum(gain_real, axis=(1, 2, 3)),
                jnp.sum(gain_imag, axis=(1, 2, 3)),
            ]
        ),
        axes,
    )
    first = rounds[-1]
    mean_field = first[:6] / count
    gain_total_real = first[6:9]
    gain_total_imag = first[9:12]
    sweep_args = (lame_first, shear, density_cells, mask, source_cells, omega_sq, impedance)
    padded = with_halo(field, (("gx", 1), ("gy", 2)), 1)
    padded = with_halo(padded, (("col", 3),), 1, 0.0 * rounds[0][0])
    tied_source = source_cells + 0.0 * first[0]
    field = sweep(padded, lame_first, shear, density_cells, mask, tied_source, omega_sq, impedance)
    second_local = jnp.sum(mask * field, axis=(1, 2, 3))
    field = add_mean(field, gain_both_real, gain_both_imag, mean_field)
    padded = with_halo(field, (("gx", 1), ("gy", 2), ("col", 3)), 1)
    field = sweep(padded, *sweep_args)
    correlation = (
        field[:3] * forward_real
        - field[3:] * forward_imag
        - DAMPING * (field[:3] * forward_imag + field[3:] * forward_real)
    )
    cell_terms = -omega_sq * jnp.sum(correlation, axis=0)
    last = group_sum(
        jnp.concatenate([second_local, block_sums(cell_terms).reshape(-1), response.reshape(-1)]),
        axes,
    )
    second = last[:6]
    grid_size = grid_shape[0] * grid_shape[1]
    response = last[6 + grid_size :].reshape(response.shape)
    mean_real = mean_field[:3]
    mean_imag = mean_field[3:]
    total_real = second[:3] + (gain_total_real * mean_real - gain_total_imag * mean_imag)
    total_imag = second[3:] + (gain_total_real * mean_imag + gain_total_imag * mean_real)
    late_mean = jnp.concatenate([total_real, total_imag]) / count
    field = add_mean(field, gain_both_real, gain_both_imag, late_mean)
    late_terms = jnp.sum(
        late_mean[:3, None, None] * response[:3] - late_mean[3:, None, None] * response[3:], axis=0
    )
    coarse = (last[6 : 6 + grid_size].reshape(grid_shape) - omega_sq * late_terms) / 64.0
    return (field, coarse)


def solution(mesh):
    in_specs = (
        P("freq", "gx", "gy", "col"),
        P("freq", "gx", "gy", "col"),
        P("freq", "gx", "gy", "col"),
        P("gx", "gy", "col"),
        P("gx", "gy", "col"),
        P(),
        P(("gx", "gy", "col"), None),
        P(),
        P("freq"),
    )
    out_specs = (P("freq", "gx", "gy", "col"), P("freq", None))
    return jax.shard_map(shards, mesh=mesh, in_specs=in_specs, out_specs=out_specs, check_vma=False)
```

```python
import jax
import jax.numpy as jnp
from jax import lax
from jax.sharding import PartitionSpec as P

DAMPING = 0.5
RELAXATION = 0.6


def with_halo(array, sides, width, tie=None):
    for axis, dim in sides:
        peers, length = (lax.axis_size(axis), array.shape[dim])
        last = lax.slice_in_dim(array, length - width, length, axis=dim)
        initial = lax.slice_in_dim(array, 0, width, axis=dim)
        if peers == 2 and dim == array.ndim - 1:
            first = lax.axis_index(axis) == 0
            sent = array if tie is None else array + tie
            got = lax.ppermute(sent, axis, [(0, 1), (1, 0)])
            got_last = lax.slice_in_dim(got, length - width, length, axis=dim)
            got_initial = lax.slice_in_dim(got, 0, width, axis=dim)
            zero = jnp.zeros_like(got_last)
            before = jnp.where(first, zero, got_last)
            after = jnp.where(first, got_initial, zero)
        elif peers == 2:
            first = lax.axis_index(axis) == 0
            got = lax.ppermute(jnp.where(first, last, initial), axis, [(0, 1), (1, 0)])
            zero = jnp.zeros_like(got)
            before = jnp.where(first, zero, got)
            after = jnp.where(first, got, zero)
        else:
            up = [(i, (i + 1) % peers) for i in range(peers - 1)]
            down = [(j, i) for i, j in up]
            before = lax.ppermute(last, axis, up)
            after = lax.ppermute(initial, axis, down)
        array = jnp.concatenate([before, array, after], axis=dim)
    return array


def window(padded, offset):
    size_x = padded.shape[1] - 2
    size_y = padded.shape[2] - 2
    size_z = padded.shape[3] - 2
    return padded[
        :,
        1 + offset[0] : 1 + offset[0] + size_x,
        1 + offset[1] : 1 + offset[1] + size_y,
        1 + offset[2] : 1 + offset[2] + size_z,
    ]


def navier(padded, lame_first, shear):
    units = ((1, 0, 0), (0, 1, 0), (0, 0, 1))
    centre = window(padded, (0, 0, 0))
    second = []
    for axis_d in range(3):
        ahead = units[axis_d]
        behind = tuple((-value for value in ahead))
        second.append(window(padded, ahead) + window(padded, behind) - 2.0 * centre)
    laplace = second[0] + second[1] + second[2]
    result = []
    for part_index in range(2):
        for component in range(3):
            channel = part_index * 3 + component
            divergence = second[component][channel]
            for other_axis in range(3):
                if other_axis != component:
                    source_channel = part_index * 3 + other_axis
                    single = padded[source_channel : source_channel + 1]
                    first_unit = units[component]
                    other_unit = units[other_axis]
                    plus_plus = tuple((first_unit[k] + other_unit[k] for k in range(3)))
                    plus_minus = tuple((first_unit[k] - other_unit[k] for k in range(3)))
                    minus_plus = tuple((-first_unit[k] + other_unit[k] for k in range(3)))
                    minus_minus = tuple((-first_unit[k] - other_unit[k] for k in range(3)))
                    mixed = (
                        window(single, plus_plus)
                        - window(single, plus_minus)
                        - window(single, minus_plus)
                        + window(single, minus_minus)
                    )
                    divergence = divergence + 0.25 * mixed[0]
            result.append(shear * laplace[channel] + (lame_first + shear) * divergence)
    return jnp.stack(result)


def sweep(padded, lame_first, shear, density, mask, source, omega_sq, impedance):
    field = window(padded, (0, 0, 0))
    elastic = navier(padded, lame_first, shear)
    real_part = field[:3]
    imag_part = field[3:]
    imp_real = impedance[0][:, None, None, None]
    imp_imag = impedance[1][:, None, None, None]
    inertia = omega_sq * density
    apply_real = (
        -elastic[:3]
        - inertia * (real_part - DAMPING * imag_part)
        + mask * (imp_real * real_part - imp_imag * imag_part)
    )
    apply_imag = (
        -elastic[3:]
        - inertia * (imag_part + DAMPING * real_part)
        + mask * (imp_real * imag_part + imp_imag * real_part)
    )
    resid_real = source[:3] - apply_real
    resid_imag = source[3:] - apply_imag
    diag_real = 8.0 * shear + 2.0 * lame_first - inertia + mask * imp_real
    diag_imag = -DAMPING * inertia + mask * imp_imag
    modulus = diag_real * diag_real + diag_imag * diag_imag
    new_real = real_part + RELAXATION * (resid_real * diag_real + resid_imag * diag_imag) / modulus
    new_imag = imag_part + RELAXATION * (resid_imag * diag_real - resid_real * diag_imag) / modulus
    return jnp.concatenate([new_real, new_imag], 0)


def mean_gain(lame_first, shear, density, mask, omega_sq, impedance):
    imp_real = impedance[0][:, None, None, None]
    imp_imag = impedance[1][:, None, None, None]
    inertia = omega_sq * density
    diag_real = 8.0 * shear + 2.0 * lame_first - inertia + mask * imp_real
    diag_imag = -DAMPING * inertia + mask * imp_imag
    scale = RELAXATION * mask / (diag_real * diag_real + diag_imag * diag_imag)
    gain_real = scale * (imp_real * diag_real + imp_imag * diag_imag)
    gain_imag = scale * (imp_imag * diag_real - imp_real * diag_imag)
    return gain_real, gain_imag


def add_mean(field, gain_real, gain_imag, mean_field):
    mean_real = mean_field[:3]
    mean_imag = mean_field[3:]
    straight = jnp.concatenate([mean_real, mean_imag])[:, None, None, None]
    crossed = jnp.concatenate([-mean_imag, mean_real])[:, None, None, None]
    return field + (gain_real * straight + gain_imag * crossed)


def group_rounds(value, axes):
    size = 1
    for axis in axes:
        size *= lax.axis_size(axis)
    if size & (size - 1):
        return [lax.psum(value, axes)]
    rounds = []
    stride = 1
    while stride < size:
        if stride * 4 <= size:
            got = [
                lax.ppermute(value, axes, [(i, i ^ (m * stride)) for i in range(size)])
                for m in (1, 2, 3)
            ]
            value = (value + got[0]) + (got[1] + got[2])
            stride *= 4
        else:
            value = value + lax.ppermute(value, axes, [(i, i ^ stride) for i in range(size)])
            stride *= 2
        rounds.append(value)
    return rounds


def group_sum(value, axes):
    return group_rounds(value, axes)[-1]


def expand(blocks):
    blocks_x, blocks_y, blocks_z = blocks.shape
    depth_tile = lax.broadcasted_iota(jnp.int32, (1, 1, blocks_z * 32), 2) // 32
    rows = jnp.zeros((blocks_x, blocks_y, blocks_z * 32), blocks.dtype)
    for tile in range(blocks_z):
        rows = jnp.where(depth_tile == tile, blocks[:, :, tile : tile + 1], rows)
    spread = jnp.broadcast_to(
        rows[:, None, :, None, :], (blocks_x, 8, blocks_y, 8, blocks_z * 32)
    )
    return spread.reshape(blocks_x * 8, blocks_y * 8, blocks_z * 32)


def material(block_ids, table):
    entries = lax.broadcasted_iota(jnp.int32, block_ids.shape + (table.shape[0],), block_ids.ndim)
    chosen = block_ids[..., None] == entries
    lame_first = jnp.sum(jnp.where(chosen, table[:, 0], 0.0), axis=-1)
    shear = jnp.sum(jnp.where(chosen, table[:, 1], 0.0), axis=-1)
    return (lame_first, shear)


def shards(
    source, warm, forward, density, material_map, material_table, iface_cells, impedance, omega2
):
    omega_sq = omega2[0]
    tile_shape = density.shape
    tile_cells = tile_shape[0] * tile_shape[1] * tile_shape[2]
    mask = jnp.zeros((tile_cells,), jnp.float32).at[iface_cells[0]].set(1.0).reshape(tile_shape)
    lame_tiles, shear_tiles = material(material_map, material_table)
    lame_first = expand(lame_tiles)
    shear = expand(shear_tiles)
    density_cells = density.astype(jnp.float32)
    source_cells = source.astype(jnp.float32)
    group_size = lax.axis_size("gx") * lax.axis_size("gy") * lax.axis_size("col")
    count = jnp.float32(group_size * iface_cells.shape[1])
    gain_real, gain_imag = mean_gain(lame_first, shear, density_cells, mask, omega_sq, impedance)
    gain_both_real = jnp.concatenate([gain_real, gain_real])
    gain_both_imag = jnp.concatenate([gain_imag, gain_imag])
    axes = ("gx", "gy", "col")
    coarse_x = tile_shape[0] // 4
    coarse_y = tile_shape[1] // 4
    grid_shape = (lax.axis_size("gx") * coarse_x, lax.axis_size("gy") * coarse_y)
    grid_at = (lax.axis_index("gx") * coarse_x, lax.axis_index("gy") * coarse_y)

    def block_sums(cells):
        lead = cells.shape[:-3]
        local = cells.reshape(lead + (coarse_x, 4, coarse_y, 4, tile_shape[2]))
        local = local.sum(axis=(-4, -2, -1))
        rows = lax.broadcasted_iota(jnp.int32, (grid_shape[0], coarse_x), 0)
        cols = lax.broadcasted_iota(jnp.int32, (grid_shape[1], coarse_y), 0)
        pick_x = (rows == grid_at[0] + lax.broadcasted_iota(jnp.int32, rows.shape, 1))
        pick_y = (cols == grid_at[1] + lax.broadcasted_iota(jnp.int32, cols.shape, 1))
        spread = (
            local[..., None, None, :, :]
            * pick_x.astype(jnp.float32)[:, None, :, None]
            * pick_y.astype(jnp.float32)[None, :, None, :]
        )
        return spread.sum(axis=(-2, -1))

    forward_cells = forward.astype(jnp.float32)
    forward_real = forward_cells[:3]
    forward_imag = forward_cells[3:]
    plain_real = gain_real * forward_real - gain_imag * forward_imag
    plain_imag = gain_real * forward_imag + gain_imag * forward_real
    response_real = plain_real - DAMPING * plain_imag
    response_imag = plain_imag + DAMPING * plain_real
    response = block_sums(jnp.concatenate([response_real, response_imag]))
    field = warm.astype(jnp.float32)
    rounds = group_rounds(
        jnp.concatenate(
            [
                jnp.sum(mask * field, axis=(1, 2, 3)),
                jnp.sum(gain_real, axis=(1, 2, 3)),
                jnp.sum(gain_imag, axis=(1, 2, 3)),
            ]
        ),
        axes,
    )
    first = rounds[-1]
    mean_field = first[:6] / count
    gain_total_real = first[6:9]
    gain_total_imag = first[9:12]
    sweep_args = (lame_first, shear, density_cells, mask, source_cells, omega_sq, impedance)
    padded = with_halo(field, (("gx", 1), ("gy", 2)), 1)
    padded = with_halo(padded, (("col", 3),), 1, 0.0 * rounds[0][0])
    tied_source = source_cells + 0.0 * first[0]
    field = sweep(padded, lame_first, shear, density_cells, mask, tied_source, omega_sq, impedance)
    second_local = jnp.sum(mask * field, axis=(1, 2, 3))
    field = add_mean(field, gain_both_real, gain_both_imag, mean_field)
    padded = with_halo(field, (("gx", 1), ("gy", 2), ("col", 3)), 1)
    field = sweep(padded, *sweep_args)
    correlation = (
        field[:3] * forward_real
        - field[3:] * forward_imag
        - DAMPING * (field[:3] * forward_imag + field[3:] * forward_real)
    )
    cell_terms = -omega_sq * jnp.sum(correlation, axis=0)
    last = group_sum(
        jnp.concatenate([second_local, block_sums(cell_terms).reshape(-1), response.reshape(-1)]),
        axes,
    )
    second = last[:6]
    grid_size = grid_shape[0] * grid_shape[1]
    response = last[6 + grid_size :].reshape(response.shape)
    mean_real = mean_field[:3]
    mean_imag = mean_field[3:]
    total_real = second[:3] + (gain_total_real * mean_real - gain_total_imag * mean_imag)
    total_imag = second[3:] + (gain_total_real * mean_imag + gain_total_imag * mean_real)
    late_mean = jnp.concatenate([total_real, total_imag]) / count
    field = add_mean(field, gain_both_real, gain_both_imag, late_mean)
    late_terms = jnp.sum(
        late_mean[:3, None, None] * response[:3] - late_mean[3:, None, None] * response[3:], axis=0
    )
    coarse = (last[6 : 6 + grid_size].reshape(grid_shape) - omega_sq * late_terms) / 64.0
    return (field, coarse)


def solution(mesh):
    in_specs = (
        P("freq", "gx", "gy", "col"),
        P("freq", "gx", "gy", "col"),
        P("freq", "gx", "gy", "col"),
        P("gx", "gy", "col"),
        P("gx", "gy", "col"),
        P(),
        P(("gx", "gy", "col"), None),
        P(),
        P("freq"),
    )
    out_specs = (P("freq", "gx", "gy", "col"), P("freq", None))
    return jax.shard_map(shards, mesh=mesh, in_specs=in_specs, out_specs=out_specs, check_vma=False)
```

```python
import jax
import jax.numpy as jnp
from jax import lax
from jax.sharding import PartitionSpec as P

DAMPING = 0.5
RELAXATION = 0.6


def with_halo(array, sides, width, tie=None):
    for axis, dim in sides:
        peers, length = (lax.axis_size(axis), array.shape[dim])
        last = lax.slice_in_dim(array, length - width, length, axis=dim)
        initial = lax.slice_in_dim(array, 0, width, axis=dim)
        if peers == 2 and dim == array.ndim - 1:
            first = lax.axis_index(axis) == 0
            sent = array if tie is None else array + tie
            got = lax.ppermute(sent, axis, [(0, 1), (1, 0)])
            got_last = lax.slice_in_dim(got, length - width, length, axis=dim)
            got_initial = lax.slice_in_dim(got, 0, width, axis=dim)
            zero = jnp.zeros_like(got_last)
            before = jnp.where(first, zero, got_last)
            after = jnp.where(first, got_initial, zero)
        elif peers == 2:
            first = lax.axis_index(axis) == 0
            got = lax.ppermute(jnp.where(first, last, initial), axis, [(0, 1), (1, 0)])
            zero = jnp.zeros_like(got)
            before = jnp.where(first, zero, got)
            after = jnp.where(first, got, zero)
        else:
            up = [(i, (i + 1) % peers) for i in range(peers - 1)]
            down = [(j, i) for i, j in up]
            before = lax.ppermute(last, axis, up)
            after = lax.ppermute(initial, axis, down)
        array = jnp.concatenate([before, array, after], axis=dim)
    return array


def window(padded, offset):
    size_x = padded.shape[1] - 2
    size_y = padded.shape[2] - 2
    size_z = padded.shape[3] - 2
    return padded[
        :,
        1 + offset[0] : 1 + offset[0] + size_x,
        1 + offset[1] : 1 + offset[1] + size_y,
        1 + offset[2] : 1 + offset[2] + size_z,
    ]


def navier(padded, lame_first, shear):
    units = ((1, 0, 0), (0, 1, 0), (0, 0, 1))
    centre = window(padded, (0, 0, 0))
    second = []
    for axis_d in range(3):
        ahead = units[axis_d]
        behind = tuple((-value for value in ahead))
        second.append(window(padded, ahead) + window(padded, behind) - 2.0 * centre)
    laplace = second[0] + second[1] + second[2]
    result = []
    for part_index in range(2):
        for component in range(3):
            channel = part_index * 3 + component
            divergence = second[component][channel]
            for other_axis in range(3):
                if other_axis != component:
                    source_channel = part_index * 3 + other_axis
                    single = padded[source_channel : source_channel + 1]
                    first_unit = units[component]
                    other_unit = units[other_axis]
                    plus_plus = tuple((first_unit[k] + other_unit[k] for k in range(3)))
                    plus_minus = tuple((first_unit[k] - other_unit[k] for k in range(3)))
                    minus_plus = tuple((-first_unit[k] + other_unit[k] for k in range(3)))
                    minus_minus = tuple((-first_unit[k] - other_unit[k] for k in range(3)))
                    mixed = (
                        window(single, plus_plus)
                        - window(single, plus_minus)
                        - window(single, minus_plus)
                        + window(single, minus_minus)
                    )
                    divergence = divergence + 0.25 * mixed[0]
            result.append(shear * laplace[channel] + (lame_first + shear) * divergence)
    return jnp.stack(result)


def sweep(padded, lame_first, shear, density, mask, source, omega_sq, impedance):
    field = window(padded, (0, 0, 0))
    elastic = navier(padded, lame_first, shear)
    real_part = field[:3]
    imag_part = field[3:]
    imp_real = impedance[0][:, None, None, None]
    imp_imag = impedance[1][:, None, None, None]
    inertia = omega_sq * density
    apply_real = (
        -elastic[:3]
        - inertia * (real_part - DAMPING * imag_part)
        + mask * (imp_real * real_part - imp_imag * imag_part)
    )
    apply_imag = (
        -elastic[3:]
        - inertia * (imag_part + DAMPING * real_part)
        + mask * (imp_real * imag_part + imp_imag * real_part)
    )
    resid_real = source[:3] - apply_real
    resid_imag = source[3:] - apply_imag
    diag_real = 8.0 * shear + 2.0 * lame_first - inertia + mask * imp_real
    diag_imag = -DAMPING * inertia + mask * imp_imag
    modulus = diag_real * diag_real + diag_imag * diag_imag
    new_real = real_part + RELAXATION * (resid_real * diag_real + resid_imag * diag_imag) / modulus
    new_imag = imag_part + RELAXATION * (resid_imag * diag_real - resid_real * diag_imag) / modulus
    return jnp.concatenate([new_real, new_imag], 0)


def mean_gain(lame_first, shear, density, mask, omega_sq, impedance):
    imp_real = impedance[0][:, None, None, None]
    imp_imag = impedance[1][:, None, None, None]
    inertia = omega_sq * density
    diag_real = 8.0 * shear + 2.0 * lame_first - inertia + mask * imp_real
    diag_imag = -DAMPING * inertia + mask * imp_imag
    scale = RELAXATION * mask / (diag_real * diag_real + diag_imag * diag_imag)
    gain_real = scale * (imp_real * diag_real + imp_imag * diag_imag)
    gain_imag = scale * (imp_imag * diag_real - imp_real * diag_imag)
    return gain_real, gain_imag


def add_mean(field, gain_real, gain_imag, mean_field):
    mean_real = mean_field[:3]
    mean_imag = mean_field[3:]
    straight = jnp.concatenate([mean_real, mean_imag])[:, None, None, None]
    crossed = jnp.concatenate([-mean_imag, mean_real])[:, None, None, None]
    return field + (gain_real * straight + gain_imag * crossed)


def group_rounds(value, axes):
    size = 1
    for axis in axes:
        size *= lax.axis_size(axis)
    if size & (size - 1):
        return [lax.psum(value, axes)]
    rounds = []
    stride = 1
    while stride < size:
        if stride * 4 <= size:
            got = [
                lax.ppermute(value, axes, [(i, i ^ (m * stride)) for i in range(size)])
                for m in (1, 2, 3)
            ]
            value = (value + got[0]) + (got[1] + got[2])
            stride *= 4
        else:
            value = value + lax.ppermute(value, axes, [(i, i ^ stride) for i in range(size)])
            stride *= 2
        rounds.append(value)
    return rounds


def group_sum(value, axes):
    return group_rounds(value, axes)[-1]


def expand(blocks):
    blocks_x, blocks_y, blocks_z = blocks.shape
    depth_tile = lax.broadcasted_iota(jnp.int32, (1, 1, blocks_z * 32), 2) // 32
    rows = jnp.zeros((blocks_x, blocks_y, blocks_z * 32), blocks.dtype)
    for tile in range(blocks_z):
        rows = jnp.where(depth_tile == tile, blocks[:, :, tile : tile + 1], rows)
    spread = jnp.broadcast_to(
        rows[:, None, :, None, :], (blocks_x, 8, blocks_y, 8, blocks_z * 32)
    )
    return spread.reshape(blocks_x * 8, blocks_y * 8, blocks_z * 32)


def material(block_ids, table):
    entries = lax.broadcasted_iota(jnp.int32, block_ids.shape + (table.shape[0],), block_ids.ndim)
    chosen = block_ids[..., None] == entries
    lame_first = jnp.sum(jnp.where(chosen, table[:, 0], 0.0), axis=-1)
    shear = jnp.sum(jnp.where(chosen, table[:, 1], 0.0), axis=-1)
    return (lame_first, shear)


def shards(
    source, warm, forward, density, material_map, material_table, iface_cells, impedance, omega2
):
    omega_sq = omega2[0]
    tile_shape = density.shape
    tile_cells = tile_shape[0] * tile_shape[1] * tile_shape[2]
    mask = jnp.zeros((tile_cells,), jnp.float32).at[iface_cells[0]].set(1.0).reshape(tile_shape)
    lame_tiles, shear_tiles = material(material_map, material_table)
    lame_first = expand(lame_tiles)
    shear = expand(shear_tiles)
    density_cells = density.astype(jnp.float32)
    source_cells = source.astype(jnp.float32)
    group_size = lax.axis_size("gx") * lax.axis_size("gy") * lax.axis_size("col")
    count = jnp.float32(group_size * iface_cells.shape[1])
    gain_real, gain_imag = mean_gain(lame_first, shear, density_cells, mask, omega_sq, impedance)
    gain_both_real = jnp.concatenate([gain_real, gain_real])
    gain_both_imag = jnp.concatenate([gain_imag, gain_imag])
    axes = ("gx", "gy", "col")
    coarse_x = tile_shape[0] // 4
    coarse_y = tile_shape[1] // 4
    grid_shape = (lax.axis_size("gx") * coarse_x, lax.axis_size("gy") * coarse_y)
    grid_at = (lax.axis_index("gx") * coarse_x, lax.axis_index("gy") * coarse_y)

    def block_sums(cells):
        lead = cells.shape[:-3]
        local = cells.reshape(lead + (coarse_x, 4, coarse_y, 4, tile_shape[2]))
        local = local.sum(axis=(-4, -2, -1))
        grid = jnp.zeros(lead + grid_shape, jnp.float32)
        return lax.dynamic_update_slice(grid, local, (0,) * len(lead) + grid_at)

    forward_cells = forward.astype(jnp.float32)
    forward_real = forward_cells[:3]
    forward_imag = forward_cells[3:]
    plain_real = gain_real * forward_real - gain_imag * forward_imag
    plain_imag = gain_real * forward_imag + gain_imag * forward_real
    response_real = plain_real - DAMPING * plain_imag
    response_imag = plain_imag + DAMPING * plain_real
    response = block_sums(jnp.concatenate([response_real, response_imag]))
    field = warm.astype(jnp.float32)
    rounds = group_rounds(
        jnp.concatenate(
            [
                jnp.sum(mask * field, axis=(1, 2, 3)),
                jnp.sum(gain_real, axis=(1, 2, 3)),
                jnp.sum(gain_imag, axis=(1, 2, 3)),
            ]
        ),
        axes,
    )
    first = rounds[-1]
    mean_field = first[:6] / count
    gain_total_real = first[6:9]
    gain_total_imag = first[9:12]
    sweep_args = (lame_first, shear, density_cells, mask, source_cells, omega_sq, impedance)
    padded = with_halo(field, (("gx", 1), ("gy", 2)), 1)
    padded = with_halo(padded, (("col", 3),), 1, 0.0 * rounds[0][0])
    tied_source = source_cells + 0.0 * first[0]
    field = sweep(padded, lame_first, shear, density_cells, mask, tied_source, omega_sq, impedance)
    second_local = jnp.sum(mask * field, axis=(1, 2, 3))
    field = add_mean(field, gain_both_real, gain_both_imag, mean_field)

    def plane(start):
        cut = slice(start, start + 1)
        part = sweep(
            padded[:, start : start + 3],
            lame_first[cut],
            shear[cut],
            density_cells[cut],
            mask[cut],
            tied_source[:, cut],
            omega_sq,
            impedance,
        )
        return add_mean(part, gain_both_real[:, cut], gain_both_imag[:, cut], mean_field)

    low_plane = plane(0)
    high_plane = plane(tile_shape[0] - 1)
    peers = lax.axis_size("gx")
    if peers == 2:
        first_x = lax.axis_index("gx") == 0
        got = lax.ppermute(jnp.where(first_x, high_plane, low_plane), "gx", [(0, 1), (1, 0)])
        zero = jnp.zeros_like(got)
        before = jnp.where(first_x, zero, got)
        after = jnp.where(first_x, got, zero)
    else:
        up = [(i, (i + 1) % peers) for i in range(peers - 1)]
        down = [(j, i) for i, j in up]
        before = lax.ppermute(high_plane, "gx", up)
        after = lax.ppermute(low_plane, "gx", down)
    padded = jnp.concatenate([before, field, after], axis=1)
    padded = with_halo(padded, (("gy", 2), ("col", 3)), 1)
    field = sweep(padded, *sweep_args)
    correlation = (
        field[:3] * forward_real
        - field[3:] * forward_imag
        - DAMPING * (field[:3] * forward_imag + field[3:] * forward_real)
    )
    cell_terms = -omega_sq * jnp.sum(correlation, axis=0)
    last = group_sum(
        jnp.concatenate([second_local, block_sums(cell_terms).reshape(-1), response.reshape(-1)]),
        axes,
    )
    second = last[:6]
    grid_size = grid_shape[0] * grid_shape[1]
    response = last[6 + grid_size :].reshape(response.shape)
    mean_real = mean_field[:3]
    mean_imag = mean_field[3:]
    total_real = second[:3] + (gain_total_real * mean_real - gain_total_imag * mean_imag)
    total_imag = second[3:] + (gain_total_real * mean_imag + gain_total_imag * mean_real)
    late_mean = jnp.concatenate([total_real, total_imag]) / count
    field = add_mean(field, gain_both_real, gain_both_imag, late_mean)
    late_terms = jnp.sum(
        late_mean[:3, None, None] * response[:3] - late_mean[3:, None, None] * response[3:], axis=0
    )
    coarse = (last[6 : 6 + grid_size].reshape(grid_shape) - omega_sq * late_terms) / 64.0
    return (field, coarse)


def solution(mesh):
    in_specs = (
        P("freq", "gx", "gy", "col"),
        P("freq", "gx", "gy", "col"),
        P("freq", "gx", "gy", "col"),
        P("gx", "gy", "col"),
        P("gx", "gy", "col"),
        P(),
        P(("gx", "gy", "col"), None),
        P(),
        P("freq"),
    )
    out_specs = (P("freq", "gx", "gy", "col"), P("freq", None))
    return jax.shard_map(shards, mesh=mesh, in_specs=in_specs, out_specs=out_specs, check_vma=False)
```

```python
import jax
import jax.numpy as jnp
from jax import lax
from jax.sharding import PartitionSpec as P

DAMPING = 0.5
RELAXATION = 0.6


def with_halo(array, sides, width, tie=None):
    for axis, dim in sides:
        peers, length = (lax.axis_size(axis), array.shape[dim])
        last = lax.slice_in_dim(array, length - width, length, axis=dim)
        initial = lax.slice_in_dim(array, 0, width, axis=dim)
        if peers == 2 and dim == array.ndim - 1:
            first = lax.axis_index(axis) == 0
            sent = array if tie is None else array + tie
            got = lax.ppermute(sent, axis, [(0, 1), (1, 0)])
            got_last = lax.slice_in_dim(got, length - width, length, axis=dim)
            got_initial = lax.slice_in_dim(got, 0, width, axis=dim)
            zero = jnp.zeros_like(got_last)
            before = jnp.where(first, zero, got_last)
            after = jnp.where(first, got_initial, zero)
        elif peers == 2:
            first = lax.axis_index(axis) == 0
            got = lax.ppermute(jnp.where(first, last, initial), axis, [(0, 1), (1, 0)])
            zero = jnp.zeros_like(got)
            before = jnp.where(first, zero, got)
            after = jnp.where(first, got, zero)
        else:
            up = [(i, (i + 1) % peers) for i in range(peers - 1)]
            down = [(j, i) for i, j in up]
            before = lax.ppermute(last, axis, up)
            after = lax.ppermute(initial, axis, down)
        array = jnp.concatenate([before, array, after], axis=dim)
    return array


def window(padded, offset):
    size_x = padded.shape[1] - 2
    size_y = padded.shape[2] - 2
    size_z = padded.shape[3] - 2
    return padded[
        :,
        1 + offset[0] : 1 + offset[0] + size_x,
        1 + offset[1] : 1 + offset[1] + size_y,
        1 + offset[2] : 1 + offset[2] + size_z,
    ]


def navier(padded, lame_first, shear):
    units = ((1, 0, 0), (0, 1, 0), (0, 0, 1))
    centre = window(padded, (0, 0, 0))
    second = []
    for axis_d in range(3):
        ahead = units[axis_d]
        behind = tuple((-value for value in ahead))
        second.append(window(padded, ahead) + window(padded, behind) - 2.0 * centre)
    laplace = second[0] + second[1] + second[2]
    result = []
    for part_index in range(2):
        for component in range(3):
            channel = part_index * 3 + component
            divergence = second[component][channel]
            for other_axis in range(3):
                if other_axis != component:
                    source_channel = part_index * 3 + other_axis
                    single = padded[source_channel : source_channel + 1]
                    first_unit = units[component]
                    other_unit = units[other_axis]
                    plus_plus = tuple((first_unit[k] + other_unit[k] for k in range(3)))
                    plus_minus = tuple((first_unit[k] - other_unit[k] for k in range(3)))
                    minus_plus = tuple((-first_unit[k] + other_unit[k] for k in range(3)))
                    minus_minus = tuple((-first_unit[k] - other_unit[k] for k in range(3)))
                    mixed = (
                        window(single, plus_plus)
                        - window(single, plus_minus)
                        - window(single, minus_plus)
                        + window(single, minus_minus)
                    )
                    divergence = divergence + 0.25 * mixed[0]
            result.append(shear * laplace[channel] + (lame_first + shear) * divergence)
    return jnp.stack(result)


def sweep(padded, lame_first, shear, density, mask, source, omega_sq, impedance):
    field = window(padded, (0, 0, 0))
    elastic = navier(padded, lame_first, shear)
    real_part = field[:3]
    imag_part = field[3:]
    imp_real = impedance[0][:, None, None, None]
    imp_imag = impedance[1][:, None, None, None]
    inertia = omega_sq * density
    apply_real = (
        -elastic[:3]
        - inertia * (real_part - DAMPING * imag_part)
        + mask * (imp_real * real_part - imp_imag * imag_part)
    )
    apply_imag = (
        -elastic[3:]
        - inertia * (imag_part + DAMPING * real_part)
        + mask * (imp_real * imag_part + imp_imag * real_part)
    )
    resid_real = source[:3] - apply_real
    resid_imag = source[3:] - apply_imag
    diag_real = 8.0 * shear + 2.0 * lame_first - inertia + mask * imp_real
    diag_imag = -DAMPING * inertia + mask * imp_imag
    modulus = diag_real * diag_real + diag_imag * diag_imag
    new_real = real_part + RELAXATION * (resid_real * diag_real + resid_imag * diag_imag) / modulus
    new_imag = imag_part + RELAXATION * (resid_imag * diag_real - resid_real * diag_imag) / modulus
    return jnp.concatenate([new_real, new_imag], 0)


def mean_gain(lame_first, shear, density, mask, omega_sq, impedance):
    imp_real = impedance[0][:, None, None, None]
    imp_imag = impedance[1][:, None, None, None]
    inertia = omega_sq * density
    diag_real = 8.0 * shear + 2.0 * lame_first - inertia + mask * imp_real
    diag_imag = -DAMPING * inertia + mask * imp_imag
    scale = RELAXATION * mask / (diag_real * diag_real + diag_imag * diag_imag)
    gain_real = scale * (imp_real * diag_real + imp_imag * diag_imag)
    gain_imag = scale * (imp_imag * diag_real - imp_real * diag_imag)
    return gain_real, gain_imag


def add_mean(field, gain_real, gain_imag, mean_field):
    mean_real = mean_field[:3]
    mean_imag = mean_field[3:]
    straight = jnp.concatenate([mean_real, mean_imag])[:, None, None, None]
    crossed = jnp.concatenate([-mean_imag, mean_real])[:, None, None, None]
    return field + (gain_real * straight + gain_imag * crossed)


def group_rounds(value, axes):
    size = 1
    for axis in axes:
        size *= lax.axis_size(axis)
    if size & (size - 1):
        return [lax.psum(value, axes)]
    rounds = []
    stride = 1
    while stride < size:
        if stride * 4 <= size:
            got = [
                lax.ppermute(value, axes, [(i, i ^ (m * stride)) for i in range(size)])
                for m in (1, 2, 3)
            ]
            value = (value + got[0]) + (got[1] + got[2])
            stride *= 4
        else:
            value = value + lax.ppermute(value, axes, [(i, i ^ stride) for i in range(size)])
            stride *= 2
        rounds.append(value)
    return rounds


def group_sum(value, axes):
    return group_rounds(value, axes)[-1]


def expand(blocks):
    blocks_x, blocks_y, blocks_z = blocks.shape
    depth_tile = lax.broadcasted_iota(jnp.int32, (1, 1, blocks_z * 32), 2) // 32
    rows = jnp.zeros((blocks_x, blocks_y, blocks_z * 32), blocks.dtype)
    for tile in range(blocks_z):
        rows = jnp.where(depth_tile == tile, blocks[:, :, tile : tile + 1], rows)
    spread = jnp.broadcast_to(
        rows[:, None, :, None, :], (blocks_x, 8, blocks_y, 8, blocks_z * 32)
    )
    return spread.reshape(blocks_x * 8, blocks_y * 8, blocks_z * 32)


def material(block_ids, table):
    entries = lax.broadcasted_iota(jnp.int32, block_ids.shape + (table.shape[0],), block_ids.ndim)
    chosen = block_ids[..., None] == entries
    lame_first = jnp.sum(jnp.where(chosen, table[:, 0], 0.0), axis=-1)
    shear = jnp.sum(jnp.where(chosen, table[:, 1], 0.0), axis=-1)
    return (lame_first, shear)


def shards(
    source, warm, forward, density, material_map, material_table, iface_cells, impedance, omega2
):
    omega_sq = omega2[0]
    tile_shape = density.shape
    tile_cells = tile_shape[0] * tile_shape[1] * tile_shape[2]
    mask = jnp.zeros((tile_cells,), jnp.float32).at[iface_cells[0]].set(1.0).reshape(tile_shape)
    lame_tiles, shear_tiles = material(material_map, material_table)
    lame_first = expand(lame_tiles)
    shear = expand(shear_tiles)
    density_cells = density.astype(jnp.float32)
    source_cells = source.astype(jnp.float32)
    group_size = lax.axis_size("gx") * lax.axis_size("gy") * lax.axis_size("col")
    count = jnp.float32(group_size * iface_cells.shape[1])
    gain_real, gain_imag = mean_gain(lame_first, shear, density_cells, mask, omega_sq, impedance)
    gain_both_real = jnp.concatenate([gain_real, gain_real])
    gain_both_imag = jnp.concatenate([gain_imag, gain_imag])
    axes = ("gx", "gy", "col")
    coarse_x = tile_shape[0] // 4
    coarse_y = tile_shape[1] // 4
    grid_shape = (lax.axis_size("gy") * coarse_y, lax.axis_size("gx") * coarse_x)
    grid_at = (lax.axis_index("gy") * coarse_y, lax.axis_index("gx") * coarse_x)

    def block_sums(cells):
        lead = cells.shape[:-3]
        local = cells.reshape(lead + (coarse_x, 4, coarse_y, 4, tile_shape[2]))
        local = jnp.swapaxes(local.sum(axis=(-4, -2, -1)), -1, -2)
        grid = jnp.zeros(lead + grid_shape, jnp.float32)
        return lax.dynamic_update_slice(grid, local, (0,) * len(lead) + grid_at)

    forward_cells = forward.astype(jnp.float32)
    forward_real = forward_cells[:3]
    forward_imag = forward_cells[3:]
    plain_real = gain_real * forward_real - gain_imag * forward_imag
    plain_imag = gain_real * forward_imag + gain_imag * forward_real
    response_real = plain_real - DAMPING * plain_imag
    response_imag = plain_imag + DAMPING * plain_real
    response = block_sums(jnp.concatenate([response_real, response_imag]))
    field = warm.astype(jnp.float32)
    rounds = group_rounds(
        jnp.concatenate(
            [
                jnp.sum(mask * field, axis=(1, 2, 3)),
                jnp.sum(gain_real, axis=(1, 2, 3)),
                jnp.sum(gain_imag, axis=(1, 2, 3)),
            ]
        ),
        axes,
    )
    first = rounds[-1]
    mean_field = first[:6] / count
    gain_total_real = first[6:9]
    gain_total_imag = first[9:12]
    sweep_args = (lame_first, shear, density_cells, mask, source_cells, omega_sq, impedance)
    padded = with_halo(field, (("gx", 1), ("gy", 2)), 1)
    padded = with_halo(padded, (("col", 3),), 1, 0.0 * rounds[0][0])
    tied_source = source_cells + 0.0 * first[0]
    field = sweep(padded, lame_first, shear, density_cells, mask, tied_source, omega_sq, impedance)
    second_local = jnp.sum(mask * field, axis=(1, 2, 3))
    field = add_mean(field, gain_both_real, gain_both_imag, mean_field)
    padded = with_halo(field, (("gx", 1), ("gy", 2), ("col", 3)), 1)
    field = sweep(padded, *sweep_args)
    correlation = (
        field[:3] * forward_real
        - field[3:] * forward_imag
        - DAMPING * (field[:3] * forward_imag + field[3:] * forward_real)
    )
    cell_terms = -omega_sq * jnp.sum(correlation, axis=0)
    last = group_sum(
        jnp.concatenate([second_local, block_sums(cell_terms).reshape(-1), response.reshape(-1)]),
        axes,
    )
    second = last[:6]
    grid_size = grid_shape[0] * grid_shape[1]
    response = last[6 + grid_size :].reshape(response.shape)
    mean_real = mean_field[:3]
    mean_imag = mean_field[3:]
    total_real = second[:3] + (gain_total_real * mean_real - gain_total_imag * mean_imag)
    total_imag = second[3:] + (gain_total_real * mean_imag + gain_total_imag * mean_real)
    late_mean = jnp.concatenate([total_real, total_imag]) / count
    field = add_mean(field, gain_both_real, gain_both_imag, late_mean)
    late_terms = jnp.sum(
        late_mean[:3, None, None] * response[:3] - late_mean[3:, None, None] * response[3:], axis=0
    )
    coarse = ((last[6 : 6 + grid_size].reshape(grid_shape) - omega_sq * late_terms) / 64.0).T
    return (field, coarse)


def solution(mesh):
    in_specs = (
        P("freq", "gx", "gy", "col"),
        P("freq", "gx", "gy", "col"),
        P("freq", "gx", "gy", "col"),
        P("gx", "gy", "col"),
        P("gx", "gy", "col"),
        P(),
        P(("gx", "gy", "col"), None),
        P(),
        P("freq"),
    )
    out_specs = (P("freq", "gx", "gy", "col"), P("freq", None))
    return jax.shard_map(shards, mesh=mesh, in_specs=in_specs, out_specs=out_specs, check_vma=False)
```

```python
import jax
import jax.numpy as jnp
from jax import lax
from jax.sharding import PartitionSpec as P

DAMPING = 0.5
RELAXATION = 0.6


def with_halo(array, sides, width, tie=None):
    for axis, dim in sides:
        peers, length = (lax.axis_size(axis), array.shape[dim])
        last = lax.slice_in_dim(array, length - width, length, axis=dim)
        initial = lax.slice_in_dim(array, 0, width, axis=dim)
        if peers == 2 and dim == array.ndim - 1:
            first = lax.axis_index(axis) == 0
            sent = array if tie is None else array + tie
            got = lax.ppermute(sent, axis, [(0, 1), (1, 0)])
            lane = lax.broadcasted_iota(jnp.int32, got.shape, dim)
            got_last = jnp.sum(jnp.where(lane == length - 1, got, 0.0), axis=dim, keepdims=True)
            got_initial = jnp.sum(jnp.where(lane == 0, got, 0.0), axis=dim, keepdims=True)
            zero = jnp.zeros_like(got_last)
            before = jnp.where(first, zero, got_last)
            after = jnp.where(first, got_initial, zero)
        elif peers == 2:
            first = lax.axis_index(axis) == 0
            got = lax.ppermute(jnp.where(first, last, initial), axis, [(0, 1), (1, 0)])
            zero = jnp.zeros_like(got)
            before = jnp.where(first, zero, got)
            after = jnp.where(first, got, zero)
        else:
            up = [(i, (i + 1) % peers) for i in range(peers - 1)]
            down = [(j, i) for i, j in up]
            before = lax.ppermute(last, axis, up)
            after = lax.ppermute(initial, axis, down)
        array = jnp.concatenate([before, array, after], axis=dim)
    return array


def window(padded, offset):
    size_x = padded.shape[1] - 2
    size_y = padded.shape[2] - 2
    size_z = padded.shape[3] - 2
    return padded[
        :,
        1 + offset[0] : 1 + offset[0] + size_x,
        1 + offset[1] : 1 + offset[1] + size_y,
        1 + offset[2] : 1 + offset[2] + size_z,
    ]


def navier(padded, lame_first, shear):
    units = ((1, 0, 0), (0, 1, 0), (0, 0, 1))
    centre = window(padded, (0, 0, 0))
    second = []
    for axis_d in range(3):
        ahead = units[axis_d]
        behind = tuple((-value for value in ahead))
        second.append(window(padded, ahead) + window(padded, behind) - 2.0 * centre)
    laplace = second[0] + second[1] + second[2]
    result = []
    for part_index in range(2):
        for component in range(3):
            channel = part_index * 3 + component
            divergence = second[component][channel]
            for other_axis in range(3):
                if other_axis != component:
                    source_channel = part_index * 3 + other_axis
                    single = padded[source_channel : source_channel + 1]
                    first_unit = units[component]
                    other_unit = units[other_axis]
                    plus_plus = tuple((first_unit[k] + other_unit[k] for k in range(3)))
                    plus_minus = tuple((first_unit[k] - other_unit[k] for k in range(3)))
                    minus_plus = tuple((-first_unit[k] + other_unit[k] for k in range(3)))
                    minus_minus = tuple((-first_unit[k] - other_unit[k] for k in range(3)))
                    mixed = (
                        window(single, plus_plus)
                        - window(single, plus_minus)
                        - window(single, minus_plus)
                        + window(single, minus_minus)
                    )
                    divergence = divergence + 0.25 * mixed[0]
            result.append(shear * laplace[channel] + (lame_first + shear) * divergence)
    return jnp.stack(result)


def sweep(padded, lame_first, shear, density, mask, source, omega_sq, impedance):
    field = window(padded, (0, 0, 0))
    elastic = navier(padded, lame_first, shear)
    real_part = field[:3]
    imag_part = field[3:]
    imp_real = impedance[0][:, None, None, None]
    imp_imag = impedance[1][:, None, None, None]
    inertia = omega_sq * density
    apply_real = (
        -elastic[:3]
        - inertia * (real_part - DAMPING * imag_part)
        + mask * (imp_real * real_part - imp_imag * imag_part)
    )
    apply_imag = (
        -elastic[3:]
        - inertia * (imag_part + DAMPING * real_part)
        + mask * (imp_real * imag_part + imp_imag * real_part)
    )
    resid_real = source[:3] - apply_real
    resid_imag = source[3:] - apply_imag
    diag_real = 8.0 * shear + 2.0 * lame_first - inertia + mask * imp_real
    diag_imag = -DAMPING * inertia + mask * imp_imag
    modulus = diag_real * diag_real + diag_imag * diag_imag
    new_real = real_part + RELAXATION * (resid_real * diag_real + resid_imag * diag_imag) / modulus
    new_imag = imag_part + RELAXATION * (resid_imag * diag_real - resid_real * diag_imag) / modulus
    return jnp.concatenate([new_real, new_imag], 0)


def mean_gain(lame_first, shear, density, mask, omega_sq, impedance):
    imp_real = impedance[0][:, None, None, None]
    imp_imag = impedance[1][:, None, None, None]
    inertia = omega_sq * density
    diag_real = 8.0 * shear + 2.0 * lame_first - inertia + mask * imp_real
    diag_imag = -DAMPING * inertia + mask * imp_imag
    scale = RELAXATION * mask / (diag_real * diag_real + diag_imag * diag_imag)
    gain_real = scale * (imp_real * diag_real + imp_imag * diag_imag)
    gain_imag = scale * (imp_imag * diag_real - imp_real * diag_imag)
    return gain_real, gain_imag


def add_mean(field, gain_real, gain_imag, mean_field):
    mean_real = mean_field[:3]
    mean_imag = mean_field[3:]
    straight = jnp.concatenate([mean_real, mean_imag])[:, None, None, None]
    crossed = jnp.concatenate([-mean_imag, mean_real])[:, None, None, None]
    return field + (gain_real * straight + gain_imag * crossed)


def group_rounds(value, axes):
    size = 1
    for axis in axes:
        size *= lax.axis_size(axis)
    if size & (size - 1):
        return [lax.psum(value, axes)]
    rounds = []
    stride = 1
    while stride < size:
        if stride * 4 <= size:
            got = [
                lax.ppermute(value, axes, [(i, i ^ (m * stride)) for i in range(size)])
                for m in (1, 2, 3)
            ]
            value = (value + got[0]) + (got[1] + got[2])
            stride *= 4
        else:
            value = value + lax.ppermute(value, axes, [(i, i ^ stride) for i in range(size)])
            stride *= 2
        rounds.append(value)
    return rounds


def group_sum(value, axes):
    return group_rounds(value, axes)[-1]


def expand(blocks):
    blocks_x, blocks_y, blocks_z = blocks.shape
    depth_tile = lax.broadcasted_iota(jnp.int32, (1, 1, blocks_z * 32), 2) // 32
    rows = jnp.zeros((blocks_x, blocks_y, blocks_z * 32), blocks.dtype)
    for tile in range(blocks_z):
        rows = jnp.where(depth_tile == tile, blocks[:, :, tile : tile + 1], rows)
    spread = jnp.broadcast_to(
        rows[:, None, :, None, :], (blocks_x, 8, blocks_y, 8, blocks_z * 32)
    )
    return spread.reshape(blocks_x * 8, blocks_y * 8, blocks_z * 32)


def material(block_ids, table):
    entries = lax.broadcasted_iota(jnp.int32, block_ids.shape + (table.shape[0],), block_ids.ndim)
    chosen = block_ids[..., None] == entries
    lame_first = jnp.sum(jnp.where(chosen, table[:, 0], 0.0), axis=-1)
    shear = jnp.sum(jnp.where(chosen, table[:, 1], 0.0), axis=-1)
    return (lame_first, shear)


def shards(
    source, warm, forward, density, material_map, material_table, iface_cells, impedance, omega2
):
    omega_sq = omega2[0]
    tile_shape = density.shape
    tile_cells = tile_shape[0] * tile_shape[1] * tile_shape[2]
    mask = jnp.zeros((tile_cells,), jnp.float32).at[iface_cells[0]].set(1.0).reshape(tile_shape)
    lame_tiles, shear_tiles = material(material_map, material_table)
    lame_first = expand(lame_tiles)
    shear = expand(shear_tiles)
    density_cells = density.astype(jnp.float32)
    source_cells = source.astype(jnp.float32)
    group_size = lax.axis_size("gx") * lax.axis_size("gy") * lax.axis_size("col")
    count = jnp.float32(group_size * iface_cells.shape[1])
    gain_real, gain_imag = mean_gain(lame_first, shear, density_cells, mask, omega_sq, impedance)
    gain_both_real = jnp.concatenate([gain_real, gain_real])
    gain_both_imag = jnp.concatenate([gain_imag, gain_imag])
    axes = ("gx", "gy", "col")
    coarse_x = tile_shape[0] // 4
    coarse_y = tile_shape[1] // 4
    grid_shape = (lax.axis_size("gx") * coarse_x, lax.axis_size("gy") * coarse_y)
    grid_at = (lax.axis_index("gx") * coarse_x, lax.axis_index("gy") * coarse_y)

    def block_sums(cells):
        lead = cells.shape[:-3]
        local = cells.reshape(lead + (coarse_x, 4, coarse_y, 4, tile_shape[2]))
        local = local.sum(axis=(-4, -2, -1))
        grid = jnp.zeros(lead + grid_shape, jnp.float32)
        return lax.dynamic_update_slice(grid, local, (0,) * len(lead) + grid_at)

    forward_cells = forward.astype(jnp.float32)
    forward_real = forward_cells[:3]
    forward_imag = forward_cells[3:]
    plain_real = gain_real * forward_real - gain_imag * forward_imag
    plain_imag = gain_real * forward_imag + gain_imag * forward_real
    response_real = plain_real - DAMPING * plain_imag
    response_imag = plain_imag + DAMPING * plain_real
    response = block_sums(jnp.concatenate([response_real, response_imag]))
    field = warm.astype(jnp.float32)
    rounds = group_rounds(
        jnp.concatenate(
            [
                jnp.sum(mask * field, axis=(1, 2, 3)),
                jnp.sum(gain_real, axis=(1, 2, 3)),
                jnp.sum(gain_imag, axis=(1, 2, 3)),
            ]
        ),
        axes,
    )
    first = rounds[-1]
    mean_field = first[:6] / count
    gain_total_real = first[6:9]
    gain_total_imag = first[9:12]
    sweep_args = (lame_first, shear, density_cells, mask, source_cells, omega_sq, impedance)
    padded = with_halo(field, (("gx", 1), ("gy", 2)), 1)
    padded = with_halo(padded, (("col", 3),), 1, 0.0 * rounds[0][0])
    tied_source = source_cells + 0.0 * first[0]
    field = sweep(padded, lame_first, shear, density_cells, mask, tied_source, omega_sq, impedance)
    second_local = jnp.sum(mask * field, axis=(1, 2, 3))
    field = add_mean(field, gain_both_real, gain_both_imag, mean_field)
    padded = with_halo(field, (("gx", 1), ("gy", 2), ("col", 3)), 1)
    field = sweep(padded, *sweep_args)
    correlation = (
        field[:3] * forward_real
        - field[3:] * forward_imag
        - DAMPING * (field[:3] * forward_imag + field[3:] * forward_real)
    )
    cell_terms = -omega_sq * jnp.sum(correlation, axis=0)
    last = group_sum(
        jnp.concatenate([second_local, block_sums(cell_terms).reshape(-1), response.reshape(-1)]),
        axes,
    )
    second = last[:6]
    grid_size = grid_shape[0] * grid_shape[1]
    response = last[6 + grid_size :].reshape(response.shape)
    mean_real = mean_field[:3]
    mean_imag = mean_field[3:]
    total_real = second[:3] + (gain_total_real * mean_real - gain_total_imag * mean_imag)
    total_imag = second[3:] + (gain_total_real * mean_imag + gain_total_imag * mean_real)
    late_mean = jnp.concatenate([total_real, total_imag]) / count
    field = add_mean(field, gain_both_real, gain_both_imag, late_mean)
    late_terms = jnp.sum(
        late_mean[:3, None, None] * response[:3] - late_mean[3:, None, None] * response[3:], axis=0
    )
    coarse = (last[6 : 6 + grid_size].reshape(grid_shape) - omega_sq * late_terms) / 64.0
    return (field, coarse)


def solution(mesh):
    in_specs = (
        P("freq", "gx", "gy", "col"),
        P("freq", "gx", "gy", "col"),
        P("freq", "gx", "gy", "col"),
        P("gx", "gy", "col"),
        P("gx", "gy", "col"),
        P(),
        P(("gx", "gy", "col"), None),
        P(),
        P("freq"),
    )
    out_specs = (P("freq", "gx", "gy", "col"), P("freq", None))
    return jax.shard_map(shards, mesh=mesh, in_specs=in_specs, out_specs=out_specs, check_vma=False)
```

```python
import jax
import jax.numpy as jnp
from jax import lax
from jax.sharding import PartitionSpec as P

DAMPING = 0.5
RELAXATION = 0.6


def with_halo(array, sides, width, tie=None):
    for axis, dim in sides:
        peers, length = (lax.axis_size(axis), array.shape[dim])
        last = lax.slice_in_dim(array, length - width, length, axis=dim)
        initial = lax.slice_in_dim(array, 0, width, axis=dim)
        if peers == 2 and dim == array.ndim - 1:
            first = lax.axis_index(axis) == 0
            sent = array if tie is None else array + tie
            got = lax.ppermute(sent, axis, [(0, 1), (1, 0)])
            got_last = lax.slice_in_dim(got, length - width, length, axis=dim)
            got_initial = lax.slice_in_dim(got, 0, width, axis=dim)
            zero = jnp.zeros_like(got_last)
            before = jnp.where(first, zero, got_last)
            after = jnp.where(first, got_initial, zero)
        elif peers == 2:
            first = lax.axis_index(axis) == 0
            got = lax.ppermute(jnp.where(first, last, initial), axis, [(0, 1), (1, 0)])
            zero = jnp.zeros_like(got)
            before = jnp.where(first, zero, got)
            after = jnp.where(first, got, zero)
        else:
            up = [(i, (i + 1) % peers) for i in range(peers - 1)]
            down = [(j, i) for i, j in up]
            before = lax.ppermute(last, axis, up)
            after = lax.ppermute(initial, axis, down)
        array = jnp.concatenate([before, array, after], axis=dim)
    return array


def window(padded, offset):
    size_x = padded.shape[1] - 2
    size_y = padded.shape[2] - 2
    size_z = padded.shape[3] - 2
    return padded[
        :,
        1 + offset[0] : 1 + offset[0] + size_x,
        1 + offset[1] : 1 + offset[1] + size_y,
        1 + offset[2] : 1 + offset[2] + size_z,
    ]


def navier(padded, lame_first, shear):
    units = ((1, 0, 0), (0, 1, 0), (0, 0, 1))
    centre = window(padded, (0, 0, 0))
    second = []
    for axis_d in range(3):
        ahead = units[axis_d]
        behind = tuple((-value for value in ahead))
        second.append(window(padded, ahead) + window(padded, behind) - 2.0 * centre)
    laplace = second[0] + second[1] + second[2]
    result = []
    for part_index in range(2):
        for component in range(3):
            channel = part_index * 3 + component
            divergence = second[component][channel]
            for other_axis in range(3):
                if other_axis != component:
                    source_channel = part_index * 3 + other_axis
                    single = padded[source_channel : source_channel + 1]
                    first_unit = units[component]
                    other_unit = units[other_axis]
                    plus_plus = tuple((first_unit[k] + other_unit[k] for k in range(3)))
                    plus_minus = tuple((first_unit[k] - other_unit[k] for k in range(3)))
                    minus_plus = tuple((-first_unit[k] + other_unit[k] for k in range(3)))
                    minus_minus = tuple((-first_unit[k] - other_unit[k] for k in range(3)))
                    mixed = (
                        window(single, plus_plus)
                        - window(single, plus_minus)
                        - window(single, minus_plus)
                        + window(single, minus_minus)
                    )
                    divergence = divergence + 0.25 * mixed[0]
            result.append(shear * laplace[channel] + (lame_first + shear) * divergence)
    return jnp.stack(result)


def sweep(padded, lame_first, shear, density, mask, source, omega_sq, impedance):
    field = window(padded, (0, 0, 0))
    elastic = navier(padded, lame_first, shear)
    real_part = field[:3]
    imag_part = field[3:]
    imp_real = impedance[0][:, None, None, None]
    imp_imag = impedance[1][:, None, None, None]
    inertia = omega_sq * density
    apply_real = (
        -elastic[:3]
        - inertia * (real_part - DAMPING * imag_part)
        + mask * (imp_real * real_part - imp_imag * imag_part)
    )
    apply_imag = (
        -elastic[3:]
        - inertia * (imag_part + DAMPING * real_part)
        + mask * (imp_real * imag_part + imp_imag * real_part)
    )
    resid_real = source[:3] - apply_real
    resid_imag = source[3:] - apply_imag
    diag_real = 8.0 * shear + 2.0 * lame_first - inertia + mask * imp_real
    diag_imag = -DAMPING * inertia + mask * imp_imag
    modulus = diag_real * diag_real + diag_imag * diag_imag
    new_real = real_part + RELAXATION * (resid_real * diag_real + resid_imag * diag_imag) / modulus
    new_imag = imag_part + RELAXATION * (resid_imag * diag_real - resid_real * diag_imag) / modulus
    return jnp.concatenate([new_real, new_imag], 0)


def mean_gain(lame_first, shear, density, mask, omega_sq, impedance):
    imp_real = impedance[0][:, None, None, None]
    imp_imag = impedance[1][:, None, None, None]
    inertia = omega_sq * density
    diag_real = 8.0 * shear + 2.0 * lame_first - inertia + mask * imp_real
    diag_imag = -DAMPING * inertia + mask * imp_imag
    scale = RELAXATION * mask / (diag_real * diag_real + diag_imag * diag_imag)
    gain_real = scale * (imp_real * diag_real + imp_imag * diag_imag)
    gain_imag = scale * (imp_imag * diag_real - imp_real * diag_imag)
    return gain_real, gain_imag


def add_mean(field, gain_real, gain_imag, mean_field):
    mean_real = mean_field[:3]
    mean_imag = mean_field[3:]
    straight = jnp.concatenate([mean_real, mean_imag])[:, None, None, None]
    crossed = jnp.concatenate([-mean_imag, mean_real])[:, None, None, None]
    return field + (gain_real * straight + gain_imag * crossed)


def group_rounds(value, axes):
    size = 1
    for axis in axes:
        size *= lax.axis_size(axis)
    if size & (size - 1):
        return [lax.psum(value, axes)]
    rounds = []
    stride = 1
    while stride < size:
        if stride * 4 <= size:
            got = [
                lax.ppermute(value, axes, [(i, i ^ (m * stride)) for i in range(size)])
                for m in (1, 2, 3)
            ]
            value = (value + got[0]) + (got[1] + got[2])
            stride *= 4
        else:
            value = value + lax.ppermute(value, axes, [(i, i ^ stride) for i in range(size)])
            stride *= 2
        rounds.append(value)
    return rounds


def group_sum(value, axes):
    return group_rounds(value, axes)[-1]


def expand(blocks):
    blocks_x, blocks_y, blocks_z = blocks.shape
    depth_tile = lax.broadcasted_iota(jnp.int32, (1, 1, blocks_z * 32), 2) // 32
    rows = jnp.zeros((blocks_x, blocks_y, blocks_z * 32), blocks.dtype)
    for tile in range(blocks_z):
        rows = jnp.where(depth_tile == tile, blocks[:, :, tile : tile + 1], rows)
    spread = jnp.broadcast_to(
        rows[:, None, :, None, :], (blocks_x, 8, blocks_y, 8, blocks_z * 32)
    )
    return spread.reshape(blocks_x * 8, blocks_y * 8, blocks_z * 32)


def material(block_ids, table):
    entries = lax.broadcasted_iota(jnp.int32, block_ids.shape + (table.shape[0],), block_ids.ndim)
    chosen = block_ids[..., None] == entries
    lame_first = jnp.sum(jnp.where(chosen, table[:, 0], 0.0), axis=-1)
    shear = jnp.sum(jnp.where(chosen, table[:, 1], 0.0), axis=-1)
    return (lame_first, shear)


def shards(
    source, warm, forward, density, material_map, material_table, iface_cells, impedance, omega2
):
    omega_sq = omega2[0]
    tile_shape = density.shape
    tile_cells = tile_shape[0] * tile_shape[1] * tile_shape[2]
    mask = jnp.zeros((tile_cells,), jnp.float32).at[iface_cells[0]].set(1.0).reshape(tile_shape)
    lame_tiles, shear_tiles = material(material_map, material_table)
    lame_first = expand(lame_tiles)
    shear = expand(shear_tiles)
    density_cells = density.astype(jnp.float32)
    source_cells = source.astype(jnp.float32)
    group_size = lax.axis_size("gx") * lax.axis_size("gy") * lax.axis_size("col")
    count = jnp.float32(group_size * iface_cells.shape[1])
    gain_real, gain_imag = mean_gain(lame_first, shear, density_cells, mask, omega_sq, impedance)
    gain_both_real = jnp.concatenate([gain_real, gain_real])
    gain_both_imag = jnp.concatenate([gain_imag, gain_imag])
    axes = ("gx", "gy", "col")
    coarse_x = tile_shape[0] // 4
    coarse_y = tile_shape[1] // 4
    grid_shape = (lax.axis_size("gx") * coarse_x, lax.axis_size("gy") * coarse_y)
    grid_at = (lax.axis_index("gx") * coarse_x, lax.axis_index("gy") * coarse_y)

    def block_sums(cells):
        lead = cells.shape[:-3]
        local = cells.reshape(lead + (coarse_x, 4, coarse_y, 4, tile_shape[2]))
        local = local.sum(axis=(-4, -2, -1))
        grid = jnp.zeros(lead + grid_shape, jnp.float32)
        return lax.dynamic_update_slice(grid, local, (0,) * len(lead) + grid_at)

    forward_cells = forward.astype(jnp.float32)
    forward_real = forward_cells[:3]
    forward_imag = forward_cells[3:]
    plain_real = gain_real * forward_real - gain_imag * forward_imag
    plain_imag = gain_real * forward_imag + gain_imag * forward_real
    response_real = plain_real - DAMPING * plain_imag
    response_imag = plain_imag + DAMPING * plain_real
    response = block_sums(jnp.concatenate([response_real, response_imag]))
    field = warm.astype(jnp.float32)
    rounds = group_rounds(
        jnp.concatenate(
            [
                jnp.sum(mask * field, axis=(1, 2, 3)),
            ]
        ),
        axes,
    )
    first = rounds[-1]
    mean_field = first[:6] / count
    sweep_args = (lame_first, shear, density_cells, mask, source_cells, omega_sq, impedance)
    padded = with_halo(field, (("gx", 1), ("gy", 2)), 1)
    padded = with_halo(padded, (("col", 3),), 1, 0.0 * rounds[0][0])
    tied_source = source_cells + 0.0 * first[0]
    field = sweep(padded, lame_first, shear, density_cells, mask, tied_source, omega_sq, impedance)
    second_local = jnp.sum(mask * field, axis=(1, 2, 3))
    field = add_mean(field, gain_both_real, gain_both_imag, mean_field)
    padded = with_halo(field, (("gx", 1), ("gy", 2), ("col", 3)), 1)
    field = sweep(padded, *sweep_args)
    correlation = (
        field[:3] * forward_real
        - field[3:] * forward_imag
        - DAMPING * (field[:3] * forward_imag + field[3:] * forward_real)
    )
    cell_terms = -omega_sq * jnp.sum(correlation, axis=0)
    last = group_sum(
        jnp.concatenate(
            [
                second_local,
                jnp.sum(gain_real, axis=(1, 2, 3)),
                jnp.sum(gain_imag, axis=(1, 2, 3)),
                block_sums(cell_terms).reshape(-1),
                response.reshape(-1),
            ]
        ),
        axes,
    )
    second = last[:6]
    gain_total_real = last[6:9]
    gain_total_imag = last[9:12]
    last = last[6:]
    grid_size = grid_shape[0] * grid_shape[1]
    response = last[6 + grid_size :].reshape(response.shape)
    mean_real = mean_field[:3]
    mean_imag = mean_field[3:]
    total_real = second[:3] + (gain_total_real * mean_real - gain_total_imag * mean_imag)
    total_imag = second[3:] + (gain_total_real * mean_imag + gain_total_imag * mean_real)
    late_mean = jnp.concatenate([total_real, total_imag]) / count
    field = add_mean(field, gain_both_real, gain_both_imag, late_mean)
    late_terms = jnp.sum(
        late_mean[:3, None, None] * response[:3] - late_mean[3:, None, None] * response[3:], axis=0
    )
    coarse = (last[6 : 6 + grid_size].reshape(grid_shape) - omega_sq * late_terms) / 64.0
    return (field, coarse)


def solution(mesh):
    in_specs = (
        P("freq", "gx", "gy", "col"),
        P("freq", "gx", "gy", "col"),
        P("freq", "gx", "gy", "col"),
        P("gx", "gy", "col"),
        P("gx", "gy", "col"),
        P(),
        P(("gx", "gy", "col"), None),
        P(),
        P("freq"),
    )
    out_specs = (P("freq", "gx", "gy", "col"), P("freq", None))
    return jax.shard_map(shards, mesh=mesh, in_specs=in_specs, out_specs=out_specs, check_vma=False)
```

```python
import jax
import jax.numpy as jnp
from jax import lax
from jax.sharding import PartitionSpec as P

DAMPING = 0.5
RELAXATION = 0.6


def with_halo(array, sides, width, tie=None):
    for axis, dim in sides:
        peers, length = (lax.axis_size(axis), array.shape[dim])
        last = lax.slice_in_dim(array, length - width, length, axis=dim)
        initial = lax.slice_in_dim(array, 0, width, axis=dim)
        if peers == 2 and dim == array.ndim - 1:
            first = lax.axis_index(axis) == 0
            sent = array if tie is None else array + tie
            got = lax.ppermute(sent, axis, [(0, 1), (1, 0)])
            got_last = lax.slice_in_dim(got, length - width, length, axis=dim)
            got_initial = lax.slice_in_dim(got, 0, width, axis=dim)
            zero = jnp.zeros_like(got_last)
            before = jnp.where(first, zero, got_last)
            after = jnp.where(first, got_initial, zero)
        elif peers == 2:
            first = lax.axis_index(axis) == 0
            got = lax.ppermute(jnp.where(first, last, initial), axis, [(0, 1), (1, 0)])
            zero = jnp.zeros_like(got)
            before = jnp.where(first, zero, got)
            after = jnp.where(first, got, zero)
        else:
            up = [(i, (i + 1) % peers) for i in range(peers - 1)]
            down = [(j, i) for i, j in up]
            before = lax.ppermute(last, axis, up)
            after = lax.ppermute(initial, axis, down)
        array = jnp.concatenate([before, array, after], axis=dim)
    return array


def window(padded, offset):
    size_x = padded.shape[1] - 2
    size_y = padded.shape[2] - 2
    size_z = padded.shape[3] - 2
    return padded[
        :,
        1 + offset[0] : 1 + offset[0] + size_x,
        1 + offset[1] : 1 + offset[1] + size_y,
        1 + offset[2] : 1 + offset[2] + size_z,
    ]


def navier(padded, lame_first, shear):
    units = ((1, 0, 0), (0, 1, 0), (0, 0, 1))
    centre = window(padded, (0, 0, 0))
    second = []
    for axis_d in range(3):
        ahead = units[axis_d]
        behind = tuple((-value for value in ahead))
        second.append(window(padded, ahead) + window(padded, behind) - 2.0 * centre)
    laplace = second[0] + second[1] + second[2]
    result = []
    for part_index in range(2):
        for component in range(3):
            channel = part_index * 3 + component
            divergence = second[component][channel]
            for other_axis in range(3):
                if other_axis != component:
                    source_channel = part_index * 3 + other_axis
                    single = padded[source_channel : source_channel + 1]
                    first_unit = units[component]
                    other_unit = units[other_axis]
                    plus_plus = tuple((first_unit[k] + other_unit[k] for k in range(3)))
                    plus_minus = tuple((first_unit[k] - other_unit[k] for k in range(3)))
                    minus_plus = tuple((-first_unit[k] + other_unit[k] for k in range(3)))
                    minus_minus = tuple((-first_unit[k] - other_unit[k] for k in range(3)))
                    mixed = (
                        window(single, plus_plus)
                        - window(single, plus_minus)
                        - window(single, minus_plus)
                        + window(single, minus_minus)
                    )
                    divergence = divergence + 0.25 * mixed[0]
            result.append(shear * laplace[channel] + (lame_first + shear) * divergence)
    return jnp.stack(result)


def sweep(padded, lame_first, shear, density, mask, source, omega_sq, impedance):
    field = window(padded, (0, 0, 0))
    elastic = navier(padded, lame_first, shear)
    cross = jnp.concatenate([-field[3:], field[:3]], 0)
    imp_real = jnp.concatenate([impedance[0], impedance[0]])[:, None, None, None]
    imp_imag = jnp.concatenate([impedance[1], impedance[1]])[:, None, None, None]
    inertia = omega_sq * density
    apply = (
        -elastic
        - inertia * (field + DAMPING * cross)
        + mask * (imp_real * field + imp_imag * cross)
    )
    resid = source - apply
    resid_cross = jnp.concatenate([resid[3:], -resid[:3]], 0)
    diag_real = 8.0 * shear + 2.0 * lame_first - inertia + mask * imp_real
    diag_imag = -DAMPING * inertia + mask * imp_imag
    modulus = diag_real * diag_real + diag_imag * diag_imag
    return field + RELAXATION * (resid * diag_real + resid_cross * diag_imag) / modulus


def mean_gain(lame_first, shear, density, mask, omega_sq, impedance):
    imp_real = impedance[0][:, None, None, None]
    imp_imag = impedance[1][:, None, None, None]
    inertia = omega_sq * density
    diag_real = 8.0 * shear + 2.0 * lame_first - inertia + mask * imp_real
    diag_imag = -DAMPING * inertia + mask * imp_imag
    scale = RELAXATION * mask / (diag_real * diag_real + diag_imag * diag_imag)
    gain_real = scale * (imp_real * diag_real + imp_imag * diag_imag)
    gain_imag = scale * (imp_imag * diag_real - imp_real * diag_imag)
    return gain_real, gain_imag


def add_mean(field, gain_real, gain_imag, mean_field):
    mean_real = mean_field[:3]
    mean_imag = mean_field[3:]
    straight = jnp.concatenate([mean_real, mean_imag])[:, None, None, None]
    crossed = jnp.concatenate([-mean_imag, mean_real])[:, None, None, None]
    return field + (gain_real * straight + gain_imag * crossed)


def group_rounds(value, axes):
    size = 1
    for axis in axes:
        size *= lax.axis_size(axis)
    if size & (size - 1):
        return [lax.psum(value, axes)]
    rounds = []
    stride = 1
    while stride < size:
        if stride * 4 <= size:
            got = [
                lax.ppermute(value, axes, [(i, i ^ (m * stride)) for i in range(size)])
                for m in (1, 2, 3)
            ]
            value = (value + got[0]) + (got[1] + got[2])
            stride *= 4
        else:
            value = value + lax.ppermute(value, axes, [(i, i ^ stride) for i in range(size)])
            stride *= 2
        rounds.append(value)
    return rounds


def group_sum(value, axes):
    return group_rounds(value, axes)[-1]


def expand(blocks):
    blocks_x, blocks_y, blocks_z = blocks.shape
    depth_tile = lax.broadcasted_iota(jnp.int32, (1, 1, blocks_z * 32), 2) // 32
    rows = jnp.zeros((blocks_x, blocks_y, blocks_z * 32), blocks.dtype)
    for tile in range(blocks_z):
        rows = jnp.where(depth_tile == tile, blocks[:, :, tile : tile + 1], rows)
    spread = jnp.broadcast_to(
        rows[:, None, :, None, :], (blocks_x, 8, blocks_y, 8, blocks_z * 32)
    )
    return spread.reshape(blocks_x * 8, blocks_y * 8, blocks_z * 32)


def material(block_ids, table):
    entries = lax.broadcasted_iota(jnp.int32, block_ids.shape + (table.shape[0],), block_ids.ndim)
    chosen = block_ids[..., None] == entries
    lame_first = jnp.sum(jnp.where(chosen, table[:, 0], 0.0), axis=-1)
    shear = jnp.sum(jnp.where(chosen, table[:, 1], 0.0), axis=-1)
    return (lame_first, shear)


def shards(
    source, warm, forward, density, material_map, material_table, iface_cells, impedance, omega2
):
    omega_sq = omega2[0]
    tile_shape = density.shape
    tile_cells = tile_shape[0] * tile_shape[1] * tile_shape[2]
    mask = jnp.zeros((tile_cells,), jnp.float32).at[iface_cells[0]].set(1.0).reshape(tile_shape)
    lame_tiles, shear_tiles = material(material_map, material_table)
    lame_first = expand(lame_tiles)
    shear = expand(shear_tiles)
    density_cells = density.astype(jnp.float32)
    source_cells = source.astype(jnp.float32)
    group_size = lax.axis_size("gx") * lax.axis_size("gy") * lax.axis_size("col")
    count = jnp.float32(group_size * iface_cells.shape[1])
    gain_real, gain_imag = mean_gain(lame_first, shear, density_cells, mask, omega_sq, impedance)
    gain_both_real = jnp.concatenate([gain_real, gain_real])
    gain_both_imag = jnp.concatenate([gain_imag, gain_imag])
    axes = ("gx", "gy", "col")
    coarse_x = tile_shape[0] // 4
    coarse_y = tile_shape[1] // 4
    grid_shape = (lax.axis_size("gx") * coarse_x, lax.axis_size("gy") * coarse_y)
    grid_at = (lax.axis_index("gx") * coarse_x, lax.axis_index("gy") * coarse_y)

    def block_sums(cells):
        lead = cells.shape[:-3]
        local = cells.reshape(lead + (coarse_x, 4, coarse_y, 4, tile_shape[2]))
        local = local.sum(axis=(-4, -2, -1))
        grid = jnp.zeros(lead + grid_shape, jnp.float32)
        return lax.dynamic_update_slice(grid, local, (0,) * len(lead) + grid_at)

    forward_cells = forward.astype(jnp.float32)
    forward_real = forward_cells[:3]
    forward_imag = forward_cells[3:]
    plain_real = gain_real * forward_real - gain_imag * forward_imag
    plain_imag = gain_real * forward_imag + gain_imag * forward_real
    response_real = plain_real - DAMPING * plain_imag
    response_imag = plain_imag + DAMPING * plain_real
    response = block_sums(jnp.concatenate([response_real, response_imag]))
    field = warm.astype(jnp.float32)
    rounds = group_rounds(
        jnp.concatenate(
            [
                jnp.sum(mask * field, axis=(1, 2, 3)),
                jnp.sum(gain_real, axis=(1, 2, 3)),
                jnp.sum(gain_imag, axis=(1, 2, 3)),
            ]
        ),
        axes,
    )
    first = rounds[-1]
    mean_field = first[:6] / count
    gain_total_real = first[6:9]
    gain_total_imag = first[9:12]
    sweep_args = (lame_first, shear, density_cells, mask, source_cells, omega_sq, impedance)
    padded = with_halo(field, (("gx", 1), ("gy", 2)), 1)
    padded = with_halo(padded, (("col", 3),), 1, 0.0 * rounds[0][0])
    tied_source = source_cells + 0.0 * first[0]
    field = sweep(padded, lame_first, shear, density_cells, mask, tied_source, omega_sq, impedance)
    second_local = jnp.sum(mask * field, axis=(1, 2, 3))
    field = add_mean(field, gain_both_real, gain_both_imag, mean_field)
    padded = with_halo(field, (("gx", 1), ("gy", 2), ("col", 3)), 1)
    field = sweep(padded, *sweep_args)
    correlation = (
        field[:3] * forward_real
        - field[3:] * forward_imag
        - DAMPING * (field[:3] * forward_imag + field[3:] * forward_real)
    )
    cell_terms = -omega_sq * jnp.sum(correlation, axis=0)
    last = group_sum(
        jnp.concatenate([second_local, block_sums(cell_terms).reshape(-1), response.reshape(-1)]),
        axes,
    )
    second = last[:6]
    grid_size = grid_shape[0] * grid_shape[1]
    response = last[6 + grid_size :].reshape(response.shape)
    mean_real = mean_field[:3]
    mean_imag = mean_field[3:]
    total_real = second[:3] + (gain_total_real * mean_real - gain_total_imag * mean_imag)
    total_imag = second[3:] + (gain_total_real * mean_imag + gain_total_imag * mean_real)
    late_mean = jnp.concatenate([total_real, total_imag]) / count
    field = add_mean(field, gain_both_real, gain_both_imag, late_mean)
    late_terms = jnp.sum(
        late_mean[:3, None, None] * response[:3] - late_mean[3:, None, None] * response[3:], axis=0
    )
    coarse = (last[6 : 6 + grid_size].reshape(grid_shape) - omega_sq * late_terms) / 64.0
    return (field, coarse)


def solution(mesh):
    in_specs = (
        P("freq", "gx", "gy", "col"),
        P("freq", "gx", "gy", "col"),
        P("freq", "gx", "gy", "col"),
        P("gx", "gy", "col"),
        P("gx", "gy", "col"),
        P(),
        P(("gx", "gy", "col"), None),
        P(),
        P("freq"),
    )
    out_specs = (P("freq", "gx", "gy", "col"), P("freq", None))
    return jax.shard_map(shards, mesh=mesh, in_specs=in_specs, out_specs=out_specs, check_vma=False)
```

```python
import jax
import jax.numpy as jnp
from jax import lax
from jax.sharding import PartitionSpec as P

DAMPING = 0.5
RELAXATION = 0.6


def with_halo(array, sides, width, tie=None):
    for axis, dim in sides:
        peers, length = (lax.axis_size(axis), array.shape[dim])
        last = lax.slice_in_dim(array, length - width, length, axis=dim)
        initial = lax.slice_in_dim(array, 0, width, axis=dim)
        if peers == 2 and dim == array.ndim - 1:
            first = lax.axis_index(axis) == 0
            sent = array if tie is None else array + tie
            got = lax.ppermute(sent, axis, [(0, 1), (1, 0)])
            got_last = lax.slice_in_dim(got, length - width, length, axis=dim)
            got_initial = lax.slice_in_dim(got, 0, width, axis=dim)
            zero = jnp.zeros_like(got_last)
            before = jnp.where(first, zero, got_last)
            after = jnp.where(first, got_initial, zero)
        elif peers == 2:
            first = lax.axis_index(axis) == 0
            got = lax.ppermute(jnp.where(first, last, initial), axis, [(0, 1), (1, 0)])
            zero = jnp.zeros_like(got)
            before = jnp.where(first, zero, got)
            after = jnp.where(first, got, zero)
        else:
            up = [(i, (i + 1) % peers) for i in range(peers - 1)]
            down = [(j, i) for i, j in up]
            before = lax.ppermute(last, axis, up)
            after = lax.ppermute(initial, axis, down)
        array = jnp.concatenate([before, array, after], axis=dim)
    return array


def window(padded, offset):
    size_x = padded.shape[1] - 2
    size_y = padded.shape[2] - 2
    size_z = padded.shape[3] - 2
    return padded[
        :,
        1 + offset[0] : 1 + offset[0] + size_x,
        1 + offset[1] : 1 + offset[1] + size_y,
        1 + offset[2] : 1 + offset[2] + size_z,
    ]


def navier(padded, lame_first, shear):
    units = ((1, 0, 0), (0, 1, 0), (0, 0, 1))
    centre = window(padded, (0, 0, 0))
    second = []
    for axis_d in range(3):
        ahead = units[axis_d]
        behind = tuple((-value for value in ahead))
        second.append(window(padded, ahead) + window(padded, behind) - 2.0 * centre)
    laplace = second[0] + second[1] + second[2]
    result = []
    for part_index in range(2):
        for component in range(3):
            channel = part_index * 3 + component
            divergence = second[component][channel]
            for other_axis in range(3):
                if other_axis != component:
                    source_channel = part_index * 3 + other_axis
                    single = padded[source_channel : source_channel + 1]
                    first_unit = units[component]
                    other_unit = units[other_axis]
                    plus_plus = tuple((first_unit[k] + other_unit[k] for k in range(3)))
                    plus_minus = tuple((first_unit[k] - other_unit[k] for k in range(3)))
                    minus_plus = tuple((-first_unit[k] + other_unit[k] for k in range(3)))
                    minus_minus = tuple((-first_unit[k] - other_unit[k] for k in range(3)))
                    mixed = (
                        window(single, plus_plus)
                        - window(single, plus_minus)
                        - window(single, minus_plus)
                        + window(single, minus_minus)
                    )
                    divergence = divergence + 0.25 * mixed[0]
            result.append(shear * laplace[channel] + (lame_first + shear) * divergence)
    return jnp.stack(result)


def sweep(padded, lame_first, shear, density, mask, source, omega_sq, impedance):
    field = window(padded, (0, 0, 0))
    elastic = navier(padded, lame_first, shear)
    real_part = field[:3]
    imag_part = field[3:]
    imp_real = impedance[0][:, None, None, None]
    imp_imag = impedance[1][:, None, None, None]
    inertia = omega_sq * density
    apply_real = (
        -elastic[:3]
        - inertia * (real_part - DAMPING * imag_part)
        + mask * (imp_real * real_part - imp_imag * imag_part)
    )
    apply_imag = (
        -elastic[3:]
        - inertia * (imag_part + DAMPING * real_part)
        + mask * (imp_real * imag_part + imp_imag * real_part)
    )
    resid_real = source[:3] - apply_real
    resid_imag = source[3:] - apply_imag
    diag_real = 8.0 * shear + 2.0 * lame_first - inertia + mask * imp_real
    diag_imag = -DAMPING * inertia + mask * imp_imag
    modulus = diag_real * diag_real + diag_imag * diag_imag
    new_real = real_part + RELAXATION * (resid_real * diag_real + resid_imag * diag_imag) / modulus
    new_imag = imag_part + RELAXATION * (resid_imag * diag_real - resid_real * diag_imag) / modulus
    return jnp.concatenate([new_real, new_imag], 0)


def mean_gain(lame_first, shear, density, mask, omega_sq, impedance):
    imp_real = impedance[0][:, None, None, None]
    imp_imag = impedance[1][:, None, None, None]
    inertia = omega_sq * density
    diag_real = 8.0 * shear + 2.0 * lame_first - inertia + mask * imp_real
    diag_imag = -DAMPING * inertia + mask * imp_imag
    scale = RELAXATION * mask / (diag_real * diag_real + diag_imag * diag_imag)
    gain_real = scale * (imp_real * diag_real + imp_imag * diag_imag)
    gain_imag = scale * (imp_imag * diag_real - imp_real * diag_imag)
    return gain_real, gain_imag


def add_mean(field, gain_real, gain_imag, mean_field):
    mean_real = mean_field[:3]
    mean_imag = mean_field[3:]
    straight = jnp.concatenate([mean_real, mean_imag])[:, None, None, None]
    crossed = jnp.concatenate([-mean_imag, mean_real])[:, None, None, None]
    return field + (gain_real * straight + gain_imag * crossed)


def group_rounds(value, axes):
    size = 1
    for axis in axes:
        size *= lax.axis_size(axis)
    if size & (size - 1):
        return [lax.psum(value, axes)]
    rounds = []
    stride = 1
    while stride < size:
        if stride * 4 <= size:
            got = [
                lax.ppermute(value, axes, [(i, i ^ (m * stride)) for i in range(size)])
                for m in (1, 2, 3)
            ]
            value = (value + got[0]) + (got[1] + got[2])
            stride *= 4
        else:
            value = value + lax.ppermute(value, axes, [(i, i ^ stride) for i in range(size)])
            stride *= 2
        rounds.append(value)
    return rounds


def group_sum(value, axes):
    return group_rounds(value, axes)[-1]


def expand(blocks):
    blocks_x, blocks_y, blocks_z = blocks.shape
    depth_tile = lax.broadcasted_iota(jnp.int32, (1, 1, blocks_z * 32), 2) // 32
    rows = jnp.zeros((blocks_x, blocks_y, blocks_z * 32), blocks.dtype)
    for tile in range(blocks_z):
        rows = jnp.where(depth_tile == tile, blocks[:, :, tile : tile + 1], rows)
    spread = jnp.broadcast_to(
        rows[:, None, :, None, :], (blocks_x, 8, blocks_y, 8, blocks_z * 32)
    )
    return spread.reshape(blocks_x * 8, blocks_y * 8, blocks_z * 32)


def material(block_ids, table):
    entries = lax.broadcasted_iota(jnp.int32, block_ids.shape + (table.shape[0],), block_ids.ndim)
    chosen = block_ids[..., None] == entries
    lame_first = jnp.sum(jnp.where(chosen, table[:, 0], 0.0), axis=-1)
    shear = jnp.sum(jnp.where(chosen, table[:, 1], 0.0), axis=-1)
    return (lame_first, shear)


def shards(
    source, warm, forward, density, material_map, material_table, iface_cells, impedance, omega2
):
    omega_sq = omega2[0]
    tile_shape = density.shape
    tile_cells = tile_shape[0] * tile_shape[1] * tile_shape[2]
    mask = jnp.zeros((tile_cells,), jnp.float32).at[iface_cells[0]].set(1.0).reshape(tile_shape)
    lame_tiles, shear_tiles = material(material_map, material_table)
    lame_first = expand(lame_tiles)
    shear = expand(shear_tiles)
    density_cells = density.astype(jnp.float32)
    source_cells = source.astype(jnp.float32)
    group_size = lax.axis_size("gx") * lax.axis_size("gy") * lax.axis_size("col")
    count = jnp.float32(group_size * iface_cells.shape[1])
    gain_real, gain_imag = mean_gain(lame_first, shear, density_cells, mask, omega_sq, impedance)
    gain_both_real = jnp.concatenate([gain_real, gain_real])
    gain_both_imag = jnp.concatenate([gain_imag, gain_imag])
    axes = ("gx", "gy", "col")
    coarse_x = tile_shape[0] // 4
    coarse_y = tile_shape[1] // 4
    grid_shape = (lax.axis_size("gx") * coarse_x, lax.axis_size("gy") * coarse_y)
    grid_at = (lax.axis_index("gx") * coarse_x, lax.axis_index("gy") * coarse_y)

    def block_sums(cells):
        lead = cells.shape[:-3]
        local = cells.reshape(lead + (coarse_x, 4, coarse_y, 4, tile_shape[2]))
        local = local.sum(axis=(-4, -2, -1))
        grid = jnp.zeros(lead + grid_shape, jnp.float32)
        return lax.dynamic_update_slice(grid, local, (0,) * len(lead) + grid_at)

    forward_cells = forward.astype(jnp.float32)
    forward_real = forward_cells[:3]
    forward_imag = forward_cells[3:]
    plain_real = gain_real * forward_real - gain_imag * forward_imag
    plain_imag = gain_real * forward_imag + gain_imag * forward_real
    response_real = plain_real - DAMPING * plain_imag
    response_imag = plain_imag + DAMPING * plain_real
    response = block_sums(jnp.concatenate([response_real, response_imag]))
    field = warm.astype(jnp.float32)
    rounds = group_rounds(
        jnp.concatenate(
            [
                jnp.sum(mask * field, axis=(1, 2, 3)),
                jnp.sum(gain_real, axis=(1, 2, 3)),
                jnp.sum(gain_imag, axis=(1, 2, 3)),
            ]
        ),
        axes,
    )
    first = rounds[-1]
    mean_field = first[:6] / count
    gain_total_real = first[6:9]
    gain_total_imag = first[9:12]
    sweep_args = (lame_first, shear, density_cells, mask, source_cells, omega_sq, impedance)
    padded = with_halo(field, (("gx", 1), ("gy", 2)), 1)
    padded = with_halo(padded, (("col", 3),), 1)
    tied_source = source_cells + 0.0 * first[0]
    field = sweep(padded, lame_first, shear, density_cells, mask, tied_source, omega_sq, impedance)
    second_local = jnp.sum(mask * field, axis=(1, 2, 3))
    field = add_mean(field, gain_both_real, gain_both_imag, mean_field)
    padded = with_halo(field, (("gx", 1), ("gy", 2), ("col", 3)), 1)
    field = sweep(padded, *sweep_args)
    correlation = (
        field[:3] * forward_real
        - field[3:] * forward_imag
        - DAMPING * (field[:3] * forward_imag + field[3:] * forward_real)
    )
    cell_terms = -omega_sq * jnp.sum(correlation, axis=0)
    last = group_sum(
        jnp.concatenate([second_local, block_sums(cell_terms).reshape(-1), response.reshape(-1)]),
        axes,
    )
    second = last[:6]
    grid_size = grid_shape[0] * grid_shape[1]
    response = last[6 + grid_size :].reshape(response.shape)
    mean_real = mean_field[:3]
    mean_imag = mean_field[3:]
    total_real = second[:3] + (gain_total_real * mean_real - gain_total_imag * mean_imag)
    total_imag = second[3:] + (gain_total_real * mean_imag + gain_total_imag * mean_real)
    late_mean = jnp.concatenate([total_real, total_imag]) / count
    field = add_mean(field, gain_both_real, gain_both_imag, late_mean)
    late_terms = jnp.sum(
        late_mean[:3, None, None] * response[:3] - late_mean[3:, None, None] * response[3:], axis=0
    )
    coarse = (last[6 : 6 + grid_size].reshape(grid_shape) - omega_sq * late_terms) / 64.0
    return (field, coarse)


def solution(mesh):
    in_specs = (
        P("freq", "gx", "gy", "col"),
        P("freq", "gx", "gy", "col"),
        P("freq", "gx", "gy", "col"),
        P("gx", "gy", "col"),
        P("gx", "gy", "col"),
        P(),
        P(("gx", "gy", "col"), None),
        P(),
        P("freq"),
    )
    out_specs = (P("freq", "gx", "gy", "col"), P("freq", None))
    return jax.shard_map(shards, mesh=mesh, in_specs=in_specs, out_specs=out_specs, check_vma=False)
```
